32 devices in a mesh: slab: 8 (over y, x, core), pencil: 4 (over z).
Axes of the slice: x: 2, y: 2, z: 4, core: 2. Of those that a mesh axis runs over, the one named last changes fastest.
Arguments:
- descriptors: bfloat16 [49152, 1600], P(('slab', 'pencil')), may hold values from -6 to 6
- species: int32 [49152], P(('slab', 'pencil')), may hold values from 0 to 3
- bucket_count: int32 [128], P(('slab', 'pencil')), may hold values from 288 to 384, as said below
- base_index: int32 [3, 49152], P(None, ('slab', 'pencil')), may hold values from 0 to 383, as said below
- fraction: float32 [3, 49152], P(None, ('slab', 'pencil')), may hold values from 0 to 0.999
- weight_in: bfloat16 [1600, 256], replicated, may hold values from -0.15625 to 0.15625
- bias_in: float32 [256], replicated, may hold values from -4 to 4
- weight_mid: bfloat16 [2, 256, 256], replicated, may hold values from -0.375 to 0.375
- bias_mid: float32 [2, 256], replicated, may hold values from -4 to 4
- weight_out: bfloat16 [3, 256], replicated, may hold values from -0.0390625 to 0.0390625
- bias_out: float32 [3], replicated, may hold values from -0.2 to 0.2
Outputs:
- energy: float32 [], replicated
- site_forces: float32 [2, 3, 49152], P(None, None, ('slab', 'pencil'))
- descriptor_grad: bfloat16 [49152, 1600], P(('slab', 'pencil'))
The draws below stay inside these ranges and needn't reach their ends.
Inputs may be any that keep to these rules, and one draw needn't show every extreme that they name: Slot i is in use when i % 384 < bucket_count[i // 384]. Among the buckets of every device at least one is full. Slots come in blocks of 1536; block d belongs to slab index d // 4 and pencil index d % 4. base_index[0, i] lies in that slab's planes, within the 4 planes of the slot's bucket (bucket b covers that slab's planes (b % 4) * 4 onwards); base_index[1, i] lies in that pencil's 48 rows; base_index[2, i] is any column.
All inputs are finite; a program needn't handle non-finite values.
Results may differ from the reference program's by a relative error of at most 0.018.
Values sent between devices are 32-bit elements; how exact they have to be, the bound alone decides.
No kernel may reach another device: no remote copies, remote signals or barrier semaphores. Data moves between devices by JAX's collectives and lax.ppermute only.
A program may use at most 192 MiB of HBM per device.

```python
import math
import jax
import jax.numpy as jnp
from jax import lax

NX = 384
CZ = 16
CY = 48
BZ = 4
CAP = 384
DESC = 1600
WIDTH = 256
ATOMS_DEV = 1536
ATOMS = 49152
N_SLAB = 8
N_PENCIL = 4


def draw_species(key, part):
    slot_total = ATOMS_DEV * N_SLAB * N_PENCIL
    picks = jax.random.randint(jax.random.fold_in(key, 5), (slot_total,), 0, 24)
    return jnp.where(picks < 21, 0, picks - 20).astype(jnp.int32)


def draw_bucket_count(key, part):
    bucket_total = CZ // BZ
    device_total = N_SLAB * N_PENCIL
    counts = jax.random.randint(key, (device_total, bucket_total), 3 * CAP // 4, CAP + 1)
    full_bucket = jax.random.randint(jax.random.fold_in(key, 7), (device_total, 1), 0, bucket_total)
    bucket_ids = jnp.arange(bucket_total, dtype=jnp.int32)
    counts = jnp.where(bucket_ids[None, :] == full_bucket, CAP, counts)
    return counts.reshape(-1).astype(jnp.int32)


def draw_base_index(key, part):
    slot_total = ATOMS_DEV * N_SLAB * N_PENCIL
    slot_ids = jnp.arange(slot_total, dtype=jnp.int32)
    device_ids = slot_ids // ATOMS_DEV
    slab_of = device_ids // N_PENCIL
    pencil_of = device_ids % N_PENCIL
    bucket_of = slot_ids % ATOMS_DEV // CAP
    key_plane = jax.random.fold_in(key, 11)
    key_row = jax.random.fold_in(key, 12)
    key_column = jax.random.fold_in(key, 13)
    plane = slab_of * CZ + bucket_of * BZ + jax.random.randint(key_plane, (slot_total,), 0, BZ)
    row_pos = pencil_of * CY + jax.random.randint(key_row, (slot_total,), 0, CY)
    column = jax.random.randint(key_column, (slot_total,), 0, NX)
    return jnp.stack([plane, row_pos, column]).astype(jnp.int32)


def shard_levels(key, shape, cuts, least, largest):
    loudness, own = 1.0, jax.random.fold_in(key, 6)
    for dim, blocks in cuts:
        steps = jnp.exp(jax.random.uniform(jax.random.fold_in(own, dim), (blocks,), jnp.float32, least / len(cuts), largest / len(cuts)))
        loudness = loudness * jnp.repeat(steps, shape[dim] // blocks).reshape([-1 if axis == dim else 1 for axis in range(len(shape))])
    return loudness


def centred(key, shape, scale, most, shards=(), kind=jnp.bfloat16):
    gain = shard_levels(key, shape, shards, -0.22, 0.18) if shards else 1.0
    values = jax.random.normal(key, shape, jnp.float32) * scale * gain
    return jnp.minimum(jnp.maximum(values, -most), most).astype(kind)


def setup_inputs(seed: int = 0) -> dict:
    streams_of = jax.random.split(jax.random.key(seed), 12)
    descriptors = centred(streams_of[0], (ATOMS, DESC), 1.0, 6.0, ((0, 32),))
    species = draw_species(jax.random.fold_in(streams_of[11], 71), 0)
    bucket_count = draw_bucket_count(jax.random.fold_in(streams_of[11], 71), 0)
    base_index = draw_base_index(jax.random.fold_in(streams_of[11], 71), 0)
    fraction = jnp.clip(0.999 * jax.random.uniform(streams_of[4], (3, ATOMS), jnp.float32) ** shard_levels(streams_of[4], (3, ATOMS), ((1, 32),), -0.2, 0.2), 0.0, 0.999)
    weight_in = centred(streams_of[5], (DESC, WIDTH), DESC ** -0.5, 0.15625)
    bias_in = centred(streams_of[6], (WIDTH,), 1.0, 4.0, (), jnp.float32)
    weight_mid = centred(streams_of[7], (2, WIDTH, WIDTH), WIDTH ** -0.5, 0.375)
    bias_mid = centred(streams_of[8], (2, WIDTH), 1.0, 4.0, (), jnp.float32)
    weight_out = centred(streams_of[9], (3, WIDTH), (96 * WIDTH) ** -0.5, 0.0390625)
    bias_out = centred(streams_of[10], (3,), 0.05, 0.2, (), jnp.float32)
    return {"descriptors": descriptors, "species": species, "bucket_count": bucket_count, "base_index": base_index, "fraction": fraction, "weight_in": weight_in, "bias_in": bias_in, "weight_mid": weight_mid, "bias_mid": bias_mid, "weight_out": weight_out, "bias_out": bias_out}


ion_table = (6.0, 1.0, 9.0, 7.0)
wannier_table = (-8.0, 0.0, -8.0, -8.0)
spline_coeffs = (1.0 / 120.0, 26.0 / 120.0, 66.0 / 120.0, 26.0 / 120.0, 1.0 / 120.0)
ewald_beta = 1.4
shift_scale = 0.9

def bspline(offset):
    folded = jnp.minimum(offset, 6.0 - offset)
    part_one = jnp.maximum(folded, 0.0)
    part_two = jnp.maximum(folded - 1.0, 0.0)
    part_three = jnp.maximum(folded - 2.0, 0.0)
    spline_val = (part_one ** 5 - 6.0 * part_two ** 5 + 15.0 * part_three ** 5) / 120.0
    spline_slope = (part_one ** 4 - 6.0 * part_two ** 4 + 15.0 * part_three ** 4) / 24.0
    return (spline_val, jnp.where(offset <= 3.0, spline_slope, -spline_slope))

def species_charge(species, charge_list):
    kind_ids = jnp.arange(len(charge_list), dtype=jnp.int32)
    levels = jnp.asarray(charge_list, jnp.float32)
    picked = jnp.where(species[None, :] == kind_ids[:, None], levels[:, None], 0.0)
    return lax.optimization_barrier(jnp.sum(picked, axis=0))

def fitting(descriptors, weight_in, bias_in, weight_mid, bias_mid, weight_out, bias_out):
    hidden = jnp.tanh(jnp.dot(descriptors, weight_in, preferred_element_type=jnp.float32) + bias_in).astype(jnp.bfloat16)
    for layer_idx in range(weight_mid.shape[0]):
        pre_act = jnp.dot(hidden, weight_mid[layer_idx], preferred_element_type=jnp.float32) + bias_mid[layer_idx]
        hidden = (hidden.astype(jnp.float32) + jnp.tanh(pre_act)).astype(jnp.bfloat16)
    output_raw = lax.dot_general(weight_out, hidden, (((1,), (1,)), ((), ())), preferred_element_type=jnp.float32)
    return shift_scale * jnp.tanh(output_raw + bias_out[:, None])

def axis_terms(index, length):
    signed = jnp.where(2 * index >= length, index - length, index).astype(jnp.float32) / length
    orders = jnp.arange(1, 6, dtype=jnp.int32)
    phases = (index[:, None] * orders[None, :] % length).astype(jnp.float32) * (2.0 * math.pi / length)
    coeffs = jnp.asarray(spline_coeffs, jnp.float32)
    real_sum = lax.optimization_barrier(jnp.sum(coeffs[None, :] * jnp.cos(phases), axis=1))
    imag_sum = lax.optimization_barrier(jnp.sum(coeffs[None, :] * jnp.sin(phases), axis=1))
    modulus = 1.0 / (real_sum * real_sum + imag_sum * imag_sum)
    damping = jnp.exp(-(math.pi / ewald_beta) ** 2 * signed * signed)
    return (signed * signed, damping * modulus)

def influence(z_index, z_len, y_index, y_len, x_index, x_len):
    z_sq, z_fac = axis_terms(z_index, z_len)
    y_sq, y_fac = axis_terms(y_index, y_len)
    x_sq, x_fac = axis_terms(x_index, x_len)
    squared = z_sq[:, None, None] + y_sq[None, :, None] + x_sq[None, None, :]
    safe_sq = jnp.where(squared > 0.0, squared, 1.0)
    volume = float(z_len * y_len * x_len)
    scaled = z_fac[:, None, None] * y_fac[None, :, None] * x_fac[None, None, :] / (math.pi * volume * safe_sq)
    return jnp.where(squared > 0.0, scaled, 0.0)

def reference(descriptors, species, bucket_count, base_index, fraction, weight_in, bias_in, weight_mid, bias_mid, weight_out, bias_out):
    z_len = CZ * N_SLAB
    y_len = CY * N_PENCIL
    x_len = NX
    blocks = N_SLAB * N_PENCIL
    slot_ids = jnp.arange(CAP, dtype=jnp.int32)
    in_use = (slot_ids[None, :] < bucket_count[:, None]).reshape(-1).astype(jnp.float32)
    charges = jnp.stack([species_charge(species, ion_table), species_charge(species, wannier_table)]) * in_use[None, :]

    def network(features):
        return fitting(features, weight_in, bias_in, weight_mid, bias_mid, weight_out, bias_out)
    centroid_shift, pullback = jax.vjp(network, descriptors)
    relative = jnp.stack([fraction, fraction + centroid_shift])
    block_charge = charges.reshape(2, blocks, ATOMS_DEV).transpose(1, 0, 2)
    block_rel = relative.reshape(2, 3, blocks, ATOMS_DEV).transpose(2, 0, 1, 3)
    block_base = base_index.reshape(3, blocks, ATOMS_DEV).transpose(1, 0, 2)
    grid_dims = jnp.asarray([z_len, y_len, x_len], jnp.int32)
    steps_idx = jnp.arange(8, dtype=jnp.int32)

    def stencil(rel_pos, base_pos):
        spline_val, spline_slope = bspline(rel_pos[..., None] - steps_idx.astype(jnp.float32) + 6.0)
        target = (base_pos[:, :, None] + steps_idx[None, None, :] - 3) % grid_dims[:, None, None]
        flat = (target[0][:, :, None, None] * y_len + target[1][:, None, :, None]) * x_len + target[2][:, None, None, :]
        return (spline_val, spline_slope, flat)

    def spread_block(grid_flat, inputs):
        charge, rel_pos, base_pos = inputs
        spline_val, spline_slope, flat = stencil(rel_pos, base_pos)
        amount = charge[:, :, None, None, None] * spline_val[:, 0, :, :, None, None] * spline_val[:, 1, :, None, :, None] * spline_val[:, 2, :, None, None, :]
        target_all = jnp.broadcast_to(flat[None], amount.shape).reshape(-1)
        return (grid_flat.at[target_all].add(amount.reshape(-1)), None)
    charge_grid, unused = lax.scan(spread_block, jnp.zeros(z_len * y_len * x_len, jnp.float32), (block_charge, block_rel, block_base))
    spectrum = jnp.fft.fftn(charge_grid.reshape(z_len, y_len, x_len))
    factor = influence(jnp.arange(z_len, dtype=jnp.int32), z_len, jnp.arange(y_len, dtype=jnp.int32), y_len, jnp.arange(x_len, dtype=jnp.int32), x_len)
    energy_sum = 0.5 * jnp.sum(factor * (jnp.real(spectrum) ** 2 + jnp.imag(spectrum) ** 2))
    potential = (jnp.real(jnp.fft.ifftn(factor * spectrum)) * float(z_len * y_len * x_len)).astype(jnp.float32).reshape(-1)

    def sample_block(inputs):
        charge, rel_pos, base_pos = inputs
        spline_val, spline_slope, flat = stencil(rel_pos, base_pos)
        patch = potential[flat]
        grad_z = jnp.einsum('kaz,kay,kax,azyx->ka', spline_slope[:, 0], spline_val[:, 1], spline_val[:, 2], patch)
        grad_y = jnp.einsum('kaz,kay,kax,azyx->ka', spline_val[:, 0], spline_slope[:, 1], spline_val[:, 2], patch)
        grad_x = jnp.einsum('kaz,kay,kax,azyx->ka', spline_val[:, 0], spline_val[:, 1], spline_slope[:, 2], patch)
        return -charge[:, None, :] * jnp.stack([grad_z, grad_y, grad_x], axis=1)
    forces = lax.map(sample_block, (block_charge, block_rel, block_base))
    site_forces = forces.transpose(1, 2, 0, 3).reshape(2, 3, -1)
    descriptor_grad, = pullback(-site_forces[1])
    energy = (energy_sum / float(ATOMS_DEV * blocks)).astype(jnp.float32)
    return (energy, site_forces, descriptor_grad)
```

```python
import math

import jax
import jax.numpy as jnp
from jax import lax
from jax.sharding import PartitionSpec as P

NX = 384
CZ = 16
CY = 48
BZ = 4


ion_table = (6.0, 1.0, 9.0, 7.0)
wannier_table = (-8.0, 0.0, -8.0, -8.0)
spline_coeffs = (1.0 / 120.0, 26.0 / 120.0, 66.0 / 120.0, 26.0 / 120.0, 1.0 / 120.0)
ewald_beta = 1.4
shift_scale = 0.9
highest = lax.Precision.HIGHEST


def extended(cells, sides, width):
    for axis, dim in sides:
        count = lax.axis_size(axis)
        head = lax.slice_in_dim(cells, 0, width, axis=dim)
        tail = lax.slice_in_dim(cells, cells.shape[dim] - width, cells.shape[dim], axis=dim)
        cells = jnp.concatenate(
            [
                lax.ppermute(tail, axis, [(i, (i + 1) % count) for i in range(count)]),
                cells,
                lax.ppermute(head, axis, [((i + 1) % count, i) for i in range(count)]),
            ],
            axis=dim,
        )
    return cells


def bspline(offset):
    folded = jnp.minimum(offset, 6.0 - offset)
    part_one = jnp.maximum(folded, 0.0)
    part_two = jnp.maximum(folded - 1.0, 0.0)
    part_three = jnp.maximum(folded - 2.0, 0.0)
    spline_val = (part_one**5 - 6.0 * part_two**5 + 15.0 * part_three**5) / 120.0
    spline_slope = (part_one**4 - 6.0 * part_two**4 + 15.0 * part_three**4) / 24.0
    return (spline_val, jnp.where(offset <= 3.0, spline_slope, -spline_slope))


def species_charge(species, charge_list):
    kind_ids = jnp.arange(len(charge_list), dtype=jnp.int32)
    levels = jnp.asarray(charge_list, jnp.float32)
    picked = jnp.where(species[None, :] == kind_ids[:, None], levels[:, None], 0.0)
    return jnp.sum(picked, axis=0)


def fitting(descriptors, weight_in, bias_in, weight_mid, bias_mid, weight_out, bias_out):
    hidden = jnp.tanh(
        jnp.dot(descriptors, weight_in, preferred_element_type=jnp.float32) + bias_in
    ).astype(jnp.bfloat16)
    for layer_idx in range(weight_mid.shape[0]):
        pre_act = (
            jnp.dot(hidden, weight_mid[layer_idx], preferred_element_type=jnp.float32)
            + bias_mid[layer_idx]
        )
        hidden = (hidden.astype(jnp.float32) + jnp.tanh(pre_act)).astype(jnp.bfloat16)
    output_raw = lax.dot_general(
        weight_out, hidden, (((1,), (1,)), ((), ())), preferred_element_type=jnp.float32
    )
    return shift_scale * jnp.tanh(output_raw + bias_out[:, None])


def axis_terms(index, length):
    signed = jnp.where(2 * index >= length, index - length, index).astype(jnp.float32) / length
    orders = jnp.arange(1, 6, dtype=jnp.int32)
    phases = (index[:, None] * orders[None, :] % length).astype(jnp.float32) * (
        2.0 * math.pi / length
    )
    coeffs = jnp.asarray(spline_coeffs, jnp.float32)
    real_sum = jnp.sum(coeffs[None, :] * jnp.cos(phases), axis=1)
    imag_sum = jnp.sum(coeffs[None, :] * jnp.sin(phases), axis=1)
    modulus = 1.0 / (real_sum * real_sum + imag_sum * imag_sum)
    damping = jnp.exp(-((math.pi / ewald_beta) ** 2) * signed * signed)
    return (signed * signed, damping * modulus)


def influence(z_index, z_len, y_index, y_len, x_index, x_len):
    z_sq, z_fac = axis_terms(z_index, z_len)
    y_sq, y_fac = axis_terms(y_index, y_len)
    x_sq, x_fac = axis_terms(x_index, x_len)
    squared = z_sq[:, None, None] + y_sq[None, :, None] + x_sq[None, None, :]
    safe_sq = jnp.where(squared > 0.0, squared, 1.0)
    volume = float(z_len * y_len * x_len)
    scaled = (
        z_fac[:, None, None]
        * y_fac[None, :, None]
        * x_fac[None, None, :]
        / (math.pi * volume * safe_sq)
    )
    return jnp.where(squared > 0.0, scaled, 0.0)


def dft_table(length):
    index = jnp.arange(length, dtype=jnp.int32)
    angles = (index[:, None] * index[None, :] % length).astype(jnp.float32) * (
        2.0 * math.pi / length
    )
    return (jnp.cos(angles), jnp.sin(angles))


def half_table(length, width):
    positions = jnp.arange(length, dtype=jnp.int32)
    wave_ids = jnp.arange(width, dtype=jnp.int32)
    angles = (positions[:, None] * wave_ids[None, :] % length).astype(jnp.float32) * (
        2.0 * math.pi / length
    )
    kept_mask = (2 * wave_ids <= length).astype(jnp.float32)
    doubled = (
        jnp.where((wave_ids == 0) | (2 * wave_ids == length), 1.0, 2.0).astype(jnp.float32)
        * kept_mask
    )
    return (jnp.cos(angles) * kept_mask[None, :], jnp.sin(angles) * kept_mask[None, :], doubled)


def dense_window(relative, start, length):
    cell_ids = jnp.arange(length, dtype=jnp.int32)
    distance = jnp.mod(cell_ids[None, :] - start[:, None], length).astype(jnp.float32)
    return bspline(relative[:, None] - distance + 6.0)


def lead_product(table, data, dim):
    return lax.dot_general(table, data, (((1,), (dim,)), ((), ())), precision=highest)


def forward_pair(cosine, sine, real_part, imag_part, dim):
    real_cos = lead_product(cosine, real_part, dim)
    imag_sin = lead_product(sine, imag_part, dim)
    imag_cos = lead_product(cosine, imag_part, dim)
    real_sin = lead_product(sine, real_part, dim)
    return (real_cos + imag_sin, imag_cos - real_sin)


def inverse_pair(cosine, sine, real_part, imag_part, dim):
    real_cos = lead_product(cosine, real_part, dim)
    imag_sin = lead_product(sine, imag_part, dim)
    imag_cos = lead_product(cosine, imag_part, dim)
    real_sin = lead_product(sine, real_part, dim)
    return (real_cos - imag_sin, real_sin + imag_cos)


def body(
    descriptors,
    species,
    bucket_count,
    base_index,
    fraction,
    weight_in,
    bias_in,
    weight_mid,
    bias_mid,
    weight_out,
    bias_out,
):
    n_slab = lax.axis_size("slab")
    n_pencil = lax.axis_size("pencil")
    slab_idx = lax.axis_index("slab")
    pencil_idx = lax.axis_index("pencil")
    rows_all = CY * n_pencil
    planes_all = CZ * n_slab
    row_part = rows_all // n_slab
    half_cols = NX // 2 + 1
    wave_cols = -(-half_cols // n_pencil) * n_pencil
    column_part = wave_cols // n_pencil
    n_buckets = bucket_count.shape[0]
    capacity = species.shape[0] // n_buckets
    site_count = 2 * capacity
    slot_ids = jnp.arange(capacity, dtype=jnp.int32)
    in_use = (slot_ids[None, :] < bucket_count[:, None]).reshape(-1).astype(jnp.float32)
    charges = (
        jnp.stack([species_charge(species, ion_table), species_charge(species, wannier_table)])
        * in_use[None, :]
    )

    def network(features):
        return fitting(features, weight_in, bias_in, weight_mid, bias_mid, weight_out, bias_out)

    centroid_shift, pullback = jax.vjp(network, descriptors)
    relative = jnp.stack([fraction, fraction + centroid_shift])
    anchor = jnp.stack([slab_idx * CZ, pencil_idx * CY, jnp.zeros((), jnp.int32)])
    local_base = base_index - anchor[:, None]
    site_charge = (
        charges.reshape(2, n_buckets, capacity).transpose(1, 0, 2).reshape(n_buckets, site_count)
    )
    site_rel = (
        relative.reshape(2, 3, n_buckets, capacity)
        .transpose(2, 1, 0, 3)
        .reshape(n_buckets, 3, site_count)
    )
    site_base = jnp.broadcast_to(
        local_base.reshape(3, n_buckets, 1, capacity), (3, n_buckets, 2, capacity)
    )
    site_base = site_base.transpose(1, 0, 2, 3).reshape(n_buckets, 3, site_count)
    bucket_ids = jnp.arange(n_buckets, dtype=jnp.int32)
    window_shape = (BZ + 8, CY + 8, NX)
    zero_index = jnp.zeros((), jnp.int32)

    def spread_step(grid_now, inputs):
        bucket, charge, rel_pos, base_pos = inputs
        plane_val, plane_slope = dense_window(rel_pos[0], base_pos[0] - bucket * BZ + 1, BZ + 8)
        row_val, row_slope = dense_window(rel_pos[1], base_pos[1] + 1, CY + 8)
        col_val, col_slope = dense_window(rel_pos[2], base_pos[2] - 3, NX)
        outer_prod = ((charge[:, None] * plane_val)[:, :, None] * row_val[:, None, :]).reshape(
            site_count, -1
        )
        block_sum = lax.dot_general(
            outer_prod, col_val, (((0,), (0,)), ((), ())), precision=highest
        )
        corner = (bucket * BZ, zero_index, zero_index)
        current = lax.dynamic_slice(grid_now, corner, window_shape)
        grid_now = lax.dynamic_update_slice(
            grid_now, current + block_sum.reshape(window_shape), corner
        )
        return (grid_now, (col_val, col_slope))

    charge_grid, windows = lax.scan(
        spread_step,
        jnp.zeros((CZ + 8, CY + 8, NX), jnp.float32),
        (bucket_ids, site_charge, site_rel, site_base),
    )
    half_cos, half_sin, doubled = half_table(NX, wave_cols)
    forward_rows = jnp.stack([half_cos.T, -half_sin.T], axis=1).reshape(2 * wave_cols, NX)
    inverse_rows = jnp.stack(
        [(half_cos * doubled[None, :]).T, (-half_sin * doubled[None, :]).T], axis=0
    )
    row_cos, row_sin = dft_table(rows_all)
    plane_cos, plane_sin = dft_table(planes_all)
    rim_planes = jnp.concatenate([charge_grid[:4], charge_grid[CZ + 4 :]], axis=0)
    arrived = extended(rim_planes, (("slab", 0),), 4)
    inner_grid = charge_grid[4 : CZ + 4].at[:4].add(arrived[:4]).at[CZ - 4 :].add(arrived[12:])
    rim_rows = jnp.concatenate([inner_grid[:, :4], inner_grid[:, CY + 4 :]], axis=1)
    arrived = extended(rim_rows, (("pencil", 1),), 4)
    source_grid = (
        inner_grid[:, 4 : CY + 4].at[:, :4].add(arrived[:, :4]).at[:, CY - 4 :].add(arrived[:, 12:])
    )
    plane_here = source_grid.shape[0]
    row_here = source_grid.shape[1]
    spectrum = lead_product(forward_rows, source_grid, 2).reshape(
        wave_cols, 2, plane_here, row_here
    )
    spectrum = lax.all_to_all(spectrum, "pencil", split_axis=0, concat_axis=3, tiled=True)
    real_y, imag_y = forward_pair(row_cos, row_sin, spectrum[:, 0], spectrum[:, 1], 2)
    spectrum = jnp.stack([real_y, imag_y], axis=1)
    spectrum = lax.all_to_all(spectrum, "slab", split_axis=0, concat_axis=3, tiled=True)
    real_z, imag_z = forward_pair(plane_cos, plane_sin, spectrum[:, 0], spectrum[:, 1], 2)
    x_ids = pencil_idx * column_part + jnp.arange(column_part, dtype=jnp.int32)
    factor = influence(
        jnp.arange(planes_all, dtype=jnp.int32),
        planes_all,
        slab_idx * row_part + jnp.arange(row_part, dtype=jnp.int32),
        rows_all,
        x_ids,
        NX,
    )
    weighted_real = real_z * factor
    weighted_imag = imag_z * factor
    power = weighted_real * real_z + weighted_imag * imag_z
    x_weight = jnp.where((x_ids == 0) | (2 * x_ids == NX), 1.0, 2.0).astype(jnp.float32)
    x_weight = x_weight * (2 * x_ids <= NX).astype(jnp.float32)
    energy_terms = 0.5 * jnp.sum(power * x_weight)
    energy_sum = lax.psum(energy_terms, ("slab", "pencil"))
    back_real, back_imag = inverse_pair(plane_cos, plane_sin, weighted_real, weighted_imag, 0)
    returned = jnp.stack([back_real, back_imag], axis=1)
    returned = lax.all_to_all(returned, "slab", split_axis=0, concat_axis=2, tiled=True)
    back_real, back_imag = inverse_pair(row_cos, row_sin, returned[:, 0], returned[:, 1], 1)
    returned = jnp.stack([back_real, back_imag], axis=1)
    returned = lax.all_to_all(returned, "pencil", split_axis=0, concat_axis=3, tiled=True)
    potential = lax.dot_general(
        returned, inverse_rows, (((1, 3), (0, 1)), ((), ())), precision=highest
    )
    potential = extended(potential, (("slab", 1), ("pencil", 0)), 4)

    flat_ids = jnp.arange((CY + 8) * (BZ + 8), dtype=jnp.int32)
    flat_row = (flat_ids // (BZ + 8)).astype(jnp.float32)
    flat_plane = (flat_ids % (BZ + 8)).astype(jnp.float32)

    def sample_step(inputs):
        bucket, rel_pos, base_pos, col_val, col_slope = inputs
        corner = (zero_index, bucket * BZ, zero_index)
        patch = lax.dynamic_slice(potential, corner, (CY + 8, BZ + 8, NX)).reshape(-1, NX)
        stacked = jnp.concatenate([col_val, col_slope], axis=0)
        both = lax.dot_general(stacked, patch, (((1,), (1,)), ((), ())), precision=highest)
        along = both[:site_count]
        across = both[site_count:]
        plane_first = (base_pos[0] - bucket * BZ + 1).astype(jnp.float32)
        row_first = (base_pos[1] + 1).astype(jnp.float32)
        plane_val, plane_slope = bspline(
            rel_pos[0][:, None] - (flat_plane[None, :] - plane_first[:, None]) + 6.0
        )
        row_val, row_slope = bspline(
            rel_pos[1][:, None] - (flat_row[None, :] - row_first[:, None]) + 6.0
        )
        grad_z = jnp.sum(plane_slope * row_val * along, axis=1)
        grad_y = jnp.sum(plane_val * row_slope * along, axis=1)
        grad_x = jnp.sum(plane_val * row_val * across, axis=1)
        return jnp.stack([grad_z, grad_y, grad_x])

    slopes = lax.map(sample_step, (bucket_ids, site_rel, site_base, windows[0], windows[1]))
    forces = -site_charge[:, None, :] * slopes
    site_forces = forces.reshape(n_buckets, 3, 2, capacity).transpose(2, 1, 0, 3).reshape(2, 3, -1)
    (descriptor_grad,) = pullback(-site_forces[1])
    total_slots = species.shape[0] * n_slab * n_pencil
    energy = energy_sum / float(total_slots)
    return (energy, site_forces, descriptor_grad)


def solution(mesh):
    in_specs = (
        P(("slab", "pencil"), None),
        P(("slab", "pencil")),
        P(("slab", "pencil")),
        P(None, ("slab", "pencil")),
        P(None, ("slab", "pencil")),
        P(),
        P(),
        P(),
        P(),
        P(),
        P(),
    )
    out_specs = (P(), P(None, None, ("slab", "pencil")), P(("slab", "pencil"), None))
    return jax.shard_map(body, mesh=mesh, in_specs=in_specs, out_specs=out_specs, check_vma=False)
```

```python
import math

import jax
import jax.numpy as jnp
from jax import lax
from jax.sharding import PartitionSpec as P

NX = 384
CZ = 16
CY = 48
BZ = 4


ion_table = (6.0, 1.0, 9.0, 7.0)
wannier_table = (-8.0, 0.0, -8.0, -8.0)
spline_coeffs = (1.0 / 120.0, 26.0 / 120.0, 66.0 / 120.0, 26.0 / 120.0, 1.0 / 120.0)
ewald_beta = 1.4
shift_scale = 0.9
highest = lax.Precision.HIGHEST


def extended(cells, sides, width):
    for axis, dim in sides:
        count = lax.axis_size(axis)
        head = lax.slice_in_dim(cells, 0, width, axis=dim)
        tail = lax.slice_in_dim(cells, cells.shape[dim] - width, cells.shape[dim], axis=dim)
        cells = jnp.concatenate(
            [
                lax.ppermute(tail, axis, [(i, (i + 1) % count) for i in range(count)]),
                cells,
                lax.ppermute(head, axis, [((i + 1) % count, i) for i in range(count)]),
            ],
            axis=dim,
        )
    return cells


def bspline(offset):
    folded = jnp.minimum(offset, 6.0 - offset)
    part_one = jnp.maximum(folded, 0.0)
    part_two = jnp.maximum(folded - 1.0, 0.0)
    part_three = jnp.maximum(folded - 2.0, 0.0)
    spline_val = (part_one**5 - 6.0 * part_two**5 + 15.0 * part_three**5) / 120.0
    spline_slope = (part_one**4 - 6.0 * part_two**4 + 15.0 * part_three**4) / 24.0
    return (spline_val, jnp.where(offset <= 3.0, spline_slope, -spline_slope))


def species_charge(species, charge_list):
    kind_ids = jnp.arange(len(charge_list), dtype=jnp.int32)
    levels = jnp.asarray(charge_list, jnp.float32)
    picked = jnp.where(species[None, :] == kind_ids[:, None], levels[:, None], 0.0)
    return jnp.sum(picked, axis=0)


def fitting(descriptors, weight_in, bias_in, weight_mid, bias_mid, weight_out, bias_out):
    hidden = jnp.tanh(
        jnp.dot(descriptors, weight_in, preferred_element_type=jnp.float32) + bias_in
    ).astype(jnp.bfloat16)
    for layer_idx in range(weight_mid.shape[0]):
        pre_act = (
            jnp.dot(hidden, weight_mid[layer_idx], preferred_element_type=jnp.float32)
            + bias_mid[layer_idx]
        )
        hidden = (hidden.astype(jnp.float32) + jnp.tanh(pre_act)).astype(jnp.bfloat16)
    output_raw = lax.dot_general(
        weight_out, hidden, (((1,), (1,)), ((), ())), preferred_element_type=jnp.float32
    )
    return shift_scale * jnp.tanh(output_raw + bias_out[:, None])


def axis_terms(index, length):
    signed = jnp.where(2 * index >= length, index - length, index).astype(jnp.float32) / length
    orders = jnp.arange(1, 6, dtype=jnp.int32)
    phases = (index[:, None] * orders[None, :] % length).astype(jnp.float32) * (
        2.0 * math.pi / length
    )
    coeffs = jnp.asarray(spline_coeffs, jnp.float32)
    real_sum = jnp.sum(coeffs[None, :] * jnp.cos(phases), axis=1)
    imag_sum = jnp.sum(coeffs[None, :] * jnp.sin(phases), axis=1)
    modulus = 1.0 / (real_sum * real_sum + imag_sum * imag_sum)
    damping = jnp.exp(-((math.pi / ewald_beta) ** 2) * signed * signed)
    return (signed * signed, damping * modulus)


def influence(z_index, z_len, y_index, y_len, x_index, x_len):
    z_sq, z_fac = axis_terms(z_index, z_len)
    y_sq, y_fac = axis_terms(y_index, y_len)
    x_sq, x_fac = axis_terms(x_index, x_len)
    squared = z_sq[:, None, None] + y_sq[None, :, None] + x_sq[None, None, :]
    safe_sq = jnp.where(squared > 0.0, squared, 1.0)
    volume = float(z_len * y_len * x_len)
    scaled = (
        z_fac[:, None, None]
        * y_fac[None, :, None]
        * x_fac[None, None, :]
        / (math.pi * volume * safe_sq)
    )
    return jnp.where(squared > 0.0, scaled, 0.0)


def block_table(length, sign):
    index = jnp.arange(length, dtype=jnp.int32)
    angles = (index[:, None] * index[None, :] % length).astype(jnp.float32) * (
        2.0 * math.pi / length
    )
    cosine = jnp.cos(angles)
    sine = jnp.sin(angles) * sign
    return jnp.stack([jnp.stack([cosine, -sine], axis=1), jnp.stack([sine, cosine], axis=1)])


def x_tables(length, part, count):
    positions = jnp.arange(length, dtype=jnp.int32)
    wave_ids = jnp.arange(part * count, dtype=jnp.int32)
    angles = (wave_ids[:, None] * positions[None, :] % length).astype(jnp.float32) * (
        2.0 * math.pi / length
    )
    kept_mask = (2 * wave_ids <= length).astype(jnp.float32)
    doubled = (
        jnp.where((wave_ids == 0) | (2 * wave_ids == length), 1.0, 2.0).astype(jnp.float32)
        * kept_mask
    )
    cosine = jnp.cos(angles).reshape(count, 1, part, length)
    sine = jnp.sin(angles).reshape(count, 1, part, length)
    kept = kept_mask.reshape(count, 1, part, 1)
    twice = doubled.reshape(count, 1, part, 1)
    forward = jnp.concatenate([cosine * kept, -sine * kept], axis=1)
    inverse = jnp.concatenate([cosine * twice, -sine * twice], axis=1)
    return (forward.reshape(-1, length), inverse.reshape(-1, length))


def dense_window(relative, start, length):
    cell_ids = jnp.arange(length, dtype=jnp.int32)
    distance = jnp.mod(cell_ids[None, :] - start[:, None], length).astype(jnp.float32)
    return bspline(relative[:, None] - distance + 6.0)


def body(
    descriptors,
    species,
    bucket_count,
    base_index,
    fraction,
    weight_in,
    bias_in,
    weight_mid,
    bias_mid,
    weight_out,
    bias_out,
):
    n_slab = lax.axis_size("slab")
    n_pencil = lax.axis_size("pencil")
    slab_idx = lax.axis_index("slab")
    pencil_idx = lax.axis_index("pencil")
    rows_all = CY * n_pencil
    planes_all = CZ * n_slab
    half_cols = NX // 2 + 1
    n_buckets = bucket_count.shape[0]
    capacity = species.shape[0] // n_buckets
    site_count = 2 * capacity
    slot_ids = jnp.arange(capacity, dtype=jnp.int32)
    in_use = (slot_ids[None, :] < bucket_count[:, None]).reshape(-1).astype(jnp.float32)
    charges = (
        jnp.stack([species_charge(species, ion_table), species_charge(species, wannier_table)])
        * in_use[None, :]
    )

    def network(features):
        return fitting(features, weight_in, bias_in, weight_mid, bias_mid, weight_out, bias_out)

    centroid_shift, pullback = jax.vjp(network, descriptors)
    relative = jnp.stack([fraction, fraction + centroid_shift])
    anchor = jnp.stack([slab_idx * CZ, pencil_idx * CY, jnp.zeros((), jnp.int32)])
    local_base = base_index - anchor[:, None]
    site_charge = (
        charges.reshape(2, n_buckets, capacity).transpose(1, 0, 2).reshape(n_buckets, site_count)
    )
    site_rel = (
        relative.reshape(2, 3, n_buckets, capacity)
        .transpose(2, 1, 0, 3)
        .reshape(n_buckets, 3, site_count)
    )
    site_base = jnp.broadcast_to(
        local_base.reshape(3, n_buckets, 1, capacity), (3, n_buckets, 2, capacity)
    )
    site_base = site_base.transpose(1, 0, 2, 3).reshape(n_buckets, 3, site_count)
    bucket_ids = jnp.arange(n_buckets, dtype=jnp.int32)
    window_shape = (BZ + 8, CY + 8, NX)
    zero_index = jnp.zeros((), jnp.int32)

    def spread_step(grid_now, inputs):
        bucket, charge, rel_pos, base_pos = inputs
        plane_val, plane_slope = dense_window(rel_pos[0], base_pos[0] - bucket * BZ + 1, BZ + 8)
        row_val, row_slope = dense_window(rel_pos[1], base_pos[1] + 1, CY + 8)
        col_val, col_slope = dense_window(rel_pos[2], base_pos[2] - 3, NX)
        outer_prod = ((charge[:, None] * plane_val)[:, :, None] * row_val[:, None, :]).reshape(
            site_count, -1
        )
        block_sum = lax.dot_general(
            outer_prod, col_val, (((0,), (0,)), ((), ())), precision=highest
        )
        corner = (bucket * BZ, zero_index, zero_index)
        current = lax.dynamic_slice(grid_now, corner, window_shape)
        grid_now = lax.dynamic_update_slice(
            grid_now, current + block_sum.reshape(window_shape), corner
        )
        return (grid_now, (col_val, col_slope))

    charge_grid, windows = lax.scan(
        spread_step,
        jnp.zeros((CZ + 8, CY + 8, NX), jnp.float32),
        (bucket_ids, site_charge, site_rel, site_base),
    )
    rim_planes = jnp.concatenate([charge_grid[:4], charge_grid[CZ + 4 :]], axis=0)
    arrived = extended(rim_planes, (("slab", 0),), 4)
    inner_grid = charge_grid[4 : CZ + 4].at[:4].add(arrived[:4]).at[CZ - 4 :].add(arrived[12:])
    rim_rows = jnp.concatenate([inner_grid[:, :4], inner_grid[:, CY + 4 :]], axis=1)
    arrived = extended(rim_rows, (("pencil", 1),), 4)
    source_grid = (
        inner_grid[:, 4 : CY + 4].at[:, :4].add(arrived[:, :4]).at[:, CY - 4 :].add(arrived[:, 12:])
    )
    rows_wave = rows_all // n_slab
    column_part = -(-(-(-half_cols // n_pencil)) // 4) * 4
    wave_all = column_part * n_pencil
    x_ids = pencil_idx * column_part + jnp.arange(column_part, dtype=jnp.int32)
    forward_x, inverse_x = x_tables(NX, column_part, n_pencil)
    forward_y = block_table(rows_all, -1.0).reshape(2, n_slab, rows_wave, 2 * rows_all)
    forward_y = forward_y.transpose(1, 0, 2, 3).reshape(2 * rows_all, 2 * rows_all)
    forward_z = block_table(planes_all, -1.0).reshape(2 * planes_all, 2 * planes_all)
    inverse_z = block_table(planes_all, 1.0).reshape(2, n_slab, CZ, 2 * planes_all)
    inverse_z = inverse_z.transpose(1, 0, 2, 3).reshape(2 * planes_all, 2 * planes_all)
    inverse_y = block_table(rows_all, 1.0).reshape(2, n_pencil, CY, 2 * rows_all)
    inverse_y = inverse_y.transpose(1, 0, 2, 3).reshape(2 * rows_all, 2 * rows_all)
    wave_x = lax.dot_general(
        forward_x, source_grid.reshape(CZ * CY, NX), (((1,), (1,)), ((), ())), precision=highest
    )
    wave_x = lax.all_to_all(
        wave_x.reshape(n_pencil, 2 * column_part, CZ * CY), "pencil", 0, 0, tiled=True
    )
    wave_x = wave_x.reshape(n_pencil, 2, column_part, CZ, CY).transpose(1, 0, 4, 2, 3)
    wave_y = jnp.dot(forward_y, wave_x.reshape(2 * rows_all, column_part * CZ), precision=highest)
    wave_y = lax.all_to_all(
        wave_y.reshape(n_slab, 2 * rows_wave, column_part * CZ), "slab", 0, 0, tiled=True
    )
    wave_y = wave_y.reshape(n_slab, 2, rows_wave, column_part, CZ).transpose(1, 0, 4, 2, 3)
    wave_z = jnp.dot(
        forward_z, wave_y.reshape(2 * planes_all, rows_wave * column_part), precision=highest
    ).reshape(2, planes_all, rows_wave, column_part)
    factor = influence(
        jnp.arange(planes_all, dtype=jnp.int32),
        planes_all,
        slab_idx * rows_wave + jnp.arange(rows_wave, dtype=jnp.int32),
        rows_all,
        x_ids,
        NX,
    )
    weighted = wave_z * factor[None]
    power = weighted[0] * wave_z[0] + weighted[1] * wave_z[1]
    x_weight = jnp.where((x_ids == 0) | (2 * x_ids == NX), 1.0, 2.0).astype(jnp.float32)
    x_weight = x_weight * (2 * x_ids <= NX).astype(jnp.float32)
    energy_terms = 0.5 * jnp.sum(power * x_weight)
    energy_sum = lax.psum(lax.psum(energy_terms, "pencil"), "slab")
    back_z = jnp.dot(
        inverse_z, weighted.reshape(2 * planes_all, rows_wave * column_part), precision=highest
    )
    back_z = lax.all_to_all(
        back_z.reshape(n_slab, 2 * CZ, rows_wave * column_part), "slab", 0, 0, tiled=True
    )
    back_z = back_z.reshape(n_slab, 2, CZ, rows_wave, column_part).transpose(1, 0, 3, 2, 4)
    back_y = jnp.dot(inverse_y, back_z.reshape(2 * rows_all, CZ * column_part), precision=highest)
    back_y = lax.all_to_all(
        back_y.reshape(n_pencil, 2 * CY, CZ * column_part), "pencil", 0, 0, tiled=True
    )
    back_y = back_y.reshape(n_pencil, 2, CY, CZ, column_part).transpose(0, 1, 4, 3, 2)
    potential = lax.dot_general(
        back_y.reshape(2 * wave_all, CZ * CY), inverse_x, (((0,), (0,)), ((), ())), precision=highest
    ).reshape(CZ, CY, NX)
    potential = extended(potential, (("slab", 0), ("pencil", 1)), 4)

    flat_ids = jnp.arange((CY + 8) * (BZ + 8), dtype=jnp.int32)
    flat_row = (flat_ids % (CY + 8)).astype(jnp.float32)
    flat_plane = (flat_ids // (CY + 8)).astype(jnp.float32)

    def sample_step(inputs):
        bucket, rel_pos, base_pos, col_val, col_slope = inputs
        corner = (bucket * BZ, zero_index, zero_index)
        patch = lax.dynamic_slice(potential, corner, (BZ + 8, CY + 8, NX)).reshape(-1, NX)
        stacked = jnp.concatenate([col_val, col_slope], axis=0)
        both = lax.dot_general(stacked, patch, (((1,), (1,)), ((), ())), precision=highest)
        along = both[:site_count]
        across = both[site_count:]
        plane_first = (base_pos[0] - bucket * BZ + 1).astype(jnp.float32)
        row_first = (base_pos[1] + 1).astype(jnp.float32)
        plane_val, plane_slope = bspline(
            rel_pos[0][:, None] - (flat_plane[None, :] - plane_first[:, None]) + 6.0
        )
        row_val, row_slope = bspline(
            rel_pos[1][:, None] - (flat_row[None, :] - row_first[:, None]) + 6.0
        )
        grad_z = jnp.sum(plane_slope * row_val * along, axis=1)
        grad_y = jnp.sum(plane_val * row_slope * along, axis=1)
        grad_x = jnp.sum(plane_val * row_val * across, axis=1)
        return jnp.stack([grad_z, grad_y, grad_x])

    slopes = lax.map(sample_step, (bucket_ids, site_rel, site_base, windows[0], windows[1]))
    forces = -site_charge[:, None, :] * slopes
    site_forces = forces.reshape(n_buckets, 3, 2, capacity).transpose(2, 1, 0, 3).reshape(2, 3, -1)
    (descriptor_grad,) = pullback(-site_forces[1])
    total_slots = species.shape[0] * n_slab * n_pencil
    energy = energy_sum / float(total_slots)
    return (energy, site_forces, descriptor_grad)


def solution(mesh):
    in_specs = (
        P(("slab", "pencil"), None),
        P(("slab", "pencil")),
        P(("slab", "pencil")),
        P(None, ("slab", "pencil")),
        P(None, ("slab", "pencil")),
        P(),
        P(),
        P(),
        P(),
        P(),
        P(),
    )
    out_specs = (P(), P(None, None, ("slab", "pencil")), P(("slab", "pencil"), None))
    return jax.shard_map(body, mesh=mesh, in_specs=in_specs, out_specs=out_specs, check_vma=False)
```

```python
import math

import jax
import jax.numpy as jnp
from jax import lax
from jax.sharding import PartitionSpec as P

NX = 384
CZ = 16
CY = 48
BZ = 4


ion_table = (6.0, 1.0, 9.0, 7.0)
wannier_table = (-8.0, 0.0, -8.0, -8.0)
spline_coeffs = (1.0 / 120.0, 26.0 / 120.0, 66.0 / 120.0, 26.0 / 120.0, 1.0 / 120.0)
ewald_beta = 1.4
shift_scale = 0.9
three_pass = lax.Precision.HIGH


def extended(cells, sides, width):
    for axis, dim in sides:
        count = lax.axis_size(axis)
        head = lax.slice_in_dim(cells, 0, width, axis=dim)
        tail = lax.slice_in_dim(cells, cells.shape[dim] - width, cells.shape[dim], axis=dim)
        cells = jnp.concatenate(
            [
                lax.ppermute(tail, axis, [(i, (i + 1) % count) for i in range(count)]),
                cells,
                lax.ppermute(head, axis, [((i + 1) % count, i) for i in range(count)]),
            ],
            axis=dim,
        )
    return cells


def bspline(offset):
    folded = jnp.minimum(offset, 6.0 - offset)
    part_one = jnp.maximum(folded, 0.0)
    part_two = jnp.maximum(folded - 1.0, 0.0)
    part_three = jnp.maximum(folded - 2.0, 0.0)
    spline_val = (part_one**5 - 6.0 * part_two**5 + 15.0 * part_three**5) / 120.0
    spline_slope = (part_one**4 - 6.0 * part_two**4 + 15.0 * part_three**4) / 24.0
    return (spline_val, jnp.where(offset <= 3.0, spline_slope, -spline_slope))


def species_charge(species, charge_list):
    kind_ids = jnp.arange(len(charge_list), dtype=jnp.int32)
    levels = jnp.asarray(charge_list, jnp.float32)
    picked = jnp.where(species[None, :] == kind_ids[:, None], levels[:, None], 0.0)
    return jnp.sum(picked, axis=0)


def fitting(descriptors, weight_in, bias_in, weight_mid, bias_mid, weight_out, bias_out):
    hidden = jnp.tanh(
        jnp.dot(descriptors, weight_in, preferred_element_type=jnp.float32) + bias_in
    ).astype(jnp.bfloat16)
    for layer_idx in range(weight_mid.shape[0]):
        pre_act = (
            jnp.dot(hidden, weight_mid[layer_idx], preferred_element_type=jnp.float32)
            + bias_mid[layer_idx]
        )
        hidden = (hidden.astype(jnp.float32) + jnp.tanh(pre_act)).astype(jnp.bfloat16)
    output_raw = lax.dot_general(
        weight_out, hidden, (((1,), (1,)), ((), ())), preferred_element_type=jnp.float32
    )
    return shift_scale * jnp.tanh(output_raw + bias_out[:, None])


def axis_terms(index, length):
    signed = jnp.where(2 * index >= length, index - length, index).astype(jnp.float32) / length
    orders = jnp.arange(1, 6, dtype=jnp.int32)
    phases = (index[:, None] * orders[None, :] % length).astype(jnp.float32) * (
        2.0 * math.pi / length
    )
    coeffs = jnp.asarray(spline_coeffs, jnp.float32)
    real_sum = jnp.sum(coeffs[None, :] * jnp.cos(phases), axis=1)
    imag_sum = jnp.sum(coeffs[None, :] * jnp.sin(phases), axis=1)
    modulus = 1.0 / (real_sum * real_sum + imag_sum * imag_sum)
    damping = jnp.exp(-((math.pi / ewald_beta) ** 2) * signed * signed)
    return (signed * signed, damping * modulus)


def influence(z_index, z_len, y_index, y_len, x_index, x_len):
    z_sq, z_fac = axis_terms(z_index, z_len)
    y_sq, y_fac = axis_terms(y_index, y_len)
    x_sq, x_fac = axis_terms(x_index, x_len)
    squared = z_sq[:, None, None] + y_sq[None, :, None] + x_sq[None, None, :]
    safe_sq = jnp.where(squared > 0.0, squared, 1.0)
    volume = float(z_len * y_len * x_len)
    scaled = (
        z_fac[:, None, None]
        * y_fac[None, :, None]
        * x_fac[None, None, :]
        / (math.pi * volume * safe_sq)
    )
    return jnp.where(squared > 0.0, scaled, 0.0)


def block_table(length, sign):
    index = jnp.arange(length, dtype=jnp.int32)
    angles = (index[:, None] * index[None, :] % length).astype(jnp.float32) * (
        2.0 * math.pi / length
    )
    cosine = jnp.cos(angles)
    sine = jnp.sin(angles) * sign
    return jnp.stack([jnp.stack([cosine, -sine], axis=1), jnp.stack([sine, cosine], axis=1)])


def x_tables(length, part, count):
    positions = jnp.arange(length, dtype=jnp.int32)
    wave_ids = jnp.arange(part * count, dtype=jnp.int32)
    angles = (wave_ids[:, None] * positions[None, :] % length).astype(jnp.float32) * (
        2.0 * math.pi / length
    )
    kept_mask = (2 * wave_ids <= length).astype(jnp.float32)
    doubled = (
        jnp.where((wave_ids == 0) | (2 * wave_ids == length), 1.0, 2.0).astype(jnp.float32)
        * kept_mask
    )
    cosine = jnp.cos(angles).reshape(count, 1, part, length)
    sine = jnp.sin(angles).reshape(count, 1, part, length)
    kept = kept_mask.reshape(count, 1, part, 1)
    twice = doubled.reshape(count, 1, part, 1)
    forward = jnp.concatenate([cosine * kept, -sine * kept], axis=1)
    inverse = jnp.concatenate([cosine * twice, -sine * twice], axis=1)
    return (forward.reshape(-1, length), inverse.reshape(-1, length))


def dense_window(relative, start, length):
    cell_ids = jnp.arange(length, dtype=jnp.int32)
    distance = jnp.mod(cell_ids[None, :] - start[:, None], length).astype(jnp.float32)
    return bspline(relative[:, None] - distance + 6.0)


def body(
    descriptors,
    species,
    bucket_count,
    base_index,
    fraction,
    weight_in,
    bias_in,
    weight_mid,
    bias_mid,
    weight_out,
    bias_out,
):
    n_slab = lax.axis_size("slab")
    n_pencil = lax.axis_size("pencil")
    slab_idx = lax.axis_index("slab")
    pencil_idx = lax.axis_index("pencil")
    rows_all = CY * n_pencil
    planes_all = CZ * n_slab
    half_cols = NX // 2 + 1
    n_buckets = bucket_count.shape[0]
    capacity = species.shape[0] // n_buckets
    site_count = 2 * capacity
    slot_ids = jnp.arange(capacity, dtype=jnp.int32)
    in_use = (slot_ids[None, :] < bucket_count[:, None]).reshape(-1).astype(jnp.float32)
    charges = (
        jnp.stack([species_charge(species, ion_table), species_charge(species, wannier_table)])
        * in_use[None, :]
    )

    def network(features):
        return fitting(features, weight_in, bias_in, weight_mid, bias_mid, weight_out, bias_out)

    centroid_shift, pullback = jax.vjp(network, descriptors)
    relative = jnp.stack([fraction, fraction + centroid_shift])
    anchor = jnp.stack([slab_idx * CZ, pencil_idx * CY, jnp.zeros((), jnp.int32)])
    local_base = base_index - anchor[:, None]
    site_charge = (
        charges.reshape(2, n_buckets, capacity).transpose(1, 0, 2).reshape(n_buckets, site_count)
    )
    site_rel = (
        relative.reshape(2, 3, n_buckets, capacity)
        .transpose(2, 1, 0, 3)
        .reshape(n_buckets, 3, site_count)
    )
    site_base = jnp.broadcast_to(
        local_base.reshape(3, n_buckets, 1, capacity), (3, n_buckets, 2, capacity)
    )
    site_base = site_base.transpose(1, 0, 2, 3).reshape(n_buckets, 3, site_count)
    bucket_ids = jnp.arange(n_buckets, dtype=jnp.int32)
    window_shape = (BZ + 8, CY + 8, NX)
    zero_index = jnp.zeros((), jnp.int32)

    def spread_step(grid_now, inputs):
        bucket, charge, rel_pos, base_pos = inputs
        plane_val, plane_slope = dense_window(rel_pos[0], base_pos[0] - bucket * BZ + 1, BZ + 8)
        row_val, row_slope = dense_window(rel_pos[1], base_pos[1] + 1, CY + 8)
        col_val, col_slope = dense_window(rel_pos[2], base_pos[2] - 3, NX)
        outer_prod = ((charge[:, None] * plane_val)[:, :, None] * row_val[:, None, :]).reshape(
            site_count, -1
        )
        block_sum = lax.dot_general(
            outer_prod, col_val, (((0,), (0,)), ((), ())), precision=three_pass
        )
        corner = (bucket * BZ, zero_index, zero_index)
        current = lax.dynamic_slice(grid_now, corner, window_shape)
        grid_now = lax.dynamic_update_slice(
            grid_now, current + block_sum.reshape(window_shape), corner
        )
        return (grid_now, (col_val, col_slope))

    charge_grid, windows = lax.scan(
        spread_step,
        jnp.zeros((CZ + 8, CY + 8, NX), jnp.float32),
        (bucket_ids, site_charge, site_rel, site_base),
    )
    rim_planes = jnp.concatenate([charge_grid[:4], charge_grid[CZ + 4 :]], axis=0)
    arrived = extended(rim_planes, (("slab", 0),), 4)
    inner_grid = charge_grid[4 : CZ + 4].at[:4].add(arrived[:4]).at[CZ - 4 :].add(arrived[12:])
    rim_rows = jnp.concatenate([inner_grid[:, :4], inner_grid[:, CY + 4 :]], axis=1)
    arrived = extended(rim_rows, (("pencil", 1),), 4)
    source_grid = (
        inner_grid[:, 4 : CY + 4].at[:, :4].add(arrived[:, :4]).at[:, CY - 4 :].add(arrived[:, 12:])
    )
    rows_wave = rows_all // n_slab
    column_part = -(-(-(-half_cols // n_pencil)) // 4) * 4
    wave_all = column_part * n_pencil
    x_ids = pencil_idx * column_part + jnp.arange(column_part, dtype=jnp.int32)
    forward_x, inverse_x = x_tables(NX, column_part, n_pencil)
    forward_y = block_table(rows_all, -1.0).reshape(2, n_slab, rows_wave, 2 * rows_all)
    forward_y = forward_y.transpose(1, 0, 2, 3).reshape(2 * rows_all, 2 * rows_all)
    forward_z = block_table(planes_all, -1.0).reshape(2 * planes_all, 2 * planes_all)
    inverse_z = block_table(planes_all, 1.0).reshape(2, n_slab, CZ, 2 * planes_all)
    inverse_z = inverse_z.transpose(1, 0, 2, 3).reshape(2 * planes_all, 2 * planes_all)
    inverse_y = block_table(rows_all, 1.0).reshape(2, n_pencil, CY, 2 * rows_all)
    inverse_y = inverse_y.transpose(1, 0, 2, 3).reshape(2 * rows_all, 2 * rows_all)
    wave_x = lax.dot_general(
        forward_x, source_grid.reshape(CZ * CY, NX), (((1,), (1,)), ((), ())), precision=three_pass
    )
    wave_x = lax.all_to_all(
        wave_x.reshape(n_pencil, 2 * column_part, CZ * CY), "pencil", 0, 0, tiled=True
    )
    wave_x = wave_x.reshape(n_pencil, 2, column_part, CZ, CY).transpose(1, 0, 4, 2, 3)
    wave_y = jnp.dot(forward_y, wave_x.reshape(2 * rows_all, column_part * CZ), precision=three_pass)
    wave_y = lax.all_to_all(
        wave_y.reshape(n_slab, 2 * rows_wave, column_part * CZ), "slab", 0, 0, tiled=True
    )
    wave_y = wave_y.reshape(n_slab, 2, rows_wave, column_part, CZ).transpose(1, 0, 4, 2, 3)
    wave_z = jnp.dot(
        forward_z, wave_y.reshape(2 * planes_all, rows_wave * column_part), precision=three_pass
    ).reshape(2, planes_all, rows_wave, column_part)
    factor = influence(
        jnp.arange(planes_all, dtype=jnp.int32),
        planes_all,
        slab_idx * rows_wave + jnp.arange(rows_wave, dtype=jnp.int32),
        rows_all,
        x_ids,
        NX,
    )
    weighted = wave_z * factor[None]
    power = weighted[0] * wave_z[0] + weighted[1] * wave_z[1]
    x_weight = jnp.where((x_ids == 0) | (2 * x_ids == NX), 1.0, 2.0).astype(jnp.float32)
    x_weight = x_weight * (2 * x_ids <= NX).astype(jnp.float32)
    energy_terms = 0.5 * jnp.sum(power * x_weight)
    energy_sum = lax.psum(lax.psum(energy_terms, "pencil"), "slab")
    back_z = jnp.dot(
        inverse_z, weighted.reshape(2 * planes_all, rows_wave * column_part), precision=three_pass
    )
    back_z = lax.all_to_all(
        back_z.reshape(n_slab, 2 * CZ, rows_wave * column_part), "slab", 0, 0, tiled=True
    )
    back_z = back_z.reshape(n_slab, 2, CZ, rows_wave, column_part).transpose(1, 0, 3, 2, 4)
    back_y = jnp.dot(inverse_y, back_z.reshape(2 * rows_all, CZ * column_part), precision=three_pass)
    back_y = lax.all_to_all(
        back_y.reshape(n_pencil, 2 * CY, CZ * column_part), "pencil", 0, 0, tiled=True
    )
    back_y = back_y.reshape(n_pencil, 2, CY, CZ, column_part).transpose(0, 1, 4, 3, 2)
    potential = lax.dot_general(
        back_y.reshape(2 * wave_all, CZ * CY), inverse_x, (((0,), (0,)), ((), ())), precision=three_pass
    ).reshape(CZ, CY, NX)
    potential = extended(potential, (("slab", 0), ("pencil", 1)), 4)

    flat_ids = jnp.arange((CY + 8) * (BZ + 8), dtype=jnp.int32)
    flat_row = (flat_ids % (CY + 8)).astype(jnp.float32)
    flat_plane = (flat_ids // (CY + 8)).astype(jnp.float32)

    def sample_step(inputs):
        bucket, rel_pos, base_pos, col_val, col_slope = inputs
        corner = (bucket * BZ, zero_index, zero_index)
        patch = lax.dynamic_slice(potential, corner, (BZ + 8, CY + 8, NX)).reshape(-1, NX)
        stacked = jnp.concatenate([col_val, col_slope], axis=0)
        both = lax.dot_general(stacked, patch, (((1,), (1,)), ((), ())), precision=three_pass)
        along = both[:site_count]
        across = both[site_count:]
        plane_first = (base_pos[0] - bucket * BZ + 1).astype(jnp.float32)
        row_first = (base_pos[1] + 1).astype(jnp.float32)
        plane_val, plane_slope = bspline(
            rel_pos[0][:, None] - (flat_plane[None, :] - plane_first[:, None]) + 6.0
        )
        row_val, row_slope = bspline(
            rel_pos[1][:, None] - (flat_row[None, :] - row_first[:, None]) + 6.0
        )
        grad_z = jnp.sum(plane_slope * row_val * along, axis=1)
        grad_y = jnp.sum(plane_val * row_slope * along, axis=1)
        grad_x = jnp.sum(plane_val * row_val * across, axis=1)
        return jnp.stack([grad_z, grad_y, grad_x])

    slopes = lax.map(sample_step, (bucket_ids, site_rel, site_base, windows[0], windows[1]))
    forces = -site_charge[:, None, :] * slopes
    site_forces = forces.reshape(n_buckets, 3, 2, capacity).transpose(2, 1, 0, 3).reshape(2, 3, -1)
    (descriptor_grad,) = pullback(-site_forces[1])
    total_slots = species.shape[0] * n_slab * n_pencil
    energy = energy_sum / float(total_slots)
    return (energy, site_forces, descriptor_grad)


def solution(mesh):
    in_specs = (
        P(("slab", "pencil"), None),
        P(("slab", "pencil")),
        P(("slab", "pencil")),
        P(None, ("slab", "pencil")),
        P(None, ("slab", "pencil")),
        P(),
        P(),
        P(),
        P(),
        P(),
        P(),
    )
    out_specs = (P(), P(None, None, ("slab", "pencil")), P(("slab", "pencil"), None))
    return jax.shard_map(body, mesh=mesh, in_specs=in_specs, out_specs=out_specs, check_vma=False)
```

```python
import math

import jax
import jax.numpy as jnp
from jax import lax
from jax.sharding import PartitionSpec as P

NX = 384
CZ = 16
CY = 48
BZ = 4


ion_table = (6.0, 1.0, 9.0, 7.0)
wannier_table = (-8.0, 0.0, -8.0, -8.0)
spline_coeffs = (1.0 / 120.0, 26.0 / 120.0, 66.0 / 120.0, 26.0 / 120.0, 1.0 / 120.0)
ewald_beta = 1.4
shift_scale = 0.9
three_pass = lax.Precision.HIGH


def extended(cells, sides, width):
    for axis, dim in sides:
        count = lax.axis_size(axis)
        head = lax.slice_in_dim(cells, 0, width, axis=dim)
        tail = lax.slice_in_dim(cells, cells.shape[dim] - width, cells.shape[dim], axis=dim)
        cells = jnp.concatenate(
            [
                lax.ppermute(tail, axis, [(i, (i + 1) % count) for i in range(count)]),
                cells,
                lax.ppermute(head, axis, [((i + 1) % count, i) for i in range(count)]),
            ],
            axis=dim,
        )
    return cells


def bspline(offset):
    folded = jnp.minimum(offset, 6.0 - offset)
    part_one = jnp.maximum(folded, 0.0)
    part_two = jnp.maximum(folded - 1.0, 0.0)
    part_three = jnp.maximum(folded - 2.0, 0.0)
    spline_val = (part_one**5 - 6.0 * part_two**5 + 15.0 * part_three**5) / 120.0
    spline_slope = (part_one**4 - 6.0 * part_two**4 + 15.0 * part_three**4) / 24.0
    return (spline_val, jnp.where(offset <= 3.0, spline_slope, -spline_slope))


def species_charge(species, charge_list):
    kind_ids = jnp.arange(len(charge_list), dtype=jnp.int32)
    levels = jnp.asarray(charge_list, jnp.float32)
    picked = jnp.where(species[None, :] == kind_ids[:, None], levels[:, None], 0.0)
    return jnp.sum(picked, axis=0)


def fitting(descriptors, weight_in, bias_in, weight_mid, bias_mid, weight_out, bias_out):
    hidden = jnp.tanh(
        jnp.dot(descriptors, weight_in, preferred_element_type=jnp.float32) + bias_in
    ).astype(jnp.bfloat16)
    for layer_idx in range(weight_mid.shape[0]):
        pre_act = (
            jnp.dot(hidden, weight_mid[layer_idx], preferred_element_type=jnp.float32)
            + bias_mid[layer_idx]
        )
        hidden = (hidden.astype(jnp.float32) + jnp.tanh(pre_act)).astype(jnp.bfloat16)
    output_raw = lax.dot_general(
        weight_out, hidden, (((1,), (1,)), ((), ())), preferred_element_type=jnp.float32
    )
    return shift_scale * jnp.tanh(output_raw + bias_out[:, None])


def axis_terms(index, length):
    signed = jnp.where(2 * index >= length, index - length, index).astype(jnp.float32) / length
    orders = jnp.arange(1, 6, dtype=jnp.int32)
    phases = (index[:, None] * orders[None, :] % length).astype(jnp.float32) * (
        2.0 * math.pi / length
    )
    coeffs = jnp.asarray(spline_coeffs, jnp.float32)
    real_sum = jnp.sum(coeffs[None, :] * jnp.cos(phases), axis=1)
    imag_sum = jnp.sum(coeffs[None, :] * jnp.sin(phases), axis=1)
    modulus = 1.0 / (real_sum * real_sum + imag_sum * imag_sum)
    damping = jnp.exp(-((math.pi / ewald_beta) ** 2) * signed * signed)
    return (signed * signed, damping * modulus)


def influence(z_index, z_len, y_index, y_len, x_index, x_len):
    z_sq, z_fac = axis_terms(z_index, z_len)
    y_sq, y_fac = axis_terms(y_index, y_len)
    x_sq, x_fac = axis_terms(x_index, x_len)
    squared = z_sq[:, None, None] + y_sq[None, :, None] + x_sq[None, None, :]
    safe_sq = jnp.where(squared > 0.0, squared, 1.0)
    volume = float(z_len * y_len * x_len)
    scaled = (
        z_fac[:, None, None]
        * y_fac[None, :, None]
        * x_fac[None, None, :]
        / (math.pi * volume * safe_sq)
    )
    return jnp.where(squared > 0.0, scaled, 0.0)


def block_table(length, sign):
    index = jnp.arange(length, dtype=jnp.int32)
    angles = (index[:, None] * index[None, :] % length).astype(jnp.float32) * (
        2.0 * math.pi / length
    )
    cosine = jnp.cos(angles)
    sine = jnp.sin(angles) * sign
    return jnp.stack([jnp.stack([cosine, -sine], axis=1), jnp.stack([sine, cosine], axis=1)])


def x_tables(length, part, count, offset, width):
    positions = jnp.arange(length, dtype=jnp.int32)
    local_ids = offset + jnp.arange(width, dtype=jnp.int32)
    wave_ids = (jnp.arange(count, dtype=jnp.int32)[:, None] * part + local_ids[None, :]).reshape(-1)
    angles = (wave_ids[:, None] * positions[None, :] % length).astype(jnp.float32) * (
        2.0 * math.pi / length
    )
    kept_mask = (2 * wave_ids <= length).astype(jnp.float32)
    doubled = (
        jnp.where((wave_ids == 0) | (2 * wave_ids == length), 1.0, 2.0).astype(jnp.float32)
        * kept_mask
    )
    cosine = jnp.cos(angles).reshape(count, 1, width, length)
    sine = jnp.sin(angles).reshape(count, 1, width, length)
    kept = kept_mask.reshape(count, 1, width, 1)
    twice = doubled.reshape(count, 1, width, 1)
    forward = jnp.concatenate([cosine * kept, -sine * kept], axis=1)
    inverse = jnp.concatenate([cosine * twice, -sine * twice], axis=1)
    return (forward.reshape(-1, length), inverse.reshape(-1, length))


def dense_window(relative, start, length):
    cell_ids = jnp.arange(length, dtype=jnp.int32)
    distance = jnp.mod(cell_ids[None, :] - start[:, None], length).astype(jnp.float32)
    return bspline(relative[:, None] - distance + 6.0)


def body(
    descriptors,
    species,
    bucket_count,
    base_index,
    fraction,
    weight_in,
    bias_in,
    weight_mid,
    bias_mid,
    weight_out,
    bias_out,
):
    n_slab = lax.axis_size("slab")
    n_pencil = lax.axis_size("pencil")
    slab_idx = lax.axis_index("slab")
    pencil_idx = lax.axis_index("pencil")
    rows_all = CY * n_pencil
    planes_all = CZ * n_slab
    half_cols = NX // 2 + 1
    n_buckets = bucket_count.shape[0]
    capacity = species.shape[0] // n_buckets
    site_count = 2 * capacity
    slot_ids = jnp.arange(capacity, dtype=jnp.int32)
    in_use = (slot_ids[None, :] < bucket_count[:, None]).reshape(-1).astype(jnp.float32)
    charges = (
        jnp.stack([species_charge(species, ion_table), species_charge(species, wannier_table)])
        * in_use[None, :]
    )

    def network(features):
        return fitting(features, weight_in, bias_in, weight_mid, bias_mid, weight_out, bias_out)

    centroid_shift, pullback = jax.vjp(network, descriptors)
    relative = jnp.stack([fraction, fraction + centroid_shift])
    anchor = jnp.stack([slab_idx * CZ, pencil_idx * CY, jnp.zeros((), jnp.int32)])
    local_base = base_index - anchor[:, None]
    site_charge = (
        charges.reshape(2, n_buckets, capacity).transpose(1, 0, 2).reshape(n_buckets, site_count)
    )
    site_rel = (
        relative.reshape(2, 3, n_buckets, capacity)
        .transpose(2, 1, 0, 3)
        .reshape(n_buckets, 3, site_count)
    )
    site_base = jnp.broadcast_to(
        local_base.reshape(3, n_buckets, 1, capacity), (3, n_buckets, 2, capacity)
    )
    site_base = site_base.transpose(1, 0, 2, 3).reshape(n_buckets, 3, site_count)
    bucket_ids = jnp.arange(n_buckets, dtype=jnp.int32)
    window_shape = (BZ + 8, CY + 8, NX)
    zero_index = jnp.zeros((), jnp.int32)

    def spread_step(grid_now, inputs):
        bucket, charge, rel_pos, base_pos = inputs
        plane_val, plane_slope = dense_window(rel_pos[0], base_pos[0] - bucket * BZ + 1, BZ + 8)
        row_val, row_slope = dense_window(rel_pos[1], base_pos[1] + 1, CY + 8)
        col_val, col_slope = dense_window(rel_pos[2], base_pos[2] - 3, NX)
        outer_prod = ((charge[:, None] * plane_val)[:, :, None] * row_val[:, None, :]).reshape(
            site_count, -1
        )
        block_sum = lax.dot_general(
            outer_prod, col_val, (((0,), (0,)), ((), ())), precision=three_pass
        )
        corner = (bucket * BZ, zero_index, zero_index)
        current = lax.dynamic_slice(grid_now, corner, window_shape)
        grid_now = lax.dynamic_update_slice(
            grid_now, current + block_sum.reshape(window_shape), corner
        )
        return (grid_now, (col_val, col_slope))

    charge_grid, windows = lax.scan(
        spread_step,
        jnp.zeros((CZ + 8, CY + 8, NX), jnp.float32),
        (bucket_ids, site_charge, site_rel, site_base),
    )
    rim_planes = jnp.concatenate([charge_grid[:4], charge_grid[CZ + 4 :]], axis=0)
    arrived = extended(rim_planes, (("slab", 0),), 4)
    inner_grid = charge_grid[4 : CZ + 4].at[:4].add(arrived[:4]).at[CZ - 4 :].add(arrived[12:])
    rim_rows = jnp.concatenate([inner_grid[:, :4], inner_grid[:, CY + 4 :]], axis=1)
    arrived = extended(rim_rows, (("pencil", 1),), 4)
    source_grid = (
        inner_grid[:, 4 : CY + 4].at[:, :4].add(arrived[:, :4]).at[:, CY - 4 :].add(arrived[:, 12:])
    )
    rows_wave = rows_all // n_slab
    column_part = -(-(-(-half_cols // n_pencil)) // 4) * 4
    wave_all = column_part * n_pencil
    forward_y = block_table(rows_all, -1.0).reshape(2, n_slab, rows_wave, 2 * rows_all)
    forward_y = forward_y.transpose(1, 0, 2, 3).reshape(2 * rows_all, 2 * rows_all)
    forward_z = block_table(planes_all, -1.0).reshape(2 * planes_all, 2 * planes_all)
    inverse_z = block_table(planes_all, 1.0).reshape(2, n_slab, CZ, 2 * planes_all)
    inverse_z = inverse_z.transpose(1, 0, 2, 3).reshape(2 * planes_all, 2 * planes_all)
    inverse_y = block_table(rows_all, 1.0).reshape(2, n_pencil, CY, 2 * rows_all)
    inverse_y = inverse_y.transpose(1, 0, 2, 3).reshape(2 * rows_all, 2 * rows_all)
    grid_rows = source_grid.reshape(CZ * CY, NX)

    def dft_chunk(offset, width):
        x_ids = pencil_idx * column_part + offset + jnp.arange(width, dtype=jnp.int32)
        forward_x, inverse_x = x_tables(NX, column_part, n_pencil, offset, width)
        wave_x = lax.dot_general(
            forward_x, grid_rows, (((1,), (1,)), ((), ())), precision=three_pass
        )
        wave_x = lax.all_to_all(
            wave_x.reshape(n_pencil, 2 * width, CZ * CY), "pencil", 0, 0, tiled=True
        )
        wave_x = wave_x.reshape(n_pencil, 2, width, CZ, CY).transpose(1, 0, 4, 2, 3)
        wave_y = jnp.dot(forward_y, wave_x.reshape(2 * rows_all, width * CZ), precision=three_pass)
        wave_y = lax.all_to_all(
            wave_y.reshape(n_slab, 2 * rows_wave, width * CZ), "slab", 0, 0, tiled=True
        )
        wave_y = wave_y.reshape(n_slab, 2, rows_wave, width, CZ).transpose(1, 0, 4, 2, 3)
        wave_z = jnp.dot(
            forward_z, wave_y.reshape(2 * planes_all, rows_wave * width), precision=three_pass
        ).reshape(2, planes_all, rows_wave, width)
        factor = influence(
            jnp.arange(planes_all, dtype=jnp.int32),
            planes_all,
            slab_idx * rows_wave + jnp.arange(rows_wave, dtype=jnp.int32),
            rows_all,
            x_ids,
            NX,
        )
        weighted = wave_z * factor[None]
        power = weighted[0] * wave_z[0] + weighted[1] * wave_z[1]
        x_weight = jnp.where((x_ids == 0) | (2 * x_ids == NX), 1.0, 2.0).astype(jnp.float32)
        x_weight = x_weight * (2 * x_ids <= NX).astype(jnp.float32)
        energy_part = 0.5 * jnp.sum(power * x_weight)
        back_z = jnp.dot(
            inverse_z, weighted.reshape(2 * planes_all, rows_wave * width), precision=three_pass
        )
        back_z = lax.all_to_all(
            back_z.reshape(n_slab, 2 * CZ, rows_wave * width), "slab", 0, 0, tiled=True
        )
        back_z = back_z.reshape(n_slab, 2, CZ, rows_wave, width).transpose(1, 0, 3, 2, 4)
        back_y = jnp.dot(inverse_y, back_z.reshape(2 * rows_all, CZ * width), precision=three_pass)
        back_y = lax.all_to_all(
            back_y.reshape(n_pencil, 2 * CY, CZ * width), "pencil", 0, 0, tiled=True
        )
        back_y = back_y.reshape(n_pencil, 2, CY, CZ, width).transpose(0, 1, 4, 3, 2)
        potential_part = lax.dot_general(
            back_y.reshape(2 * n_pencil * width, CZ * CY),
            inverse_x,
            (((0,), (0,)), ((), ())),
            precision=three_pass,
        )
        return (potential_part, energy_part)

    first_width = -(-column_part // 8) * 4
    potential_a, energy_a = dft_chunk(0, first_width)
    potential_b, energy_b = dft_chunk(first_width, column_part - first_width)
    energy_terms = energy_a + energy_b
    energy_sum = lax.psum(lax.psum(energy_terms, "pencil"), "slab")
    potential = (potential_a + potential_b).reshape(CZ, CY, NX)
    potential = extended(potential, (("slab", 0), ("pencil", 1)), 4)

    flat_ids = jnp.arange((CY + 8) * (BZ + 8), dtype=jnp.int32)
    flat_row = (flat_ids % (CY + 8)).astype(jnp.float32)
    flat_plane = (flat_ids // (CY + 8)).astype(jnp.float32)

    def sample_step(inputs):
        bucket, rel_pos, base_pos, col_val, col_slope = inputs
        corner = (bucket * BZ, zero_index, zero_index)
        patch = lax.dynamic_slice(potential, corner, (BZ + 8, CY + 8, NX)).reshape(-1, NX)
        stacked = jnp.concatenate([col_val, col_slope], axis=0)
        both = lax.dot_general(stacked, patch, (((1,), (1,)), ((), ())), precision=three_pass)
        along = both[:site_count]
        across = both[site_count:]
        plane_first = (base_pos[0] - bucket * BZ + 1).astype(jnp.float32)
        row_first = (base_pos[1] + 1).astype(jnp.float32)
        plane_val, plane_slope = bspline(
            rel_pos[0][:, None] - (flat_plane[None, :] - plane_first[:, None]) + 6.0
        )
        row_val, row_slope = bspline(
            rel_pos[1][:, None] - (flat_row[None, :] - row_first[:, None]) + 6.0
        )
        grad_z = jnp.sum(plane_slope * row_val * along, axis=1)
        grad_y = jnp.sum(plane_val * row_slope * along, axis=1)
        grad_x = jnp.sum(plane_val * row_val * across, axis=1)
        return jnp.stack([grad_z, grad_y, grad_x])

    slopes = lax.map(sample_step, (bucket_ids, site_rel, site_base, windows[0], windows[1]))
    forces = -site_charge[:, None, :] * slopes
    site_forces = forces.reshape(n_buckets, 3, 2, capacity).transpose(2, 1, 0, 3).reshape(2, 3, -1)
    (descriptor_grad,) = pullback(-site_forces[1])
    total_slots = species.shape[0] * n_slab * n_pencil
    energy = energy_sum / float(total_slots)
    return (energy, site_forces, descriptor_grad)


def solution(mesh):
    in_specs = (
        P(("slab", "pencil"), None),
        P(("slab", "pencil")),
        P(("slab", "pencil")),
        P(None, ("slab", "pencil")),
        P(None, ("slab", "pencil")),
        P(),
        P(),
        P(),
        P(),
        P(),
        P(),
    )
    out_specs = (P(), P(None, None, ("slab", "pencil")), P(("slab", "pencil"), None))
    return jax.shard_map(body, mesh=mesh, in_specs=in_specs, out_specs=out_specs, check_vma=False)
```

```python
import math

import jax
import jax.numpy as jnp
from jax import lax
from jax.sharding import PartitionSpec as P

NX = 384
CZ = 16
CY = 48
BZ = 4


ion_table = (6.0, 1.0, 9.0, 7.0)
wannier_table = (-8.0, 0.0, -8.0, -8.0)
spline_coeffs = (1.0 / 120.0, 26.0 / 120.0, 66.0 / 120.0, 26.0 / 120.0, 1.0 / 120.0)
ewald_beta = 1.4
shift_scale = 0.9
three_pass = lax.Precision.HIGH


def extended(cells, sides, width):
    for axis, dim in sides:
        count = lax.axis_size(axis)
        head = lax.slice_in_dim(cells, 0, width, axis=dim)
        tail = lax.slice_in_dim(cells, cells.shape[dim] - width, cells.shape[dim], axis=dim)
        cells = jnp.concatenate(
            [
                lax.ppermute(tail, axis, [(i, (i + 1) % count) for i in range(count)]),
                cells,
                lax.ppermute(head, axis, [((i + 1) % count, i) for i in range(count)]),
            ],
            axis=dim,
        )
    return cells


def bspline(offset):
    folded = jnp.minimum(offset, 6.0 - offset)
    part_one = jnp.maximum(folded, 0.0)
    part_two = jnp.maximum(folded - 1.0, 0.0)
    part_three = jnp.maximum(folded - 2.0, 0.0)
    spline_val = (part_one**5 - 6.0 * part_two**5 + 15.0 * part_three**5) / 120.0
    spline_slope = (part_one**4 - 6.0 * part_two**4 + 15.0 * part_three**4) / 24.0
    return (spline_val, jnp.where(offset <= 3.0, spline_slope, -spline_slope))


def species_charge(species, charge_list):
    kind_ids = jnp.arange(len(charge_list), dtype=jnp.int32)
    levels = jnp.asarray(charge_list, jnp.float32)
    picked = jnp.where(species[None, :] == kind_ids[:, None], levels[:, None], 0.0)
    return jnp.sum(picked, axis=0)


def fitting(descriptors, weight_in, bias_in, weight_mid, bias_mid, weight_out, bias_out):
    hidden = jnp.tanh(
        jnp.dot(descriptors, weight_in, preferred_element_type=jnp.float32) + bias_in
    ).astype(jnp.bfloat16)
    for layer_idx in range(weight_mid.shape[0]):
        pre_act = (
            jnp.dot(hidden, weight_mid[layer_idx], preferred_element_type=jnp.float32)
            + bias_mid[layer_idx]
        )
        hidden = (hidden.astype(jnp.float32) + jnp.tanh(pre_act)).astype(jnp.bfloat16)
    output_raw = lax.dot_general(
        weight_out, hidden, (((1,), (1,)), ((), ())), preferred_element_type=jnp.float32
    )
    return shift_scale * jnp.tanh(output_raw + bias_out[:, None])


def axis_terms(index, length):
    signed = jnp.where(2 * index >= length, index - length, index).astype(jnp.float32) / length
    orders = jnp.arange(1, 6, dtype=jnp.int32)
    phases = (index[:, None] * orders[None, :] % length).astype(jnp.float32) * (
        2.0 * math.pi / length
    )
    coeffs = jnp.asarray(spline_coeffs, jnp.float32)
    real_sum = jnp.sum(coeffs[None, :] * jnp.cos(phases), axis=1)
    imag_sum = jnp.sum(coeffs[None, :] * jnp.sin(phases), axis=1)
    modulus = 1.0 / (real_sum * real_sum + imag_sum * imag_sum)
    damping = jnp.exp(-((math.pi / ewald_beta) ** 2) * signed * signed)
    return (signed * signed, damping * modulus)


def influence(z_index, z_len, y_index, y_len, x_index, x_len):
    z_sq, z_fac = axis_terms(z_index, z_len)
    y_sq, y_fac = axis_terms(y_index, y_len)
    x_sq, x_fac = axis_terms(x_index, x_len)
    squared = z_sq[:, None, None] + y_sq[None, :, None] + x_sq[None, None, :]
    safe_sq = jnp.where(squared > 0.0, squared, 1.0)
    volume = float(z_len * y_len * x_len)
    scaled = (
        z_fac[:, None, None]
        * y_fac[None, :, None]
        * x_fac[None, None, :]
        / (math.pi * volume * safe_sq)
    )
    return jnp.where(squared > 0.0, scaled, 0.0)


def block_table(length, sign):
    index = jnp.arange(length, dtype=jnp.int32)
    angles = (index[:, None] * index[None, :] % length).astype(jnp.float32) * (
        2.0 * math.pi / length
    )
    cosine = jnp.cos(angles)
    sine = jnp.sin(angles) * sign
    return jnp.stack([jnp.stack([cosine, -sine], axis=1), jnp.stack([sine, cosine], axis=1)])


def x_tables(length, part, count):
    positions = jnp.arange(length, dtype=jnp.int32)
    wave_ids = jnp.arange(part * count, dtype=jnp.int32)
    angles = (wave_ids[:, None] * positions[None, :] % length).astype(jnp.float32) * (
        2.0 * math.pi / length
    )
    kept_mask = (2 * wave_ids <= length).astype(jnp.float32)
    doubled = (
        jnp.where((wave_ids == 0) | (2 * wave_ids == length), 1.0, 2.0).astype(jnp.float32)
        * kept_mask
    )
    cosine = jnp.cos(angles).reshape(count, 1, part, length)
    sine = jnp.sin(angles).reshape(count, 1, part, length)
    kept = kept_mask.reshape(count, 1, part, 1)
    twice = doubled.reshape(count, 1, part, 1)
    forward = jnp.concatenate([cosine * kept, -sine * kept], axis=1)
    inverse = jnp.concatenate([cosine * twice, -sine * twice], axis=1)
    return (forward.reshape(-1, length), inverse.reshape(-1, length))


def dense_window(relative, start, length):
    cell_ids = jnp.arange(length, dtype=jnp.int32)
    distance = jnp.mod(cell_ids[None, :] - start[:, None], length).astype(jnp.float32)
    return bspline(relative[:, None] - distance + 6.0)


def body(
    descriptors,
    species,
    bucket_count,
    base_index,
    fraction,
    weight_in,
    bias_in,
    weight_mid,
    bias_mid,
    weight_out,
    bias_out,
):
    n_slab = lax.axis_size("slab")
    n_pencil = lax.axis_size("pencil")
    slab_idx = lax.axis_index("slab")
    pencil_idx = lax.axis_index("pencil")
    rows_all = CY * n_pencil
    planes_all = CZ * n_slab
    half_cols = NX // 2 + 1
    n_buckets = bucket_count.shape[0]
    capacity = species.shape[0] // n_buckets
    site_count = 2 * capacity
    slot_ids = jnp.arange(capacity, dtype=jnp.int32)
    in_use = (slot_ids[None, :] < bucket_count[:, None]).reshape(-1).astype(jnp.float32)
    charges = (
        jnp.stack([species_charge(species, ion_table), species_charge(species, wannier_table)])
        * in_use[None, :]
    )

    def network(features):
        return fitting(features, weight_in, bias_in, weight_mid, bias_mid, weight_out, bias_out)

    centroid_shift, pullback = jax.vjp(network, descriptors)
    relative = jnp.stack([fraction, fraction + centroid_shift])
    anchor = jnp.stack([slab_idx * CZ, pencil_idx * CY, jnp.zeros((), jnp.int32)])
    local_base = base_index - anchor[:, None]
    site_charge = (
        charges.reshape(2, n_buckets, capacity).transpose(1, 0, 2).reshape(n_buckets, site_count)
    )
    site_rel = (
        relative.reshape(2, 3, n_buckets, capacity)
        .transpose(2, 1, 0, 3)
        .reshape(n_buckets, 3, site_count)
    )
    site_base = jnp.broadcast_to(
        local_base.reshape(3, n_buckets, 1, capacity), (3, n_buckets, 2, capacity)
    )
    site_base = site_base.transpose(1, 0, 2, 3).reshape(n_buckets, 3, site_count)
    bucket_ids = jnp.arange(n_buckets, dtype=jnp.int32)
    window_shape = (BZ + 8, CY + 8, NX)
    zero_index = jnp.zeros((), jnp.int32)

    def spread_step(grid_now, inputs):
        bucket, charge, rel_pos, base_pos = inputs
        plane_val, plane_slope = dense_window(rel_pos[0], base_pos[0] - bucket * BZ + 1, BZ + 8)
        row_val, row_slope = dense_window(rel_pos[1], base_pos[1] + 1, CY + 8)
        col_val, col_slope = dense_window(rel_pos[2], base_pos[2] - 3, NX)
        outer_prod = ((charge[:, None] * plane_val)[:, :, None] * row_val[:, None, :]).reshape(
            site_count, -1
        )
        block_sum = lax.dot_general(
            outer_prod, col_val, (((0,), (0,)), ((), ())), precision=three_pass
        )
        corner = (bucket * BZ, zero_index, zero_index)
        current = lax.dynamic_slice(grid_now, corner, window_shape)
        grid_now = lax.dynamic_update_slice(
            grid_now, current + block_sum.reshape(window_shape), corner
        )
        return (grid_now, (col_val, col_slope))

    charge_grid, windows = lax.scan(
        spread_step,
        jnp.zeros((CZ + 8, CY + 8, NX), jnp.float32),
        (bucket_ids, site_charge, site_rel, site_base),
    )
    rim_planes = jnp.concatenate([charge_grid[:4], charge_grid[CZ + 4 :]], axis=0)
    arrived = extended(rim_planes, (("slab", 0),), 4)
    inner_grid = charge_grid[4 : CZ + 4].at[:4].add(arrived[:4]).at[CZ - 4 :].add(arrived[12:])
    rim_rows = jnp.concatenate([inner_grid[:, :4], inner_grid[:, CY + 4 :]], axis=1)
    arrived = extended(rim_rows, (("pencil", 1),), 4)
    source_grid = (
        inner_grid[:, 4 : CY + 4].at[:, :4].add(arrived[:, :4]).at[:, CY - 4 :].add(arrived[:, 12:])
    )
    rows_wave = rows_all // n_slab
    column_part = -(-(-(-half_cols // n_pencil)) // 4) * 4
    wave_all = column_part * n_pencil
    x_ids = pencil_idx * column_part + jnp.arange(column_part, dtype=jnp.int32)
    forward_x, inverse_x = x_tables(NX, column_part, n_pencil)
    forward_y = block_table(rows_all, -1.0).reshape(2, n_slab, rows_wave, 2 * rows_all)
    forward_y = forward_y.transpose(1, 0, 2, 3).reshape(2 * rows_all, 2 * rows_all)
    forward_z = block_table(planes_all, -1.0).reshape(2 * planes_all, 2 * planes_all)
    inverse_z = block_table(planes_all, 1.0).reshape(2, n_slab, CZ, 2 * planes_all)
    inverse_z = inverse_z.transpose(1, 0, 2, 3).reshape(2 * planes_all, 2 * planes_all)
    inverse_y = block_table(rows_all, 1.0).reshape(2, n_pencil, CY, 2 * rows_all)
    inverse_y = inverse_y.transpose(1, 0, 2, 3).reshape(2 * rows_all, 2 * rows_all)
    wave_x = lax.dot_general(
        forward_x, source_grid.reshape(CZ * CY, NX), (((1,), (1,)), ((), ())), precision=three_pass
    )
    wave_x = lax.all_to_all(
        wave_x.reshape(n_pencil, 2 * column_part, CZ * CY), "pencil", 0, 0, tiled=True
    )
    wave_x = wave_x.reshape(n_pencil, 2, column_part, CZ, CY).transpose(1, 0, 4, 2, 3)
    wave_y = jnp.dot(forward_y, wave_x.reshape(2 * rows_all, column_part * CZ), precision=three_pass)
    wave_y = lax.all_to_all(
        wave_y.reshape(n_slab, 2 * rows_wave, column_part * CZ), "slab", 0, 0, tiled=True
    )
    wave_y = wave_y.reshape(n_slab, 2, rows_wave, column_part, CZ).transpose(1, 0, 4, 2, 3)
    wave_z = jnp.dot(
        forward_z, wave_y.reshape(2 * planes_all, rows_wave * column_part), precision=three_pass
    ).reshape(2, planes_all, rows_wave, column_part)
    factor = influence(
        jnp.arange(planes_all, dtype=jnp.int32),
        planes_all,
        slab_idx * rows_wave + jnp.arange(rows_wave, dtype=jnp.int32),
        rows_all,
        x_ids,
        NX,
    )
    weighted = wave_z * factor[None]
    power = weighted[0] * wave_z[0] + weighted[1] * wave_z[1]
    x_weight = jnp.where((x_ids == 0) | (2 * x_ids == NX), 1.0, 2.0).astype(jnp.float32)
    x_weight = x_weight * (2 * x_ids <= NX).astype(jnp.float32)
    energy_terms = 0.5 * jnp.sum(power * x_weight)
    back_z = jnp.dot(
        inverse_z, weighted.reshape(2 * planes_all, rows_wave * column_part), precision=three_pass
    ).reshape(n_slab, 2 * CZ, rows_wave * column_part)
    carried = jnp.broadcast_to(energy_terms, (n_slab, 8, rows_wave * column_part))
    back_z = lax.all_to_all(
        jnp.concatenate([back_z, carried], axis=1), "slab", 0, 0, tiled=True
    )
    slab_energy = jnp.sum(back_z[:, 2 * CZ, 0])
    back_z = back_z[:, : 2 * CZ].reshape(n_slab, 2, CZ, rows_wave, column_part)
    back_z = back_z.transpose(1, 0, 3, 2, 4)
    back_y = jnp.dot(
        inverse_y, back_z.reshape(2 * rows_all, CZ * column_part), precision=three_pass
    ).reshape(n_pencil, 2 * CY, CZ * column_part)
    carried = jnp.broadcast_to(slab_energy, (n_pencil, 8, CZ * column_part))
    back_y = lax.all_to_all(
        jnp.concatenate([back_y, carried], axis=1), "pencil", 0, 0, tiled=True
    )
    energy_sum = jnp.sum(back_y[:, 2 * CY, 0])
    back_y = back_y[:, : 2 * CY].reshape(n_pencil, 2, CY, CZ, column_part)
    back_y = back_y.transpose(0, 1, 4, 3, 2)
    potential = lax.dot_general(
        back_y.reshape(2 * wave_all, CZ * CY), inverse_x, (((0,), (0,)), ((), ())), precision=three_pass
    ).reshape(CZ, CY, NX)
    potential = extended(potential, (("slab", 0), ("pencil", 1)), 4)

    flat_ids = jnp.arange((CY + 8) * (BZ + 8), dtype=jnp.int32)
    flat_row = (flat_ids % (CY + 8)).astype(jnp.float32)
    flat_plane = (flat_ids // (CY + 8)).astype(jnp.float32)

    def sample_step(inputs):
        bucket, rel_pos, base_pos, col_val, col_slope = inputs
        corner = (bucket * BZ, zero_index, zero_index)
        patch = lax.dynamic_slice(potential, corner, (BZ + 8, CY + 8, NX)).reshape(-1, NX)
        stacked = jnp.concatenate([col_val, col_slope], axis=0)
        both = lax.dot_general(stacked, patch, (((1,), (1,)), ((), ())), precision=three_pass)
        along = both[:site_count]
        across = both[site_count:]
        plane_first = (base_pos[0] - bucket * BZ + 1).astype(jnp.float32)
        row_first = (base_pos[1] + 1).astype(jnp.float32)
        plane_val, plane_slope = bspline(
            rel_pos[0][:, None] - (flat_plane[None, :] - plane_first[:, None]) + 6.0
        )
        row_val, row_slope = bspline(
            rel_pos[1][:, None] - (flat_row[None, :] - row_first[:, None]) + 6.0
        )
        grad_z = jnp.sum(plane_slope * row_val * along, axis=1)
        grad_y = jnp.sum(plane_val * row_slope * along, axis=1)
        grad_x = jnp.sum(plane_val * row_val * across, axis=1)
        return jnp.stack([grad_z, grad_y, grad_x])

    slopes = lax.map(sample_step, (bucket_ids, site_rel, site_base, windows[0], windows[1]))
    forces = -site_charge[:, None, :] * slopes
    site_forces = forces.reshape(n_buckets, 3, 2, capacity).transpose(2, 1, 0, 3).reshape(2, 3, -1)
    (descriptor_grad,) = pullback(-site_forces[1])
    total_slots = species.shape[0] * n_slab * n_pencil
    energy = energy_sum / float(total_slots)
    return (energy, site_forces, descriptor_grad)


def solution(mesh):
    in_specs = (
        P(("slab", "pencil"), None),
        P(("slab", "pencil")),
        P(("slab", "pencil")),
        P(None, ("slab", "pencil")),
        P(None, ("slab", "pencil")),
        P(),
        P(),
        P(),
        P(),
        P(),
        P(),
    )
    out_specs = (P(), P(None, None, ("slab", "pencil")), P(("slab", "pencil"), None))
    return jax.shard_map(body, mesh=mesh, in_specs=in_specs, out_specs=out_specs, check_vma=False)
```

```python
import math

import jax
import jax.numpy as jnp
from jax import lax
from jax.sharding import PartitionSpec as P

NX = 384
CZ = 16
CY = 48
BZ = 4


ion_table = (6.0, 1.0, 9.0, 7.0)
wannier_table = (-8.0, 0.0, -8.0, -8.0)
spline_coeffs = (1.0 / 120.0, 26.0 / 120.0, 66.0 / 120.0, 26.0 / 120.0, 1.0 / 120.0)
ewald_beta = 1.4
shift_scale = 0.9
three_pass = lax.Precision.HIGH


def extended(cells, sides, width):
    for axis, dim in sides:
        count = lax.axis_size(axis)
        head = lax.slice_in_dim(cells, 0, width, axis=dim)
        tail = lax.slice_in_dim(cells, cells.shape[dim] - width, cells.shape[dim], axis=dim)
        cells = jnp.concatenate(
            [
                lax.ppermute(tail, axis, [(i, (i + 1) % count) for i in range(count)]),
                cells,
                lax.ppermute(head, axis, [((i + 1) % count, i) for i in range(count)]),
            ],
            axis=dim,
        )
    return cells


def bspline(offset):
    folded = jnp.minimum(offset, 6.0 - offset)
    part_one = jnp.maximum(folded, 0.0)
    part_two = jnp.maximum(folded - 1.0, 0.0)
    part_three = jnp.maximum(folded - 2.0, 0.0)
    spline_val = (part_one**5 - 6.0 * part_two**5 + 15.0 * part_three**5) / 120.0
    spline_slope = (part_one**4 - 6.0 * part_two**4 + 15.0 * part_three**4) / 24.0
    return (spline_val, jnp.where(offset <= 3.0, spline_slope, -spline_slope))


def species_charge(species, charge_list):
    kind_ids = jnp.arange(len(charge_list), dtype=jnp.int32)
    levels = jnp.asarray(charge_list, jnp.float32)
    picked = jnp.where(species[None, :] == kind_ids[:, None], levels[:, None], 0.0)
    return jnp.sum(picked, axis=0)


def fitting(descriptors, weight_in, bias_in, weight_mid, bias_mid, weight_out, bias_out):
    hidden = jnp.tanh(
        jnp.dot(descriptors, weight_in, preferred_element_type=jnp.float32) + bias_in
    ).astype(jnp.bfloat16)
    for layer_idx in range(weight_mid.shape[0]):
        pre_act = (
            jnp.dot(hidden, weight_mid[layer_idx], preferred_element_type=jnp.float32)
            + bias_mid[layer_idx]
        )
        hidden = (hidden.astype(jnp.float32) + jnp.tanh(pre_act)).astype(jnp.bfloat16)
    output_raw = lax.dot_general(
        weight_out, hidden, (((1,), (1,)), ((), ())), preferred_element_type=jnp.float32
    )
    return shift_scale * jnp.tanh(output_raw + bias_out[:, None])


def axis_terms(index, length):
    signed = jnp.where(2 * index >= length, index - length, index).astype(jnp.float32) / length
    orders = jnp.arange(1, 6, dtype=jnp.int32)
    phases = (index[:, None] * orders[None, :] % length).astype(jnp.float32) * (
        2.0 * math.pi / length
    )
    coeffs = jnp.asarray(spline_coeffs, jnp.float32)
    real_sum = jnp.sum(coeffs[None, :] * jnp.cos(phases), axis=1)
    imag_sum = jnp.sum(coeffs[None, :] * jnp.sin(phases), axis=1)
    modulus = 1.0 / (real_sum * real_sum + imag_sum * imag_sum)
    damping = jnp.exp(-((math.pi / ewald_beta) ** 2) * signed * signed)
    return (signed * signed, damping * modulus)


def influence(z_index, z_len, y_index, y_len, x_index, x_len):
    z_sq, z_fac = axis_terms(z_index, z_len)
    y_sq, y_fac = axis_terms(y_index, y_len)
    x_sq, x_fac = axis_terms(x_index, x_len)
    squared = z_sq[:, None, None] + y_sq[None, :, None] + x_sq[None, None, :]
    safe_sq = jnp.where(squared > 0.0, squared, 1.0)
    volume = float(z_len * y_len * x_len)
    scaled = (
        z_fac[:, None, None]
        * y_fac[None, :, None]
        * x_fac[None, None, :]
        / (math.pi * volume * safe_sq)
    )
    return jnp.where(squared > 0.0, scaled, 0.0)


def block_table(length, sign):
    index = jnp.arange(length, dtype=jnp.int32)
    angles = (index[:, None] * index[None, :] % length).astype(jnp.float32) * (
        2.0 * math.pi / length
    )
    cosine = jnp.cos(angles)
    sine = jnp.sin(angles) * sign
    return jnp.stack([jnp.stack([cosine, -sine], axis=1), jnp.stack([sine, cosine], axis=1)])


def x_tables(length, part, count):
    positions = jnp.arange(length, dtype=jnp.int32)
    wave_ids = jnp.arange(part * count, dtype=jnp.int32)
    angles = (wave_ids[:, None] * positions[None, :] % length).astype(jnp.float32) * (
        2.0 * math.pi / length
    )
    kept_mask = (2 * wave_ids <= length).astype(jnp.float32)
    doubled = (
        jnp.where((wave_ids == 0) | (2 * wave_ids == length), 1.0, 2.0).astype(jnp.float32)
        * kept_mask
    )
    cosine = jnp.cos(angles).reshape(count, 1, part, length)
    sine = jnp.sin(angles).reshape(count, 1, part, length)
    kept = kept_mask.reshape(count, 1, part, 1)
    twice = doubled.reshape(count, 1, part, 1)
    forward = jnp.concatenate([cosine * kept, -sine * kept], axis=1)
    inverse = jnp.concatenate([cosine * twice, -sine * twice], axis=1)
    return (forward.reshape(-1, length), inverse.reshape(-1, length))


def dense_window(relative, start, length):
    cell_ids = jnp.arange(length, dtype=jnp.int32)
    distance = jnp.mod(cell_ids[None, :] - start[:, None], length).astype(jnp.float32)
    return bspline(relative[:, None] - distance + 6.0)


def body(
    descriptors,
    species,
    bucket_count,
    base_index,
    fraction,
    weight_in,
    bias_in,
    weight_mid,
    bias_mid,
    weight_out,
    bias_out,
):
    n_slab = lax.axis_size("slab")
    n_pencil = lax.axis_size("pencil")
    slab_idx = lax.axis_index("slab")
    pencil_idx = lax.axis_index("pencil")
    rows_all = CY * n_pencil
    planes_all = CZ * n_slab
    half_cols = NX // 2 + 1
    n_buckets = bucket_count.shape[0]
    capacity = species.shape[0] // n_buckets
    site_count = 2 * capacity
    slot_ids = jnp.arange(capacity, dtype=jnp.int32)
    in_use = (slot_ids[None, :] < bucket_count[:, None]).reshape(-1).astype(jnp.float32)
    charges = (
        jnp.stack([species_charge(species, ion_table), species_charge(species, wannier_table)])
        * in_use[None, :]
    )

    def network(features):
        return fitting(features, weight_in, bias_in, weight_mid, bias_mid, weight_out, bias_out)

    centroid_shift, pullback = jax.vjp(network, descriptors)
    relative = jnp.stack([fraction, fraction + centroid_shift])
    anchor = jnp.stack([slab_idx * CZ, pencil_idx * CY, jnp.zeros((), jnp.int32)])
    local_base = base_index - anchor[:, None]
    site_charge = (
        charges.reshape(2, n_buckets, capacity).transpose(1, 0, 2).reshape(n_buckets, site_count)
    )
    site_rel = (
        relative.reshape(2, 3, n_buckets, capacity)
        .transpose(2, 1, 0, 3)
        .reshape(n_buckets, 3, site_count)
    )
    site_base = jnp.broadcast_to(
        local_base.reshape(3, n_buckets, 1, capacity), (3, n_buckets, 2, capacity)
    )
    site_base = site_base.transpose(1, 0, 2, 3).reshape(n_buckets, 3, site_count)
    bucket_ids = jnp.arange(n_buckets, dtype=jnp.int32)
    window_shape = (BZ + 8, CY + 8, NX)
    zero_index = jnp.zeros((), jnp.int32)

    def spread_step(grid_now, inputs):
        bucket, charge, rel_pos, base_pos = inputs
        plane_val, plane_slope = dense_window(rel_pos[0], base_pos[0] - bucket * BZ + 1, BZ + 8)
        row_val, row_slope = dense_window(rel_pos[1], base_pos[1] + 1, CY + 8)
        col_val, col_slope = dense_window(rel_pos[2], base_pos[2] - 3, NX)
        outer_prod = ((charge[:, None] * plane_val)[:, :, None] * row_val[:, None, :]).reshape(
            site_count, -1
        )
        block_sum = lax.dot_general(
            outer_prod, col_val, (((0,), (0,)), ((), ())), precision=three_pass
        )
        corner = (bucket * BZ, zero_index, zero_index)
        current = lax.dynamic_slice(grid_now, corner, window_shape)
        grid_now = lax.dynamic_update_slice(
            grid_now, current + block_sum.reshape(window_shape), corner
        )
        return (grid_now, (col_val, col_slope))

    charge_grid = jnp.zeros((CZ + 8, CY + 8, NX), jnp.float32)
    col_windows = []
    for bucket in range(n_buckets):
        charge_grid, window = spread_step(
            charge_grid, (bucket, site_charge[bucket], site_rel[bucket], site_base[bucket])
        )
        col_windows.append(window)
    rim_planes = jnp.concatenate([charge_grid[:4], charge_grid[CZ + 4 :]], axis=0)
    arrived = extended(rim_planes, (("slab", 0),), 4)
    inner_grid = charge_grid[4 : CZ + 4].at[:4].add(arrived[:4]).at[CZ - 4 :].add(arrived[12:])
    rim_rows = jnp.concatenate([inner_grid[:, :4], inner_grid[:, CY + 4 :]], axis=1)
    arrived = extended(rim_rows, (("pencil", 1),), 4)
    source_grid = (
        inner_grid[:, 4 : CY + 4].at[:, :4].add(arrived[:, :4]).at[:, CY - 4 :].add(arrived[:, 12:])
    )
    rows_wave = rows_all // n_slab
    column_part = -(-(-(-half_cols // n_pencil)) // 4) * 4
    wave_all = column_part * n_pencil
    x_ids = pencil_idx * column_part + jnp.arange(column_part, dtype=jnp.int32)
    forward_x, inverse_x = x_tables(NX, column_part, n_pencil)
    forward_y = block_table(rows_all, -1.0).reshape(2, n_slab, rows_wave, 2 * rows_all)
    forward_y = forward_y.transpose(1, 0, 2, 3).reshape(2 * rows_all, 2 * rows_all)
    forward_z = block_table(planes_all, -1.0).reshape(2 * planes_all, 2 * planes_all)
    inverse_z = block_table(planes_all, 1.0).reshape(2, n_slab, CZ, 2 * planes_all)
    inverse_z = inverse_z.transpose(1, 0, 2, 3).reshape(2 * planes_all, 2 * planes_all)
    inverse_y = block_table(rows_all, 1.0).reshape(2, n_pencil, CY, 2 * rows_all)
    inverse_y = inverse_y.transpose(1, 0, 2, 3).reshape(2 * rows_all, 2 * rows_all)
    wave_x = lax.dot_general(
        forward_x, source_grid.reshape(CZ * CY, NX), (((1,), (1,)), ((), ())), precision=three_pass
    )
    wave_x = lax.all_to_all(
        wave_x.reshape(n_pencil, 2 * column_part, CZ * CY), "pencil", 0, 0, tiled=True
    )
    wave_x = wave_x.reshape(n_pencil, 2, column_part, CZ, CY).transpose(1, 0, 4, 2, 3)
    wave_y = jnp.dot(forward_y, wave_x.reshape(2 * rows_all, column_part * CZ), precision=three_pass)
    wave_y = lax.all_to_all(
        wave_y.reshape(n_slab, 2 * rows_wave, column_part * CZ), "slab", 0, 0, tiled=True
    )
    wave_y = wave_y.reshape(n_slab, 2, rows_wave, column_part, CZ).transpose(1, 0, 4, 2, 3)
    wave_z = jnp.dot(
        forward_z, wave_y.reshape(2 * planes_all, rows_wave * column_part), precision=three_pass
    ).reshape(2, planes_all, rows_wave, column_part)
    factor = influence(
        jnp.arange(planes_all, dtype=jnp.int32),
        planes_all,
        slab_idx * rows_wave + jnp.arange(rows_wave, dtype=jnp.int32),
        rows_all,
        x_ids,
        NX,
    )
    weighted = wave_z * factor[None]
    power = weighted[0] * wave_z[0] + weighted[1] * wave_z[1]
    x_weight = jnp.where((x_ids == 0) | (2 * x_ids == NX), 1.0, 2.0).astype(jnp.float32)
    x_weight = x_weight * (2 * x_ids <= NX).astype(jnp.float32)
    energy_terms = 0.5 * jnp.sum(power * x_weight)
    back_z = jnp.dot(
        inverse_z, weighted.reshape(2 * planes_all, rows_wave * column_part), precision=three_pass
    ).reshape(n_slab, 2 * CZ, rows_wave * column_part)
    carried = jnp.broadcast_to(energy_terms, (n_slab, 8, rows_wave * column_part))
    back_z = lax.all_to_all(
        jnp.concatenate([back_z, carried], axis=1), "slab", 0, 0, tiled=True
    )
    slab_energy = jnp.sum(back_z[:, 2 * CZ, 0])
    back_z = back_z[:, : 2 * CZ].reshape(n_slab, 2, CZ, rows_wave, column_part)
    back_z = back_z.transpose(1, 0, 3, 2, 4)
    back_y = jnp.dot(
        inverse_y, back_z.reshape(2 * rows_all, CZ * column_part), precision=three_pass
    ).reshape(n_pencil, 2 * CY, CZ * column_part)
    carried = jnp.broadcast_to(slab_energy, (n_pencil, 8, CZ * column_part))
    back_y = lax.all_to_all(
        jnp.concatenate([back_y, carried], axis=1), "pencil", 0, 0, tiled=True
    )
    energy_sum = jnp.sum(back_y[:, 2 * CY, 0])
    back_y = back_y[:, : 2 * CY].reshape(n_pencil, 2, CY, CZ, column_part)
    back_y = back_y.transpose(0, 1, 4, 3, 2)
    potential = lax.dot_general(
        back_y.reshape(2 * wave_all, CZ * CY), inverse_x, (((0,), (0,)), ((), ())), precision=three_pass
    ).reshape(CZ, CY, NX)
    potential = extended(potential, (("slab", 0), ("pencil", 1)), 4)

    flat_ids = jnp.arange((CY + 8) * (BZ + 8), dtype=jnp.int32)
    flat_row = (flat_ids % (CY + 8)).astype(jnp.float32)
    flat_plane = (flat_ids // (CY + 8)).astype(jnp.float32)

    def sample_step(inputs):
        bucket, rel_pos, base_pos, col_val, col_slope = inputs
        corner = (bucket * BZ, zero_index, zero_index)
        patch = lax.dynamic_slice(potential, corner, (BZ + 8, CY + 8, NX)).reshape(-1, NX)
        stacked = jnp.concatenate([col_val, col_slope], axis=0)
        both = lax.dot_general(stacked, patch, (((1,), (1,)), ((), ())), precision=three_pass)
        along = both[:site_count]
        across = both[site_count:]
        plane_first = (base_pos[0] - bucket * BZ + 1).astype(jnp.float32)
        row_first = (base_pos[1] + 1).astype(jnp.float32)
        plane_val, plane_slope = bspline(
            rel_pos[0][:, None] - (flat_plane[None, :] - plane_first[:, None]) + 6.0
        )
        row_val, row_slope = bspline(
            rel_pos[1][:, None] - (flat_row[None, :] - row_first[:, None]) + 6.0
        )
        grad_z = jnp.sum(plane_slope * row_val * along, axis=1)
        grad_y = jnp.sum(plane_val * row_slope * along, axis=1)
        grad_x = jnp.sum(plane_val * row_val * across, axis=1)
        return jnp.stack([grad_z, grad_y, grad_x])

    slopes = jnp.stack(
        [
            sample_step((bucket, site_rel[bucket], site_base[bucket]) + col_windows[bucket])
            for bucket in range(n_buckets)
        ]
    )
    forces = -site_charge[:, None, :] * slopes
    site_forces = forces.reshape(n_buckets, 3, 2, capacity).transpose(2, 1, 0, 3).reshape(2, 3, -1)
    (descriptor_grad,) = pullback(-site_forces[1])
    total_slots = species.shape[0] * n_slab * n_pencil
    energy = energy_sum / float(total_slots)
    return (energy, site_forces, descriptor_grad)


def solution(mesh):
    in_specs = (
        P(("slab", "pencil"), None),
        P(("slab", "pencil")),
        P(("slab", "pencil")),
        P(None, ("slab", "pencil")),
        P(None, ("slab", "pencil")),
        P(),
        P(),
        P(),
        P(),
        P(),
        P(),
    )
    out_specs = (P(), P(None, None, ("slab", "pencil")), P(("slab", "pencil"), None))
    return jax.shard_map(body, mesh=mesh, in_specs=in_specs, out_specs=out_specs, check_vma=False)
```

```python
import math

import jax
import jax.numpy as jnp
from jax import lax
from jax.sharding import PartitionSpec as P

NX = 384
CZ = 16
CY = 48
BZ = 4


ion_table = (6.0, 1.0, 9.0, 7.0)
wannier_table = (-8.0, 0.0, -8.0, -8.0)
spline_coeffs = (1.0 / 120.0, 26.0 / 120.0, 66.0 / 120.0, 26.0 / 120.0, 1.0 / 120.0)
ewald_beta = 1.4
shift_scale = 0.9
three_pass = lax.Precision.HIGH


def extended(cells, sides, width):
    for axis, dim in sides:
        count = lax.axis_size(axis)
        head = lax.slice_in_dim(cells, 0, width, axis=dim)
        tail = lax.slice_in_dim(cells, cells.shape[dim] - width, cells.shape[dim], axis=dim)
        cells = jnp.concatenate(
            [
                lax.ppermute(tail, axis, [(i, (i + 1) % count) for i in range(count)]),
                cells,
                lax.ppermute(head, axis, [((i + 1) % count, i) for i in range(count)]),
            ],
            axis=dim,
        )
    return cells


def bspline(offset):
    folded = jnp.minimum(offset, 6.0 - offset)
    part_one = jnp.maximum(folded, 0.0)
    part_two = jnp.maximum(folded - 1.0, 0.0)
    part_three = jnp.maximum(folded - 2.0, 0.0)
    spline_val = (part_one**5 - 6.0 * part_two**5 + 15.0 * part_three**5) / 120.0
    spline_slope = (part_one**4 - 6.0 * part_two**4 + 15.0 * part_three**4) / 24.0
    return (spline_val, jnp.where(offset <= 3.0, spline_slope, -spline_slope))


def species_charge(species, charge_list):
    kind_ids = jnp.arange(len(charge_list), dtype=jnp.int32)
    levels = jnp.asarray(charge_list, jnp.float32)
    picked = jnp.where(species[None, :] == kind_ids[:, None], levels[:, None], 0.0)
    return jnp.sum(picked, axis=0)


def fitting(descriptors, weight_in, bias_in, weight_mid, bias_mid, weight_out, bias_out):
    hidden = jnp.tanh(
        jnp.dot(descriptors, weight_in, preferred_element_type=jnp.float32) + bias_in
    ).astype(jnp.bfloat16)
    for layer_idx in range(weight_mid.shape[0]):
        pre_act = (
            jnp.dot(hidden, weight_mid[layer_idx], preferred_element_type=jnp.float32)
            + bias_mid[layer_idx]
        )
        hidden = (hidden.astype(jnp.float32) + jnp.tanh(pre_act)).astype(jnp.bfloat16)
    output_raw = lax.dot_general(
        weight_out, hidden, (((1,), (1,)), ((), ())), preferred_element_type=jnp.float32
    )
    return shift_scale * jnp.tanh(output_raw + bias_out[:, None])


def axis_terms(index, length):
    signed = jnp.where(2 * index >= length, index - length, index).astype(jnp.float32) / length
    orders = jnp.arange(1, 6, dtype=jnp.int32)
    phases = (index[:, None] * orders[None, :] % length).astype(jnp.float32) * (
        2.0 * math.pi / length
    )
    coeffs = jnp.asarray(spline_coeffs, jnp.float32)
    real_sum = jnp.sum(coeffs[None, :] * jnp.cos(phases), axis=1)
    imag_sum = jnp.sum(coeffs[None, :] * jnp.sin(phases), axis=1)
    modulus = 1.0 / (real_sum * real_sum + imag_sum * imag_sum)
    damping = jnp.exp(-((math.pi / ewald_beta) ** 2) * signed * signed)
    return (signed * signed, damping * modulus)


def influence(z_index, z_len, y_index, y_len, x_index, x_len):
    z_sq, z_fac = axis_terms(z_index, z_len)
    y_sq, y_fac = axis_terms(y_index, y_len)
    x_sq, x_fac = axis_terms(x_index, x_len)
    squared = z_sq[:, None, None] + y_sq[None, :, None] + x_sq[None, None, :]
    safe_sq = jnp.where(squared > 0.0, squared, 1.0)
    volume = float(z_len * y_len * x_len)
    scaled = (
        z_fac[:, None, None]
        * y_fac[None, :, None]
        * x_fac[None, None, :]
        / (math.pi * volume * safe_sq)
    )
    return jnp.where(squared > 0.0, scaled, 0.0)


def block_table(length, sign):
    index = jnp.arange(length, dtype=jnp.int32)
    angles = (index[:, None] * index[None, :] % length).astype(jnp.float32) * (
        2.0 * math.pi / length
    )
    cosine = jnp.cos(angles)
    sine = jnp.sin(angles) * sign
    return jnp.stack([jnp.stack([cosine, -sine], axis=1), jnp.stack([sine, cosine], axis=1)])


def x_tables(length, part, count):
    positions = jnp.arange(length, dtype=jnp.int32)
    wave_ids = jnp.arange(part * count, dtype=jnp.int32)
    angles = (wave_ids[:, None] * positions[None, :] % length).astype(jnp.float32) * (
        2.0 * math.pi / length
    )
    kept_mask = (2 * wave_ids <= length).astype(jnp.float32)
    doubled = (
        jnp.where((wave_ids == 0) | (2 * wave_ids == length), 1.0, 2.0).astype(jnp.float32)
        * kept_mask
    )
    cosine = jnp.cos(angles).reshape(count, 1, part, length)
    sine = jnp.sin(angles).reshape(count, 1, part, length)
    kept = kept_mask.reshape(count, 1, part, 1)
    twice = doubled.reshape(count, 1, part, 1)
    forward = jnp.concatenate([cosine * kept, -sine * kept], axis=1)
    inverse = jnp.concatenate([cosine * twice, -sine * twice], axis=1)
    return (forward.reshape(-1, length), inverse.reshape(-1, length))


def dense_window(relative, start, length):
    cell_ids = jnp.arange(length, dtype=jnp.int32)
    distance = jnp.mod(cell_ids[None, :] - start[:, None], length).astype(jnp.float32)
    return bspline(relative[:, None] - distance + 6.0)


def body(
    descriptors,
    species,
    bucket_count,
    base_index,
    fraction,
    weight_in,
    bias_in,
    weight_mid,
    bias_mid,
    weight_out,
    bias_out,
):
    n_slab = lax.axis_size("slab")
    n_pencil = lax.axis_size("pencil")
    slab_idx = lax.axis_index("slab")
    pencil_idx = lax.axis_index("pencil")
    rows_all = CY * n_pencil
    planes_all = CZ * n_slab
    half_cols = NX // 2 + 1
    n_buckets = bucket_count.shape[0]
    capacity = species.shape[0] // n_buckets
    site_count = 2 * capacity
    slot_ids = jnp.arange(capacity, dtype=jnp.int32)
    in_use = (slot_ids[None, :] < bucket_count[:, None]).reshape(-1).astype(jnp.float32)
    charges = (
        jnp.stack([species_charge(species, ion_table), species_charge(species, wannier_table)])
        * in_use[None, :]
    )

    def network(features):
        return fitting(features, weight_in, bias_in, weight_mid, bias_mid, weight_out, bias_out)

    centroid_shift, pullback = jax.vjp(network, descriptors)
    relative = jnp.stack([fraction, fraction + centroid_shift])
    anchor = jnp.stack([slab_idx * CZ, pencil_idx * CY, jnp.zeros((), jnp.int32)])
    local_base = base_index - anchor[:, None]
    site_charge = (
        charges.reshape(2, n_buckets, capacity).transpose(1, 0, 2).reshape(n_buckets, site_count)
    )
    site_rel = (
        relative.reshape(2, 3, n_buckets, capacity)
        .transpose(2, 1, 0, 3)
        .reshape(n_buckets, 3, site_count)
    )
    site_base = jnp.broadcast_to(
        local_base.reshape(3, n_buckets, 1, capacity), (3, n_buckets, 2, capacity)
    )
    site_base = site_base.transpose(1, 0, 2, 3).reshape(n_buckets, 3, site_count)
    bucket_ids = jnp.arange(n_buckets, dtype=jnp.int32)
    window_shape = (BZ + 8, CY + 8, NX)
    zero_index = jnp.zeros((), jnp.int32)

    def spread_step(grid_now, inputs):
        bucket, charge, rel_pos, base_pos = inputs
        plane_val, plane_slope = dense_window(rel_pos[0], base_pos[0] - bucket * BZ + 1, BZ + 8)
        row_val, row_slope = dense_window(rel_pos[1], base_pos[1] + 1, CY + 8)
        col_val, col_slope = dense_window(rel_pos[2], base_pos[2] - 3, NX)
        outer_prod = ((charge[:, None] * plane_val)[:, :, None] * row_val[:, None, :]).reshape(
            site_count, -1
        )
        block_sum = lax.dot_general(
            outer_prod, col_val, (((0,), (0,)), ((), ())), precision=three_pass
        )
        corner = (bucket * BZ, zero_index, zero_index)
        current = lax.dynamic_slice(grid_now, corner, window_shape)
        grid_now = lax.dynamic_update_slice(
            grid_now, current + block_sum.reshape(window_shape), corner
        )
        return (grid_now, (col_val, col_slope))

    charge_grid = jnp.zeros((CZ + 8, CY + 8, NX), jnp.float32)
    col_windows = []
    for bucket in range(n_buckets):
        charge_grid, window = spread_step(
            charge_grid, (bucket, site_charge[bucket], site_rel[bucket], site_base[bucket])
        )
        col_windows.append(window)
    rim_planes = jnp.concatenate([charge_grid[:4], charge_grid[CZ + 4 :]], axis=0)
    arrived = extended(rim_planes, (("slab", 0),), 4)
    inner_grid = charge_grid[4 : CZ + 4].at[:4].add(arrived[:4]).at[CZ - 4 :].add(arrived[12:])
    rim_rows = jnp.concatenate([inner_grid[:, :4], inner_grid[:, CY + 4 :]], axis=1)
    arrived = extended(rim_rows, (("pencil", 1),), 4)
    source_grid = (
        inner_grid[:, 4 : CY + 4].at[:, :4].add(arrived[:, :4]).at[:, CY - 4 :].add(arrived[:, 12:])
    )
    rows_wave = rows_all // n_slab
    column_part = -(-(-(-half_cols // n_pencil)) // 4) * 4
    wave_all = column_part * n_pencil
    x_ids = pencil_idx * column_part + jnp.arange(column_part, dtype=jnp.int32)
    forward_x, inverse_x = x_tables(NX, column_part, n_pencil)
    forward_y = block_table(rows_all, -1.0).reshape(2, n_slab, rows_wave, 2 * rows_all)
    forward_y = forward_y.transpose(1, 0, 2, 3).reshape(2 * rows_all, 2 * rows_all)
    forward_z = block_table(planes_all, -1.0).reshape(2 * planes_all, 2 * planes_all)
    inverse_z = block_table(planes_all, 1.0).reshape(2, n_slab, CZ, 2 * planes_all)
    inverse_z = inverse_z.transpose(1, 0, 2, 3).reshape(2 * planes_all, 2 * planes_all)
    inverse_y = block_table(rows_all, 1.0).reshape(2, n_pencil, CY, 2 * rows_all)
    inverse_y = inverse_y.transpose(1, 0, 2, 3).reshape(2 * rows_all, 2 * rows_all)
    wave_x = lax.dot_general(
        forward_x, source_grid.reshape(CZ * CY, NX), (((1,), (1,)), ((), ())), precision=three_pass
    )
    wave_x = lax.all_to_all(
        wave_x.reshape(n_pencil, 2 * column_part, CZ * CY), "pencil", 0, 0, tiled=True
    )
    wave_x = wave_x.reshape(n_pencil, 2, column_part, CZ, CY).transpose(1, 0, 4, 3, 2)
    wave_y = jnp.dot(forward_y, wave_x.reshape(2 * rows_all, column_part * CZ), precision=three_pass)
    wave_y = lax.all_to_all(
        wave_y.reshape(n_slab, 2 * rows_wave, column_part * CZ), "slab", 0, 0, tiled=True
    )
    wave_y = wave_y.reshape(n_slab, 2, rows_wave, CZ, column_part).transpose(1, 0, 3, 2, 4)
    wave_z = jnp.dot(
        forward_z, wave_y.reshape(2 * planes_all, rows_wave * column_part), precision=three_pass
    ).reshape(2, planes_all, rows_wave, column_part)
    factor = influence(
        jnp.arange(planes_all, dtype=jnp.int32),
        planes_all,
        slab_idx * rows_wave + jnp.arange(rows_wave, dtype=jnp.int32),
        rows_all,
        x_ids,
        NX,
    )
    weighted = wave_z * factor[None]
    power = weighted[0] * wave_z[0] + weighted[1] * wave_z[1]
    x_weight = jnp.where((x_ids == 0) | (2 * x_ids == NX), 1.0, 2.0).astype(jnp.float32)
    x_weight = x_weight * (2 * x_ids <= NX).astype(jnp.float32)
    energy_terms = 0.5 * jnp.sum(power * x_weight)
    back_z = jnp.dot(
        inverse_z, weighted.reshape(2 * planes_all, rows_wave * column_part), precision=three_pass
    ).reshape(n_slab, 2 * CZ, rows_wave * column_part)
    carried = jnp.broadcast_to(energy_terms, (n_slab, 8, rows_wave * column_part))
    back_z = lax.all_to_all(
        jnp.concatenate([back_z, carried], axis=1), "slab", 0, 0, tiled=True
    )
    slab_energy = jnp.sum(back_z[:, 2 * CZ, 0])
    back_z = back_z[:, : 2 * CZ].reshape(n_slab, 2, CZ, rows_wave, column_part)
    back_z = back_z.transpose(1, 0, 3, 2, 4)
    back_y = jnp.dot(
        inverse_y, back_z.reshape(2 * rows_all, CZ * column_part), precision=three_pass
    ).reshape(n_pencil, 2 * CY, CZ * column_part)
    carried = jnp.broadcast_to(slab_energy, (n_pencil, 8, CZ * column_part))
    back_y = lax.all_to_all(
        jnp.concatenate([back_y, carried], axis=1), "pencil", 0, 0, tiled=True
    )
    energy_sum = jnp.sum(back_y[:, 2 * CY, 0])
    back_y = back_y[:, : 2 * CY].reshape(n_pencil, 2, CY, CZ, column_part)
    back_y = back_y.transpose(0, 1, 4, 3, 2)
    potential = lax.dot_general(
        back_y.reshape(2 * wave_all, CZ * CY), inverse_x, (((0,), (0,)), ((), ())), precision=three_pass
    ).reshape(CZ, CY, NX)
    potential = extended(potential, (("slab", 0), ("pencil", 1)), 4)

    flat_ids = jnp.arange((CY + 8) * (BZ + 8), dtype=jnp.int32)
    flat_row = (flat_ids % (CY + 8)).astype(jnp.float32)
    flat_plane = (flat_ids // (CY + 8)).astype(jnp.float32)

    def sample_step(inputs):
        bucket, rel_pos, base_pos, col_val, col_slope = inputs
        corner = (bucket * BZ, zero_index, zero_index)
        patch = lax.dynamic_slice(potential, corner, (BZ + 8, CY + 8, NX)).reshape(-1, NX)
        stacked = jnp.concatenate([col_val, col_slope], axis=0)
        both = lax.dot_general(stacked, patch, (((1,), (1,)), ((), ())), precision=three_pass)
        along = both[:site_count]
        across = both[site_count:]
        plane_first = (base_pos[0] - bucket * BZ + 1).astype(jnp.float32)
        row_first = (base_pos[1] + 1).astype(jnp.float32)
        plane_val, plane_slope = bspline(
            rel_pos[0][:, None] - (flat_plane[None, :] - plane_first[:, None]) + 6.0
        )
        row_val, row_slope = bspline(
            rel_pos[1][:, None] - (flat_row[None, :] - row_first[:, None]) + 6.0
        )
        grad_z = jnp.sum(plane_slope * row_val * along, axis=1)
        grad_y = jnp.sum(plane_val * row_slope * along, axis=1)
        grad_x = jnp.sum(plane_val * row_val * across, axis=1)
        return jnp.stack([grad_z, grad_y, grad_x])

    slopes = jnp.stack(
        [
            sample_step((bucket, site_rel[bucket], site_base[bucket]) + col_windows[bucket])
            for bucket in range(n_buckets)
        ]
    )
    forces = -site_charge[:, None, :] * slopes
    site_forces = forces.reshape(n_buckets, 3, 2, capacity).transpose(2, 1, 0, 3).reshape(2, 3, -1)
    (descriptor_grad,) = pullback(-site_forces[1])
    total_slots = species.shape[0] * n_slab * n_pencil
    energy = energy_sum / float(total_slots)
    return (energy, site_forces, descriptor_grad)


def solution(mesh):
    in_specs = (
        P(("slab", "pencil"), None),
        P(("slab", "pencil")),
        P(("slab", "pencil")),
        P(None, ("slab", "pencil")),
        P(None, ("slab", "pencil")),
        P(),
        P(),
        P(),
        P(),
        P(),
        P(),
    )
    out_specs = (P(), P(None, None, ("slab", "pencil")), P(("slab", "pencil"), None))
    return jax.shard_map(body, mesh=mesh, in_specs=in_specs, out_specs=out_specs, check_vma=False)
```

```python
import math

import jax
import jax.numpy as jnp
from jax import lax
from jax.sharding import PartitionSpec as P

NX = 384
CZ = 16
CY = 48
BZ = 4


ion_table = (6.0, 1.0, 9.0, 7.0)
wannier_table = (-8.0, 0.0, -8.0, -8.0)
spline_coeffs = (1.0 / 120.0, 26.0 / 120.0, 66.0 / 120.0, 26.0 / 120.0, 1.0 / 120.0)
ewald_beta = 1.4
shift_scale = 0.9
three_pass = lax.Precision.HIGH


def extended(cells, sides, width):
    for axis, dim in sides:
        count = lax.axis_size(axis)
        head = lax.slice_in_dim(cells, 0, width, axis=dim)
        tail = lax.slice_in_dim(cells, cells.shape[dim] - width, cells.shape[dim], axis=dim)
        cells = jnp.concatenate(
            [
                lax.ppermute(tail, axis, [(i, (i + 1) % count) for i in range(count)]),
                cells,
                lax.ppermute(head, axis, [((i + 1) % count, i) for i in range(count)]),
            ],
            axis=dim,
        )
    return cells


def bspline(offset):
    folded = jnp.minimum(offset, 6.0 - offset)
    part_one = jnp.maximum(folded, 0.0)
    part_two = jnp.maximum(folded - 1.0, 0.0)
    part_three = jnp.maximum(folded - 2.0, 0.0)
    spline_val = (part_one**5 - 6.0 * part_two**5 + 15.0 * part_three**5) / 120.0
    spline_slope = (part_one**4 - 6.0 * part_two**4 + 15.0 * part_three**4) / 24.0
    return (spline_val, jnp.where(offset <= 3.0, spline_slope, -spline_slope))


def species_charge(species, charge_list):
    kind_ids = jnp.arange(len(charge_list), dtype=jnp.int32)
    levels = jnp.asarray(charge_list, jnp.float32)
    picked = jnp.where(species[None, :] == kind_ids[:, None], levels[:, None], 0.0)
    return jnp.sum(picked, axis=0)


def fitting(descriptors, weight_in, bias_in, weight_mid, bias_mid, weight_out, bias_out):
    hidden = jnp.tanh(
        jnp.dot(descriptors, weight_in, preferred_element_type=jnp.float32) + bias_in
    ).astype(jnp.bfloat16)
    for layer_idx in range(weight_mid.shape[0]):
        pre_act = (
            jnp.dot(hidden, weight_mid[layer_idx], preferred_element_type=jnp.float32)
            + bias_mid[layer_idx]
        )
        hidden = (hidden.astype(jnp.float32) + jnp.tanh(pre_act)).astype(jnp.bfloat16)
    output_raw = lax.dot_general(
        weight_out, hidden, (((1,), (1,)), ((), ())), preferred_element_type=jnp.float32
    )
    return shift_scale * jnp.tanh(output_raw + bias_out[:, None])


def axis_terms(index, length):
    signed = jnp.where(2 * index >= length, index - length, index).astype(jnp.float32) / length
    orders = jnp.arange(1, 6, dtype=jnp.int32)
    phases = (index[:, None] * orders[None, :] % length).astype(jnp.float32) * (
        2.0 * math.pi / length
    )
    coeffs = jnp.asarray(spline_coeffs, jnp.float32)
    real_sum = jnp.sum(coeffs[None, :] * jnp.cos(phases), axis=1)
    imag_sum = jnp.sum(coeffs[None, :] * jnp.sin(phases), axis=1)
    modulus = 1.0 / (real_sum * real_sum + imag_sum * imag_sum)
    damping = jnp.exp(-((math.pi / ewald_beta) ** 2) * signed * signed)
    return (signed * signed, damping * modulus)


def influence(z_index, z_len, y_index, y_len, x_index, x_len):
    z_sq, z_fac = axis_terms(z_index, z_len)
    y_sq, y_fac = axis_terms(y_index, y_len)
    x_sq, x_fac = axis_terms(x_index, x_len)
    squared = z_sq[:, None, None] + y_sq[None, :, None] + x_sq[None, None, :]
    safe_sq = jnp.where(squared > 0.0, squared, 1.0)
    volume = float(z_len * y_len * x_len)
    scaled = (
        z_fac[:, None, None]
        * y_fac[None, :, None]
        * x_fac[None, None, :]
        / (math.pi * volume * safe_sq)
    )
    return jnp.where(squared > 0.0, scaled, 0.0)


def block_table(length, sign, out_ids=None):
    index = jnp.arange(length, dtype=jnp.int32)
    out_ids = index if out_ids is None else out_ids
    angles = (out_ids[:, None] * index[None, :] % length).astype(jnp.float32) * (
        2.0 * math.pi / length
    )
    cosine = jnp.cos(angles)
    sine = jnp.sin(angles) * sign
    return jnp.stack([jnp.stack([cosine, -sine], axis=1), jnp.stack([sine, cosine], axis=1)])


def x_tables(length, part, count):
    positions = jnp.arange(length, dtype=jnp.int32)
    wave_ids = jnp.arange(part * count, dtype=jnp.int32)
    angles = (wave_ids[:, None] * positions[None, :] % length).astype(jnp.float32) * (
        2.0 * math.pi / length
    )
    kept_mask = (2 * wave_ids <= length).astype(jnp.float32)
    doubled = (
        jnp.where((wave_ids == 0) | (2 * wave_ids == length), 1.0, 2.0).astype(jnp.float32)
        * kept_mask
    )
    cosine = jnp.cos(angles).reshape(count, 1, part, length)
    sine = jnp.sin(angles).reshape(count, 1, part, length)
    kept = kept_mask.reshape(count, 1, part, 1)
    twice = doubled.reshape(count, 1, part, 1)
    forward = jnp.concatenate([cosine * kept, -sine * kept], axis=1)
    inverse = jnp.concatenate([cosine * twice, -sine * twice], axis=1)
    return (forward.reshape(-1, length), inverse.reshape(-1, length))


def dense_window(relative, start, length):
    cell_ids = jnp.arange(length, dtype=jnp.int32)
    distance = jnp.mod(cell_ids[None, :] - start[:, None], length).astype(jnp.float32)
    return bspline(relative[:, None] - distance + 6.0)


def body(
    descriptors,
    species,
    bucket_count,
    base_index,
    fraction,
    weight_in,
    bias_in,
    weight_mid,
    bias_mid,
    weight_out,
    bias_out,
):
    n_slab = lax.axis_size("slab")
    n_pencil = lax.axis_size("pencil")
    slab_idx = lax.axis_index("slab")
    pencil_idx = lax.axis_index("pencil")
    rows_all = CY * n_pencil
    planes_all = CZ * n_slab
    half_cols = NX // 2 + 1
    n_buckets = bucket_count.shape[0]
    capacity = species.shape[0] // n_buckets
    site_count = 2 * capacity
    slot_ids = jnp.arange(capacity, dtype=jnp.int32)
    in_use = (slot_ids[None, :] < bucket_count[:, None]).reshape(-1).astype(jnp.float32)
    charges = (
        jnp.stack([species_charge(species, ion_table), species_charge(species, wannier_table)])
        * in_use[None, :]
    )

    def network(features):
        return fitting(features, weight_in, bias_in, weight_mid, bias_mid, weight_out, bias_out)

    centroid_shift, pullback = jax.vjp(network, descriptors)
    relative = jnp.stack([fraction, fraction + centroid_shift])
    anchor = jnp.stack([slab_idx * CZ, pencil_idx * CY, jnp.zeros((), jnp.int32)])
    local_base = base_index - anchor[:, None]
    site_charge = (
        charges.reshape(2, n_buckets, capacity).transpose(1, 0, 2).reshape(n_buckets, site_count)
    )
    site_rel = (
        relative.reshape(2, 3, n_buckets, capacity)
        .transpose(2, 1, 0, 3)
        .reshape(n_buckets, 3, site_count)
    )
    site_base = jnp.broadcast_to(
        local_base.reshape(3, n_buckets, 1, capacity), (3, n_buckets, 2, capacity)
    )
    site_base = site_base.transpose(1, 0, 2, 3).reshape(n_buckets, 3, site_count)
    bucket_ids = jnp.arange(n_buckets, dtype=jnp.int32)
    window_shape = (BZ + 8, CY + 8, NX)
    zero_index = jnp.zeros((), jnp.int32)

    def spread_step(grid_now, inputs):
        bucket, charge, rel_pos, base_pos = inputs
        plane_val, plane_slope = dense_window(rel_pos[0], base_pos[0] - bucket * BZ + 1, BZ + 8)
        row_val, row_slope = dense_window(rel_pos[1], base_pos[1] + 1, CY + 8)
        col_val, col_slope = dense_window(rel_pos[2], base_pos[2] - 3, NX)
        outer_prod = ((charge[:, None] * plane_val)[:, :, None] * row_val[:, None, :]).reshape(
            site_count, -1
        )
        block_sum = lax.dot_general(
            outer_prod, col_val, (((0,), (0,)), ((), ())), precision=three_pass
        )
        corner = (bucket * BZ, zero_index, zero_index)
        current = lax.dynamic_slice(grid_now, corner, window_shape)
        grid_now = lax.dynamic_update_slice(
            grid_now, current + block_sum.reshape(window_shape), corner
        )
        return (grid_now, (col_val, col_slope))

    charge_grid = jnp.zeros((CZ + 8, CY + 8, NX), jnp.float32)
    col_windows = []
    for bucket in range(n_buckets):
        charge_grid, window = spread_step(
            charge_grid, (bucket, site_charge[bucket], site_rel[bucket], site_base[bucket])
        )
        col_windows.append(window)
    rim_planes = jnp.concatenate([charge_grid[:4], charge_grid[CZ + 4 :]], axis=0)
    arrived = extended(rim_planes, (("slab", 0),), 4)
    inner_grid = charge_grid[4 : CZ + 4].at[:4].add(arrived[:4]).at[CZ - 4 :].add(arrived[12:])
    rim_rows = jnp.concatenate([inner_grid[:, :4], inner_grid[:, CY + 4 :]], axis=1)
    arrived = extended(rim_rows, (("pencil", 1),), 4)
    source_grid = (
        inner_grid[:, 4 : CY + 4].at[:, :4].add(arrived[:, :4]).at[:, CY - 4 :].add(arrived[:, 12:])
    )
    rows_wave = rows_all // n_slab
    column_part = -(-(-(-half_cols // n_pencil)) // 4) * 4
    wave_all = column_part * n_pencil
    x_ids = pencil_idx * column_part + jnp.arange(column_part, dtype=jnp.int32)
    forward_x, inverse_x = x_tables(NX, column_part, n_pencil)
    forward_y = block_table(rows_all, -1.0).reshape(2, n_slab, rows_wave, 2 * rows_all)
    forward_y = forward_y.transpose(1, 0, 2, 3).reshape(2 * rows_all, 2 * rows_all)
    forward_z = block_table(planes_all, -1.0).reshape(2 * planes_all, 2 * planes_all)
    inverse_z = block_table(planes_all, 1.0).reshape(2, n_slab, CZ, 2 * planes_all)
    inverse_z = inverse_z.transpose(1, 0, 2, 3).reshape(2 * planes_all, 2 * planes_all)
    rows_ext = CY + 8
    row_out = jnp.arange(n_pencil, dtype=jnp.int32)[:, None] * CY - 4
    row_out = jnp.mod(row_out + jnp.arange(rows_ext, dtype=jnp.int32)[None, :], rows_all)
    inverse_y = block_table(rows_all, 1.0, row_out.reshape(-1))
    inverse_y = inverse_y.reshape(2, n_pencil, rows_ext, 2 * rows_all).transpose(1, 0, 2, 3)
    inverse_y = inverse_y.reshape(n_pencil * 2 * rows_ext, 2 * rows_all)
    wave_x = lax.dot_general(
        forward_x, source_grid.reshape(CZ * CY, NX), (((1,), (1,)), ((), ())), precision=three_pass
    )
    wave_x = lax.all_to_all(
        wave_x.reshape(n_pencil, 2 * column_part, CZ * CY), "pencil", 0, 0, tiled=True
    )
    wave_x = wave_x.reshape(n_pencil, 2, column_part, CZ, CY).transpose(1, 0, 4, 3, 2)
    wave_y = jnp.dot(forward_y, wave_x.reshape(2 * rows_all, column_part * CZ), precision=three_pass)
    wave_y = lax.all_to_all(
        wave_y.reshape(n_slab, 2 * rows_wave, column_part * CZ), "slab", 0, 0, tiled=True
    )
    wave_y = wave_y.reshape(n_slab, 2, rows_wave, CZ, column_part).transpose(1, 0, 3, 2, 4)
    wave_z = jnp.dot(
        forward_z, wave_y.reshape(2 * planes_all, rows_wave * column_part), precision=three_pass
    ).reshape(2, planes_all, rows_wave, column_part)
    factor = influence(
        jnp.arange(planes_all, dtype=jnp.int32),
        planes_all,
        slab_idx * rows_wave + jnp.arange(rows_wave, dtype=jnp.int32),
        rows_all,
        x_ids,
        NX,
    )
    weighted = wave_z * factor[None]
    power = weighted[0] * wave_z[0] + weighted[1] * wave_z[1]
    x_weight = jnp.where((x_ids == 0) | (2 * x_ids == NX), 1.0, 2.0).astype(jnp.float32)
    x_weight = x_weight * (2 * x_ids <= NX).astype(jnp.float32)
    energy_terms = 0.5 * jnp.sum(power * x_weight)
    back_z = jnp.dot(
        inverse_z, weighted.reshape(2 * planes_all, rows_wave * column_part), precision=three_pass
    ).reshape(n_slab, 2 * CZ, rows_wave * column_part)
    carried = jnp.broadcast_to(energy_terms, (n_slab, 8, rows_wave * column_part))
    back_z = lax.all_to_all(
        jnp.concatenate([back_z, carried], axis=1), "slab", 0, 0, tiled=True
    )
    slab_energy = jnp.sum(back_z[:, 2 * CZ, 0])
    back_z = back_z[:, : 2 * CZ].reshape(n_slab, 2, CZ, rows_wave, column_part)
    back_z = back_z.transpose(1, 0, 3, 2, 4)
    back_y = jnp.dot(
        inverse_y, back_z.reshape(2 * rows_all, CZ * column_part), precision=three_pass
    ).reshape(n_pencil, 2 * rows_ext, CZ * column_part)
    carried = jnp.broadcast_to(slab_energy, (n_pencil, 8, CZ * column_part))
    back_y = lax.all_to_all(
        jnp.concatenate([back_y, carried], axis=1), "pencil", 0, 0, tiled=True
    )
    energy_sum = jnp.sum(back_y[:, 2 * rows_ext, 0])
    back_y = back_y[:, : 2 * rows_ext].reshape(n_pencil, 2, rows_ext, CZ, column_part)
    back_y = back_y.transpose(0, 1, 4, 3, 2)
    potential = lax.dot_general(
        back_y.reshape(2 * wave_all, CZ * rows_ext),
        inverse_x,
        (((0,), (0,)), ((), ())),
        precision=three_pass,
    ).reshape(CZ, rows_ext, NX)
    potential = extended(potential, (("slab", 0),), 4)

    flat_ids = jnp.arange((CY + 8) * (BZ + 8), dtype=jnp.int32)
    flat_row = (flat_ids % (CY + 8)).astype(jnp.float32)
    flat_plane = (flat_ids // (CY + 8)).astype(jnp.float32)

    def sample_step(inputs):
        bucket, rel_pos, base_pos, col_val, col_slope = inputs
        corner = (bucket * BZ, zero_index, zero_index)
        patch = lax.dynamic_slice(potential, corner, (BZ + 8, CY + 8, NX)).reshape(-1, NX)
        stacked = jnp.concatenate([col_val, col_slope], axis=0)
        both = lax.dot_general(stacked, patch, (((1,), (1,)), ((), ())), precision=three_pass)
        along = both[:site_count]
        across = both[site_count:]
        plane_first = (base_pos[0] - bucket * BZ + 1).astype(jnp.float32)
        row_first = (base_pos[1] + 1).astype(jnp.float32)
        plane_val, plane_slope = bspline(
            rel_pos[0][:, None] - (flat_plane[None, :] - plane_first[:, None]) + 6.0
        )
        row_val, row_slope = bspline(
            rel_pos[1][:, None] - (flat_row[None, :] - row_first[:, None]) + 6.0
        )
        grad_z = jnp.sum(plane_slope * row_val * along, axis=1)
        grad_y = jnp.sum(plane_val * row_slope * along, axis=1)
        grad_x = jnp.sum(plane_val * row_val * across, axis=1)
        return jnp.stack([grad_z, grad_y, grad_x])

    slopes = jnp.stack(
        [
            sample_step((bucket, site_rel[bucket], site_base[bucket]) + col_windows[bucket])
            for bucket in range(n_buckets)
        ]
    )
    forces = -site_charge[:, None, :] * slopes
    site_forces = forces.reshape(n_buckets, 3, 2, capacity).transpose(2, 1, 0, 3).reshape(2, 3, -1)
    (descriptor_grad,) = pullback(-site_forces[1])
    total_slots = species.shape[0] * n_slab * n_pencil
    energy = energy_sum / float(total_slots)
    return (energy, site_forces, descriptor_grad)


def solution(mesh):
    in_specs = (
        P(("slab", "pencil"), None),
        P(("slab", "pencil")),
        P(("slab", "pencil")),
        P(None, ("slab", "pencil")),
        P(None, ("slab", "pencil")),
        P(),
        P(),
        P(),
        P(),
        P(),
        P(),
    )
    out_specs = (P(), P(None, None, ("slab", "pencil")), P(("slab", "pencil"), None))
    return jax.shard_map(body, mesh=mesh, in_specs=in_specs, out_specs=out_specs, check_vma=False)
```

```python
import math

import jax
import jax.numpy as jnp
from jax import lax
from jax.sharding import PartitionSpec as P

NX = 384
CZ = 16
CY = 48
BZ = 4


ion_table = (6.0, 1.0, 9.0, 7.0)
wannier_table = (-8.0, 0.0, -8.0, -8.0)
spline_coeffs = (1.0 / 120.0, 26.0 / 120.0, 66.0 / 120.0, 26.0 / 120.0, 1.0 / 120.0)
ewald_beta = 1.4
shift_scale = 0.9
three_pass = lax.Precision.HIGH


def extended(cells, sides, width):
    for axis, dim in sides:
        count = lax.axis_size(axis)
        head = lax.slice_in_dim(cells, 0, width, axis=dim)
        tail = lax.slice_in_dim(cells, cells.shape[dim] - width, cells.shape[dim], axis=dim)
        cells = jnp.concatenate(
            [
                lax.ppermute(tail, axis, [(i, (i + 1) % count) for i in range(count)]),
                cells,
                lax.ppermute(head, axis, [((i + 1) % count, i) for i in range(count)]),
            ],
            axis=dim,
        )
    return cells


def bspline(offset):
    folded = jnp.minimum(offset, 6.0 - offset)
    part_one = jnp.maximum(folded, 0.0)
    part_two = jnp.maximum(folded - 1.0, 0.0)
    part_three = jnp.maximum(folded - 2.0, 0.0)
    spline_val = (part_one**5 - 6.0 * part_two**5 + 15.0 * part_three**5) / 120.0
    spline_slope = (part_one**4 - 6.0 * part_two**4 + 15.0 * part_three**4) / 24.0
    return (spline_val, jnp.where(offset <= 3.0, spline_slope, -spline_slope))


def species_charge(species, charge_list):
    kind_ids = jnp.arange(len(charge_list), dtype=jnp.int32)
    levels = jnp.asarray(charge_list, jnp.float32)
    picked = jnp.where(species[None, :] == kind_ids[:, None], levels[:, None], 0.0)
    return jnp.sum(picked, axis=0)


def fitting(descriptors, weight_in, bias_in, weight_mid, bias_mid, weight_out, bias_out):
    hidden = jnp.tanh(
        jnp.dot(descriptors, weight_in, preferred_element_type=jnp.float32) + bias_in
    ).astype(jnp.bfloat16)
    for layer_idx in range(weight_mid.shape[0]):
        pre_act = (
            jnp.dot(hidden, weight_mid[layer_idx], preferred_element_type=jnp.float32)
            + bias_mid[layer_idx]
        )
        hidden = (hidden.astype(jnp.float32) + jnp.tanh(pre_act)).astype(jnp.bfloat16)
    output_raw = lax.dot_general(
        weight_out, hidden, (((1,), (1,)), ((), ())), preferred_element_type=jnp.float32
    )
    return shift_scale * jnp.tanh(output_raw + bias_out[:, None])


def axis_terms(index, length):
    signed = jnp.where(2 * index >= length, index - length, index).astype(jnp.float32) / length
    orders = jnp.arange(1, 6, dtype=jnp.int32)
    phases = (index[:, None] * orders[None, :] % length).astype(jnp.float32) * (
        2.0 * math.pi / length
    )
    coeffs = jnp.asarray(spline_coeffs, jnp.float32)
    real_sum = jnp.sum(coeffs[None, :] * jnp.cos(phases), axis=1)
    imag_sum = jnp.sum(coeffs[None, :] * jnp.sin(phases), axis=1)
    modulus = 1.0 / (real_sum * real_sum + imag_sum * imag_sum)
    damping = jnp.exp(-((math.pi / ewald_beta) ** 2) * signed * signed)
    return (signed * signed, damping * modulus)


def influence(z_index, z_len, y_index, y_len, x_index, x_len):
    z_sq, z_fac = axis_terms(z_index, z_len)
    y_sq, y_fac = axis_terms(y_index, y_len)
    x_sq, x_fac = axis_terms(x_index, x_len)
    squared = z_sq[:, None, None] + y_sq[None, :, None] + x_sq[None, None, :]
    safe_sq = jnp.where(squared > 0.0, squared, 1.0)
    volume = float(z_len * y_len * x_len)
    scaled = (
        z_fac[:, None, None]
        * y_fac[None, :, None]
        * x_fac[None, None, :]
        / (math.pi * volume * safe_sq)
    )
    return jnp.where(squared > 0.0, scaled, 0.0)


def block_table(length, sign, out_ids=None, in_ids=None):
    index = jnp.arange(length, dtype=jnp.int32)
    out_ids = index if out_ids is None else out_ids
    in_ids = index if in_ids is None else in_ids
    angles = (out_ids[:, None] * in_ids[None, :] % length).astype(jnp.float32) * (
        2.0 * math.pi / length
    )
    cosine = jnp.cos(angles)
    sine = jnp.sin(angles) * sign
    return jnp.stack([jnp.stack([cosine, -sine], axis=1), jnp.stack([sine, cosine], axis=1)])


def x_tables(length, part, count):
    positions = jnp.arange(length, dtype=jnp.int32)
    wave_ids = jnp.arange(part * count, dtype=jnp.int32)
    angles = (wave_ids[:, None] * positions[None, :] % length).astype(jnp.float32) * (
        2.0 * math.pi / length
    )
    kept_mask = (2 * wave_ids <= length).astype(jnp.float32)
    doubled = (
        jnp.where((wave_ids == 0) | (2 * wave_ids == length), 1.0, 2.0).astype(jnp.float32)
        * kept_mask
    )
    cosine = jnp.cos(angles).reshape(count, 1, part, length)
    sine = jnp.sin(angles).reshape(count, 1, part, length)
    kept = kept_mask.reshape(count, 1, part, 1)
    twice = doubled.reshape(count, 1, part, 1)
    forward = jnp.concatenate([cosine * kept, -sine * kept], axis=1)
    inverse = jnp.concatenate([cosine * twice, -sine * twice], axis=1)
    return (forward.reshape(-1, length), inverse.reshape(-1, length))


def dense_window(relative, start, length):
    cell_ids = jnp.arange(length, dtype=jnp.int32)
    distance = jnp.mod(cell_ids[None, :] - start[:, None], length).astype(jnp.float32)
    return bspline(relative[:, None] - distance + 6.0)


def body(
    descriptors,
    species,
    bucket_count,
    base_index,
    fraction,
    weight_in,
    bias_in,
    weight_mid,
    bias_mid,
    weight_out,
    bias_out,
):
    n_slab = lax.axis_size("slab")
    n_pencil = lax.axis_size("pencil")
    slab_idx = lax.axis_index("slab")
    pencil_idx = lax.axis_index("pencil")
    rows_all = CY * n_pencil
    planes_all = CZ * n_slab
    half_cols = NX // 2 + 1
    n_buckets = bucket_count.shape[0]
    capacity = species.shape[0] // n_buckets
    site_count = 2 * capacity
    slot_ids = jnp.arange(capacity, dtype=jnp.int32)
    in_use = (slot_ids[None, :] < bucket_count[:, None]).reshape(-1).astype(jnp.float32)
    charges = (
        jnp.stack([species_charge(species, ion_table), species_charge(species, wannier_table)])
        * in_use[None, :]
    )

    def network(features):
        return fitting(features, weight_in, bias_in, weight_mid, bias_mid, weight_out, bias_out)

    centroid_shift, pullback = jax.vjp(network, descriptors)
    relative = jnp.stack([fraction, fraction + centroid_shift])
    anchor = jnp.stack([slab_idx * CZ, pencil_idx * CY, jnp.zeros((), jnp.int32)])
    local_base = base_index - anchor[:, None]
    site_charge = (
        charges.reshape(2, n_buckets, capacity).transpose(1, 0, 2).reshape(n_buckets, site_count)
    )
    site_rel = (
        relative.reshape(2, 3, n_buckets, capacity)
        .transpose(2, 1, 0, 3)
        .reshape(n_buckets, 3, site_count)
    )
    site_base = jnp.broadcast_to(
        local_base.reshape(3, n_buckets, 1, capacity), (3, n_buckets, 2, capacity)
    )
    site_base = site_base.transpose(1, 0, 2, 3).reshape(n_buckets, 3, site_count)
    bucket_ids = jnp.arange(n_buckets, dtype=jnp.int32)
    window_shape = (BZ + 8, CY + 8, NX)
    zero_index = jnp.zeros((), jnp.int32)

    def spread_step(grid_now, inputs):
        bucket, charge, rel_pos, base_pos = inputs
        plane_val, plane_slope = dense_window(rel_pos[0], base_pos[0] - bucket * BZ + 1, BZ + 8)
        row_val, row_slope = dense_window(rel_pos[1], base_pos[1] + 1, CY + 8)
        col_val, col_slope = dense_window(rel_pos[2], base_pos[2] - 3, NX)
        outer_prod = ((charge[:, None] * plane_val)[:, :, None] * row_val[:, None, :]).reshape(
            site_count, -1
        )
        block_sum = lax.dot_general(
            outer_prod, col_val, (((0,), (0,)), ((), ())), precision=three_pass
        )
        corner = (bucket * BZ, zero_index, zero_index)
        current = lax.dynamic_slice(grid_now, corner, window_shape)
        grid_now = lax.dynamic_update_slice(
            grid_now, current + block_sum.reshape(window_shape), corner
        )
        return (grid_now, (col_val, col_slope))

    charge_grid = jnp.zeros((CZ + 8, CY + 8, NX), jnp.float32)
    col_windows = []
    for bucket in range(n_buckets):
        charge_grid, window = spread_step(
            charge_grid, (bucket, site_charge[bucket], site_rel[bucket], site_base[bucket])
        )
        col_windows.append(window)
    rim_planes = jnp.concatenate([charge_grid[:4], charge_grid[CZ + 4 :]], axis=0)
    arrived = extended(rim_planes, (("slab", 0),), 4)
    inner_grid = charge_grid[4 : CZ + 4].at[:4].add(arrived[:4]).at[CZ - 4 :].add(arrived[12:])
    source_grid = inner_grid
    rows_wave = rows_all // n_slab
    column_part = -(-(-(-half_cols // n_pencil)) // 4) * 4
    wave_all = column_part * n_pencil
    x_ids = pencil_idx * column_part + jnp.arange(column_part, dtype=jnp.int32)
    forward_x, inverse_x = x_tables(NX, column_part, n_pencil)
    rows_ext = CY + 8
    row_out = jnp.arange(n_pencil, dtype=jnp.int32)[:, None] * CY - 4
    row_out = jnp.mod(row_out + jnp.arange(rows_ext, dtype=jnp.int32)[None, :], rows_all)
    forward_y = block_table(rows_all, -1.0, None, row_out.reshape(-1))
    forward_y = forward_y.reshape(2, n_slab, rows_wave, 2 * n_pencil * rows_ext)
    forward_y = forward_y.transpose(1, 0, 2, 3).reshape(2 * rows_all, 2 * n_pencil * rows_ext)
    forward_z = block_table(planes_all, -1.0).reshape(2 * planes_all, 2 * planes_all)
    inverse_z = block_table(planes_all, 1.0).reshape(2, n_slab, CZ, 2 * planes_all)
    inverse_z = inverse_z.transpose(1, 0, 2, 3).reshape(2 * planes_all, 2 * planes_all)
    inverse_y = block_table(rows_all, 1.0, row_out.reshape(-1))
    inverse_y = inverse_y.reshape(2, n_pencil, rows_ext, 2 * rows_all).transpose(1, 0, 2, 3)
    inverse_y = inverse_y.reshape(n_pencil * 2 * rows_ext, 2 * rows_all)
    wave_x = lax.dot_general(
        forward_x, source_grid.reshape(CZ * rows_ext, NX), (((1,), (1,)), ((), ())), precision=three_pass
    )
    wave_x = lax.all_to_all(
        wave_x.reshape(n_pencil, 2 * column_part, CZ * rows_ext), "pencil", 0, 0, tiled=True
    )
    wave_x = wave_x.reshape(n_pencil, 2, column_part, CZ, rows_ext).transpose(1, 0, 4, 3, 2)
    wave_y = jnp.dot(
        forward_y, wave_x.reshape(2 * n_pencil * rows_ext, column_part * CZ), precision=three_pass
    )
    wave_y = lax.all_to_all(
        wave_y.reshape(n_slab, 2 * rows_wave, column_part * CZ), "slab", 0, 0, tiled=True
    )
    wave_y = wave_y.reshape(n_slab, 2, rows_wave, CZ, column_part).transpose(1, 0, 3, 2, 4)
    wave_z = jnp.dot(
        forward_z, wave_y.reshape(2 * planes_all, rows_wave * column_part), precision=three_pass
    ).reshape(2, planes_all, rows_wave, column_part)
    factor = influence(
        jnp.arange(planes_all, dtype=jnp.int32),
        planes_all,
        slab_idx * rows_wave + jnp.arange(rows_wave, dtype=jnp.int32),
        rows_all,
        x_ids,
        NX,
    )
    weighted = wave_z * factor[None]
    power = weighted[0] * wave_z[0] + weighted[1] * wave_z[1]
    x_weight = jnp.where((x_ids == 0) | (2 * x_ids == NX), 1.0, 2.0).astype(jnp.float32)
    x_weight = x_weight * (2 * x_ids <= NX).astype(jnp.float32)
    energy_terms = 0.5 * jnp.sum(power * x_weight)
    back_z = jnp.dot(
        inverse_z, weighted.reshape(2 * planes_all, rows_wave * column_part), precision=three_pass
    ).reshape(n_slab, 2 * CZ, rows_wave * column_part)
    carried = jnp.broadcast_to(energy_terms, (n_slab, 8, rows_wave * column_part))
    back_z = lax.all_to_all(
        jnp.concatenate([back_z, carried], axis=1), "slab", 0, 0, tiled=True
    )
    slab_energy = jnp.sum(back_z[:, 2 * CZ, 0])
    back_z = back_z[:, : 2 * CZ].reshape(n_slab, 2, CZ, rows_wave, column_part)
    back_z = back_z.transpose(1, 0, 3, 2, 4)
    back_y = jnp.dot(
        inverse_y, back_z.reshape(2 * rows_all, CZ * column_part), precision=three_pass
    ).reshape(n_pencil, 2 * rows_ext, CZ * column_part)
    carried = jnp.broadcast_to(slab_energy, (n_pencil, 8, CZ * column_part))
    back_y = lax.all_to_all(
        jnp.concatenate([back_y, carried], axis=1), "pencil", 0, 0, tiled=True
    )
    energy_sum = jnp.sum(back_y[:, 2 * rows_ext, 0])
    back_y = back_y[:, : 2 * rows_ext].reshape(n_pencil, 2, rows_ext, CZ, column_part)
    back_y = back_y.transpose(0, 1, 4, 3, 2)
    potential = lax.dot_general(
        back_y.reshape(2 * wave_all, CZ * rows_ext),
        inverse_x,
        (((0,), (0,)), ((), ())),
        precision=three_pass,
    ).reshape(CZ, rows_ext, NX)
    potential = extended(potential, (("slab", 0),), 4)

    flat_ids = jnp.arange((CY + 8) * (BZ + 8), dtype=jnp.int32)
    flat_row = (flat_ids % (CY + 8)).astype(jnp.float32)
    flat_plane = (flat_ids // (CY + 8)).astype(jnp.float32)

    def sample_step(inputs):
        bucket, rel_pos, base_pos, col_val, col_slope = inputs
        corner = (bucket * BZ, zero_index, zero_index)
        patch = lax.dynamic_slice(potential, corner, (BZ + 8, CY + 8, NX)).reshape(-1, NX)
        stacked = jnp.concatenate([col_val, col_slope], axis=0)
        both = lax.dot_general(stacked, patch, (((1,), (1,)), ((), ())), precision=three_pass)
        along = both[:site_count]
        across = both[site_count:]
        plane_first = (base_pos[0] - bucket * BZ + 1).astype(jnp.float32)
        row_first = (base_pos[1] + 1).astype(jnp.float32)
        plane_val, plane_slope = bspline(
            rel_pos[0][:, None] - (flat_plane[None, :] - plane_first[:, None]) + 6.0
        )
        row_val, row_slope = bspline(
            rel_pos[1][:, None] - (flat_row[None, :] - row_first[:, None]) + 6.0
        )
        grad_z = jnp.sum(plane_slope * row_val * along, axis=1)
        grad_y = jnp.sum(plane_val * row_slope * along, axis=1)
        grad_x = jnp.sum(plane_val * row_val * across, axis=1)
        return jnp.stack([grad_z, grad_y, grad_x])

    slopes = jnp.stack(
        [
            sample_step((bucket, site_rel[bucket], site_base[bucket]) + col_windows[bucket])
            for bucket in range(n_buckets)
        ]
    )
    forces = -site_charge[:, None, :] * slopes
    site_forces = forces.reshape(n_buckets, 3, 2, capacity).transpose(2, 1, 0, 3).reshape(2, 3, -1)
    (descriptor_grad,) = pullback(-site_forces[1])
    total_slots = species.shape[0] * n_slab * n_pencil
    energy = energy_sum / float(total_slots)
    return (energy, site_forces, descriptor_grad)


def solution(mesh):
    in_specs = (
        P(("slab", "pencil"), None),
        P(("slab", "pencil")),
        P(("slab", "pencil")),
        P(None, ("slab", "pencil")),
        P(None, ("slab", "pencil")),
        P(),
        P(),
        P(),
        P(),
        P(),
        P(),
    )
    out_specs = (P(), P(None, None, ("slab", "pencil")), P(("slab", "pencil"), None))
    return jax.shard_map(body, mesh=mesh, in_specs=in_specs, out_specs=out_specs, check_vma=False)
```

```python
import math

import jax
import jax.numpy as jnp
from jax import lax
from jax.sharding import PartitionSpec as P

NX = 384
CZ = 16
CY = 48
BZ = 4


ion_table = (6.0, 1.0, 9.0, 7.0)
wannier_table = (-8.0, 0.0, -8.0, -8.0)
spline_coeffs = (1.0 / 120.0, 26.0 / 120.0, 66.0 / 120.0, 26.0 / 120.0, 1.0 / 120.0)
ewald_beta = 1.4
shift_scale = 0.9
three_pass = lax.Precision.HIGH


def extended(cells, sides, width):
    for axis, dim in sides:
        count = lax.axis_size(axis)
        head = lax.slice_in_dim(cells, 0, width, axis=dim)
        tail = lax.slice_in_dim(cells, cells.shape[dim] - width, cells.shape[dim], axis=dim)
        cells = jnp.concatenate(
            [
                lax.ppermute(tail, axis, [(i, (i + 1) % count) for i in range(count)]),
                cells,
                lax.ppermute(head, axis, [((i + 1) % count, i) for i in range(count)]),
            ],
            axis=dim,
        )
    return cells


def bspline(offset):
    folded = jnp.minimum(offset, 6.0 - offset)
    part_one = jnp.maximum(folded, 0.0)
    part_two = jnp.maximum(folded - 1.0, 0.0)
    part_three = jnp.maximum(folded - 2.0, 0.0)
    spline_val = (part_one**5 - 6.0 * part_two**5 + 15.0 * part_three**5) / 120.0
    spline_slope = (part_one**4 - 6.0 * part_two**4 + 15.0 * part_three**4) / 24.0
    return (spline_val, jnp.where(offset <= 3.0, spline_slope, -spline_slope))


def species_charge(species, charge_list):
    kind_ids = jnp.arange(len(charge_list), dtype=jnp.int32)
    levels = jnp.asarray(charge_list, jnp.float32)
    picked = jnp.where(species[None, :] == kind_ids[:, None], levels[:, None], 0.0)
    return jnp.sum(picked, axis=0)


def fitting(descriptors, weight_in, bias_in, weight_mid, bias_mid, weight_out, bias_out):
    hidden = jnp.tanh(
        jnp.dot(descriptors, weight_in, preferred_element_type=jnp.float32) + bias_in
    ).astype(jnp.bfloat16)
    for layer_idx in range(weight_mid.shape[0]):
        pre_act = (
            jnp.dot(hidden, weight_mid[layer_idx], preferred_element_type=jnp.float32)
            + bias_mid[layer_idx]
        )
        hidden = (hidden.astype(jnp.float32) + jnp.tanh(pre_act)).astype(jnp.bfloat16)
    output_raw = lax.dot_general(
        weight_out, hidden, (((1,), (1,)), ((), ())), preferred_element_type=jnp.float32
    )
    return shift_scale * jnp.tanh(output_raw + bias_out[:, None])


def axis_terms(index, length):
    signed = jnp.where(2 * index >= length, index - length, index).astype(jnp.float32) / length
    orders = jnp.arange(1, 6, dtype=jnp.int32)
    phases = (index[:, None] * orders[None, :] % length).astype(jnp.float32) * (
        2.0 * math.pi / length
    )
    coeffs = jnp.asarray(spline_coeffs, jnp.float32)
    real_sum = jnp.sum(coeffs[None, :] * jnp.cos(phases), axis=1)
    imag_sum = jnp.sum(coeffs[None, :] * jnp.sin(phases), axis=1)
    modulus = 1.0 / (real_sum * real_sum + imag_sum * imag_sum)
    damping = jnp.exp(-((math.pi / ewald_beta) ** 2) * signed * signed)
    return (signed * signed, damping * modulus)


def influence(z_index, z_len, y_index, y_len, x_index, x_len):
    z_sq, z_fac = axis_terms(z_index, z_len)
    y_sq, y_fac = axis_terms(y_index, y_len)
    x_sq, x_fac = axis_terms(x_index, x_len)
    squared = z_sq[:, None, None] + y_sq[None, :, None] + x_sq[None, None, :]
    safe_sq = jnp.where(squared > 0.0, squared, 1.0)
    volume = float(z_len * y_len * x_len)
    scaled = (
        z_fac[:, None, None]
        * y_fac[None, :, None]
        * x_fac[None, None, :]
        / (math.pi * volume * safe_sq)
    )
    return jnp.where(squared > 0.0, scaled, 0.0)


def block_table(length, sign, out_ids=None):
    index = jnp.arange(length, dtype=jnp.int32)
    out_ids = index if out_ids is None else out_ids
    angles = (out_ids[:, None] * index[None, :] % length).astype(jnp.float32) * (
        2.0 * math.pi / length
    )
    cosine = jnp.cos(angles)
    sine = jnp.sin(angles) * sign
    return jnp.stack([jnp.stack([cosine, -sine], axis=1), jnp.stack([sine, cosine], axis=1)])


def x_tables(length, part, count):
    positions = jnp.arange(length, dtype=jnp.int32)
    wave_ids = jnp.arange(part * count, dtype=jnp.int32)
    angles = (wave_ids[:, None] * positions[None, :] % length).astype(jnp.float32) * (
        2.0 * math.pi / length
    )
    kept_mask = (2 * wave_ids <= length).astype(jnp.float32)
    doubled = (
        jnp.where((wave_ids == 0) | (2 * wave_ids == length), 1.0, 2.0).astype(jnp.float32)
        * kept_mask
    )
    cosine = jnp.cos(angles).reshape(count, 1, part, length)
    sine = jnp.sin(angles).reshape(count, 1, part, length)
    kept = kept_mask.reshape(count, 1, part, 1)
    twice = doubled.reshape(count, 1, part, 1)
    forward = jnp.concatenate([cosine * kept, -sine * kept], axis=1)
    inverse = jnp.concatenate([cosine * twice, -sine * twice], axis=1)
    return (forward.reshape(-1, length), inverse.reshape(-1, length))


def dense_window(relative, start, length):
    cell_ids = jnp.arange(length, dtype=jnp.int32)
    distance = jnp.mod(cell_ids[None, :] - start[:, None], length).astype(jnp.float32)
    return bspline(relative[:, None] - distance + 6.0)


def body(
    descriptors,
    species,
    bucket_count,
    base_index,
    fraction,
    weight_in,
    bias_in,
    weight_mid,
    bias_mid,
    weight_out,
    bias_out,
):
    n_slab = lax.axis_size("slab")
    n_pencil = lax.axis_size("pencil")
    slab_idx = lax.axis_index("slab")
    pencil_idx = lax.axis_index("pencil")
    rows_all = CY * n_pencil
    planes_all = CZ * n_slab
    half_cols = NX // 2 + 1
    n_buckets = bucket_count.shape[0]
    capacity = species.shape[0] // n_buckets
    site_count = 2 * capacity
    slot_ids = jnp.arange(capacity, dtype=jnp.int32)
    in_use = (slot_ids[None, :] < bucket_count[:, None]).reshape(-1).astype(jnp.float32)
    charges = (
        jnp.stack([species_charge(species, ion_table), species_charge(species, wannier_table)])
        * in_use[None, :]
    )

    def network(features):
        return fitting(features, weight_in, bias_in, weight_mid, bias_mid, weight_out, bias_out)

    centroid_shift, pullback = jax.vjp(network, descriptors)
    relative = jnp.stack([fraction, fraction + centroid_shift])
    anchor = jnp.stack([slab_idx * CZ, pencil_idx * CY, jnp.zeros((), jnp.int32)])
    local_base = base_index - anchor[:, None]
    site_charge = (
        charges.reshape(2, n_buckets, capacity).transpose(1, 0, 2).reshape(n_buckets, site_count)
    )
    site_rel = (
        relative.reshape(2, 3, n_buckets, capacity)
        .transpose(2, 1, 0, 3)
        .reshape(n_buckets, 3, site_count)
    )
    site_base = jnp.broadcast_to(
        local_base.reshape(3, n_buckets, 1, capacity), (3, n_buckets, 2, capacity)
    )
    site_base = site_base.transpose(1, 0, 2, 3).reshape(n_buckets, 3, site_count)
    bucket_ids = jnp.arange(n_buckets, dtype=jnp.int32)
    window_shape = (BZ + 8, CY + 8, NX)
    zero_index = jnp.zeros((), jnp.int32)

    def spread_step(grid_now, inputs):
        bucket, charge, rel_pos, base_pos = inputs
        plane_val, plane_slope = dense_window(rel_pos[0], base_pos[0] - bucket * BZ + 1, BZ + 8)
        row_val, row_slope = dense_window(rel_pos[1], base_pos[1] + 1, CY + 8)
        col_val, col_slope = dense_window(rel_pos[2], base_pos[2] - 3, NX)
        outer_prod = ((charge[:, None] * plane_val)[:, :, None] * row_val[:, None, :]).reshape(
            site_count, -1
        )
        block_sum = lax.dot_general(
            outer_prod, col_val, (((0,), (0,)), ((), ())), precision=three_pass
        )
        corner = (bucket * BZ, zero_index, zero_index)
        current = lax.dynamic_slice(grid_now, corner, window_shape)
        grid_now = lax.dynamic_update_slice(
            grid_now, current + block_sum.reshape(window_shape), corner
        )
        return (grid_now, (col_val, col_slope))

    charge_grid = jnp.zeros((CZ + 8, CY + 8, NX), jnp.float32)
    col_windows = []
    for bucket in range(n_buckets):
        charge_grid, window = spread_step(
            charge_grid, (bucket, site_charge[bucket], site_rel[bucket], site_base[bucket])
        )
        col_windows.append(window)
    rim_planes = jnp.concatenate([charge_grid[:4], charge_grid[CZ + 4 :]], axis=0)
    arrived = extended(rim_planes, (("slab", 0),), 4)
    inner_grid = charge_grid[4 : CZ + 4].at[:4].add(arrived[:4]).at[CZ - 4 :].add(arrived[12:])
    rim_rows = jnp.concatenate([inner_grid[:, :4], inner_grid[:, CY + 4 :]], axis=1)
    arrived = extended(rim_rows, (("pencil", 1),), 4)
    source_grid = (
        inner_grid[:, 4 : CY + 4].at[:, :4].add(arrived[:, :4]).at[:, CY - 4 :].add(arrived[:, 12:])
    )
    rows_wave = rows_all // n_slab
    column_part = -(-(-(-half_cols // n_pencil)) // 4) * 4
    wave_all = column_part * n_pencil
    x_ids = pencil_idx * column_part + jnp.arange(column_part, dtype=jnp.int32)
    forward_x, inverse_x = x_tables(NX, column_part, n_pencil)
    forward_y = block_table(rows_all, -1.0).reshape(2, n_slab, rows_wave, 2 * rows_all)
    forward_y = forward_y.transpose(1, 0, 2, 3).reshape(2 * rows_all, 2 * rows_all)
    forward_z = block_table(planes_all, -1.0).reshape(2 * planes_all, 2 * planes_all)
    inverse_z = block_table(planes_all, 1.0).reshape(2, n_slab, CZ, 2 * planes_all)
    inverse_z = inverse_z.transpose(1, 0, 2, 3).reshape(2 * planes_all, 2 * planes_all)
    rows_ext = CY + 8
    row_out = jnp.arange(n_pencil, dtype=jnp.int32)[:, None] * CY - 4
    row_out = jnp.mod(row_out + jnp.arange(rows_ext, dtype=jnp.int32)[None, :], rows_all)
    inverse_y = block_table(rows_all, 1.0, row_out.reshape(-1))
    inverse_y = inverse_y.reshape(2, n_pencil, rows_ext, 2 * rows_all).transpose(1, 0, 2, 3)
    inverse_y = inverse_y.reshape(n_pencil * 2 * rows_ext, 2 * rows_all)
    wave_x = lax.dot_general(
        forward_x, source_grid.reshape(CZ * CY, NX), (((1,), (1,)), ((), ())), precision=three_pass
    )
    wave_x = lax.all_to_all(
        wave_x.reshape(n_pencil, 2 * column_part, CZ * CY), "pencil", 0, 0, tiled=True
    )
    wave_x = wave_x.reshape(n_pencil, 2, column_part, CZ, CY).transpose(1, 0, 4, 3, 2)
    wave_y = jnp.dot(forward_y, wave_x.reshape(2 * rows_all, column_part * CZ), precision=three_pass)
    wave_y = lax.all_to_all(
        wave_y.reshape(n_slab, 2 * rows_wave, column_part * CZ), "slab", 0, 0, tiled=True
    )
    wave_y = wave_y.reshape(n_slab, 2, rows_wave, CZ, column_part).transpose(1, 0, 3, 2, 4)
    wave_z = jnp.dot(
        forward_z, wave_y.reshape(2 * planes_all, rows_wave * column_part), precision=three_pass
    ).reshape(2, planes_all, rows_wave, column_part)
    factor = influence(
        jnp.arange(planes_all, dtype=jnp.int32),
        planes_all,
        slab_idx * rows_wave + jnp.arange(rows_wave, dtype=jnp.int32),
        rows_all,
        x_ids,
        NX,
    )
    weighted = wave_z * factor[None]
    power = weighted[0] * wave_z[0] + weighted[1] * wave_z[1]
    x_weight = jnp.where((x_ids == 0) | (2 * x_ids == NX), 1.0, 2.0).astype(jnp.float32)
    x_weight = x_weight * (2 * x_ids <= NX).astype(jnp.float32)
    energy_terms = 0.5 * jnp.sum(power * x_weight)
    back_z = jnp.dot(
        inverse_z, weighted.reshape(2 * planes_all, rows_wave * column_part), precision=three_pass
    ).reshape(n_slab, 2 * CZ, rows_wave * column_part)
    carried = jnp.broadcast_to(energy_terms, (n_slab, 8, rows_wave * column_part))
    back_z = lax.all_to_all(
        jnp.concatenate([back_z, carried], axis=1), "slab", 0, 0, tiled=True
    )
    slab_energy = jnp.sum(back_z[:, 2 * CZ, 0])
    back_z = back_z[:, : 2 * CZ].reshape(n_slab, 2, CZ, rows_wave, column_part)
    back_z = back_z.transpose(1, 0, 3, 2, 4)
    back_y = jnp.dot(
        inverse_y, back_z.reshape(2 * rows_all, CZ * column_part), precision=three_pass
    ).reshape(n_pencil, 2 * rows_ext, CZ * column_part)
    carried = jnp.broadcast_to(slab_energy, (n_pencil, 8, CZ * column_part))
    back_y = lax.all_to_all(
        jnp.concatenate([back_y, carried], axis=1), "pencil", 0, 0, tiled=True
    )
    energy_sum = jnp.sum(back_y[:, 2 * rows_ext, 0])
    back_y = back_y[:, : 2 * rows_ext].reshape(n_pencil, 2, rows_ext, CZ, column_part)
    back_y = back_y.transpose(0, 1, 4, 3, 2)
    potential = lax.dot_general(
        back_y.reshape(2 * wave_all, CZ * rows_ext),
        inverse_x,
        (((0,), (0,)), ((), ())),
        precision=three_pass,
    ).reshape(CZ, rows_ext, NX)
    potential = extended(potential, (("slab", 0),), 4)

    flat_ids = jnp.arange((CY + 8) * (BZ + 8), dtype=jnp.int32)
    flat_row = (flat_ids % (CY + 8)).astype(jnp.float32)
    flat_plane = (flat_ids // (CY + 8)).astype(jnp.float32)

    def sample_step(inputs):
        bucket, rel_pos, base_pos, col_val, col_slope = inputs
        corner = (bucket * BZ, zero_index, zero_index)
        patch = lax.dynamic_slice(potential, corner, (BZ + 8, CY + 8, NX)).reshape(-1, NX)
        plane_first = (base_pos[0] - bucket * BZ + 1).astype(jnp.float32)
        row_first = (base_pos[1] + 1).astype(jnp.float32)
        plane_val, plane_slope = bspline(
            rel_pos[0][:, None] - (flat_plane[None, :] - plane_first[:, None]) + 6.0
        )
        row_val, row_slope = bspline(
            rel_pos[1][:, None] - (flat_row[None, :] - row_first[:, None]) + 6.0
        )
        weights = jnp.concatenate(
            [plane_slope * row_val, plane_val * row_slope, plane_val * row_val], axis=0
        )
        folded = jnp.dot(weights, patch, precision=three_pass)
        grad_z = jnp.sum(folded[:site_count] * col_val, axis=1)
        grad_y = jnp.sum(folded[site_count : 2 * site_count] * col_val, axis=1)
        grad_x = jnp.sum(folded[2 * site_count :] * col_slope, axis=1)
        return jnp.stack([grad_z, grad_y, grad_x])

    slopes = jnp.stack(
        [
            sample_step((bucket, site_rel[bucket], site_base[bucket]) + col_windows[bucket])
            for bucket in range(n_buckets)
        ]
    )
    forces = -site_charge[:, None, :] * slopes
    site_forces = forces.reshape(n_buckets, 3, 2, capacity).transpose(2, 1, 0, 3).reshape(2, 3, -1)
    (descriptor_grad,) = pullback(-site_forces[1])
    total_slots = species.shape[0] * n_slab * n_pencil
    energy = energy_sum / float(total_slots)
    return (energy, site_forces, descriptor_grad)


def solution(mesh):
    in_specs = (
        P(("slab", "pencil"), None),
        P(("slab", "pencil")),
        P(("slab", "pencil")),
        P(None, ("slab", "pencil")),
        P(None, ("slab", "pencil")),
        P(),
        P(),
        P(),
        P(),
        P(),
        P(),
    )
    out_specs = (P(), P(None, None, ("slab", "pencil")), P(("slab", "pencil"), None))
    return jax.shard_map(body, mesh=mesh, in_specs=in_specs, out_specs=out_specs, check_vma=False)
```

```python
import math

import jax
import jax.numpy as jnp
from jax import lax
from jax.sharding import PartitionSpec as P

NX = 384
CZ = 16
CY = 48
BZ = 4


ion_table = (6.0, 1.0, 9.0, 7.0)
wannier_table = (-8.0, 0.0, -8.0, -8.0)
spline_coeffs = (1.0 / 120.0, 26.0 / 120.0, 66.0 / 120.0, 26.0 / 120.0, 1.0 / 120.0)
ewald_beta = 1.4
shift_scale = 0.9
three_pass = lax.Precision.HIGH


def extended(cells, sides, width):
    for axis, dim in sides:
        count = lax.axis_size(axis)
        head = lax.slice_in_dim(cells, 0, width, axis=dim)
        tail = lax.slice_in_dim(cells, cells.shape[dim] - width, cells.shape[dim], axis=dim)
        cells = jnp.concatenate(
            [
                lax.ppermute(tail, axis, [(i, (i + 1) % count) for i in range(count)]),
                cells,
                lax.ppermute(head, axis, [((i + 1) % count, i) for i in range(count)]),
            ],
            axis=dim,
        )
    return cells


def bspline(offset):
    folded = jnp.minimum(offset, 6.0 - offset)
    part_one = jnp.maximum(folded, 0.0)
    part_two = jnp.maximum(folded - 1.0, 0.0)
    part_three = jnp.maximum(folded - 2.0, 0.0)
    spline_val = (part_one**5 - 6.0 * part_two**5 + 15.0 * part_three**5) / 120.0
    spline_slope = (part_one**4 - 6.0 * part_two**4 + 15.0 * part_three**4) / 24.0
    return (spline_val, jnp.where(offset <= 3.0, spline_slope, -spline_slope))


def species_charge(species, charge_list):
    kind_ids = jnp.arange(len(charge_list), dtype=jnp.int32)
    levels = jnp.asarray(charge_list, jnp.float32)
    picked = jnp.where(species[None, :] == kind_ids[:, None], levels[:, None], 0.0)
    return jnp.sum(picked, axis=0)


def fitting(descriptors, weight_in, bias_in, weight_mid, bias_mid, weight_out, bias_out):
    hidden = jnp.tanh(
        jnp.dot(descriptors, weight_in, preferred_element_type=jnp.float32) + bias_in
    ).astype(jnp.bfloat16)
    for layer_idx in range(weight_mid.shape[0]):
        pre_act = (
            jnp.dot(hidden, weight_mid[layer_idx], preferred_element_type=jnp.float32)
            + bias_mid[layer_idx]
        )
        hidden = (hidden.astype(jnp.float32) + jnp.tanh(pre_act)).astype(jnp.bfloat16)
    output_raw = lax.dot_general(
        weight_out, hidden, (((1,), (1,)), ((), ())), preferred_element_type=jnp.float32
    )
    return shift_scale * jnp.tanh(output_raw + bias_out[:, None])


def axis_terms(index, length):
    signed = jnp.where(2 * index >= length, index - length, index).astype(jnp.float32) / length
    orders = jnp.arange(1, 6, dtype=jnp.int32)
    phases = (index[:, None] * orders[None, :] % length).astype(jnp.float32) * (
        2.0 * math.pi / length
    )
    coeffs = jnp.asarray(spline_coeffs, jnp.float32)
    real_sum = jnp.sum(coeffs[None, :] * jnp.cos(phases), axis=1)
    imag_sum = jnp.sum(coeffs[None, :] * jnp.sin(phases), axis=1)
    modulus = 1.0 / (real_sum * real_sum + imag_sum * imag_sum)
    damping = jnp.exp(-((math.pi / ewald_beta) ** 2) * signed * signed)
    return (signed * signed, damping * modulus)


def influence(z_index, z_len, y_index, y_len, x_index, x_len):
    z_sq, z_fac = axis_terms(z_index, z_len)
    y_sq, y_fac = axis_terms(y_index, y_len)
    x_sq, x_fac = axis_terms(x_index, x_len)
    squared = z_sq[:, None, None] + y_sq[None, :, None] + x_sq[None, None, :]
    safe_sq = jnp.where(squared > 0.0, squared, 1.0)
    volume = float(z_len * y_len * x_len)
    scaled = (
        z_fac[:, None, None]
        * y_fac[None, :, None]
        * x_fac[None, None, :]
        / (math.pi * volume * safe_sq)
    )
    return jnp.where(squared > 0.0, scaled, 0.0)


def block_table(length, sign, out_ids=None):
    index = jnp.arange(length, dtype=jnp.int32)
    out_ids = index if out_ids is None else out_ids
    angles = (out_ids[:, None] * index[None, :] % length).astype(jnp.float32) * (
        2.0 * math.pi / length
    )
    cosine = jnp.cos(angles)
    sine = jnp.sin(angles) * sign
    return jnp.stack([jnp.stack([cosine, -sine], axis=1), jnp.stack([sine, cosine], axis=1)])


def x_tables(length, part, count):
    positions = jnp.arange(length, dtype=jnp.int32)
    wave_ids = jnp.arange(part * count, dtype=jnp.int32)
    angles = (wave_ids[:, None] * positions[None, :] % length).astype(jnp.float32) * (
        2.0 * math.pi / length
    )
    kept_mask = (2 * wave_ids <= length).astype(jnp.float32)
    doubled = (
        jnp.where((wave_ids == 0) | (2 * wave_ids == length), 1.0, 2.0).astype(jnp.float32)
        * kept_mask
    )
    cosine = jnp.cos(angles).reshape(count, 1, part, length)
    sine = jnp.sin(angles).reshape(count, 1, part, length)
    kept = kept_mask.reshape(count, 1, part, 1)
    twice = doubled.reshape(count, 1, part, 1)
    forward = jnp.concatenate([cosine * kept, -sine * kept], axis=1)
    inverse = jnp.concatenate([cosine * twice, -sine * twice], axis=1)
    return (forward.reshape(-1, length), inverse.reshape(-1, length))


def dense_window(relative, start, length):
    cell_ids = jnp.arange(length, dtype=jnp.int32)
    distance = jnp.mod(cell_ids[None, :] - start[:, None], length).astype(jnp.float32)
    return bspline(relative[:, None] - distance + 6.0)


def body(
    descriptors,
    species,
    bucket_count,
    base_index,
    fraction,
    weight_in,
    bias_in,
    weight_mid,
    bias_mid,
    weight_out,
    bias_out,
):
    n_slab = lax.axis_size("slab")
    n_pencil = lax.axis_size("pencil")
    slab_idx = lax.axis_index("slab")
    pencil_idx = lax.axis_index("pencil")
    rows_all = CY * n_pencil
    planes_all = CZ * n_slab
    half_cols = NX // 2 + 1
    n_buckets = bucket_count.shape[0]
    capacity = species.shape[0] // n_buckets
    site_count = 2 * capacity
    slot_ids = jnp.arange(capacity, dtype=jnp.int32)
    in_use = (slot_ids[None, :] < bucket_count[:, None]).reshape(-1).astype(jnp.float32)
    charges = (
        jnp.stack([species_charge(species, ion_table), species_charge(species, wannier_table)])
        * in_use[None, :]
    )

    def network(features):
        return fitting(features, weight_in, bias_in, weight_mid, bias_mid, weight_out, bias_out)

    centroid_shift, pullback = jax.vjp(network, descriptors)
    relative = jnp.stack([fraction, fraction + centroid_shift])
    anchor = jnp.stack([slab_idx * CZ, pencil_idx * CY, jnp.zeros((), jnp.int32)])
    local_base = base_index - anchor[:, None]
    site_charge = (
        charges.reshape(2, n_buckets, capacity).transpose(1, 0, 2).reshape(n_buckets, site_count)
    )
    site_rel = (
        relative.reshape(2, 3, n_buckets, capacity)
        .transpose(2, 1, 0, 3)
        .reshape(n_buckets, 3, site_count)
    )
    site_base = jnp.broadcast_to(
        local_base.reshape(3, n_buckets, 1, capacity), (3, n_buckets, 2, capacity)
    )
    site_base = site_base.transpose(1, 0, 2, 3).reshape(n_buckets, 3, site_count)
    bucket_ids = jnp.arange(n_buckets, dtype=jnp.int32)
    window_shape = (BZ + 8, CY + 8, NX)
    zero_index = jnp.zeros((), jnp.int32)

    def spread_step(grid_now, inputs):
        bucket, charge, rel_pos, base_pos = inputs
        plane_val, plane_slope = dense_window(rel_pos[0], base_pos[0] - bucket * BZ + 1, BZ + 8)
        row_val, row_slope = dense_window(rel_pos[1], base_pos[1] + 1, CY + 8)
        col_val, col_slope = dense_window(rel_pos[2], base_pos[2] - 3, NX)
        outer_prod = ((charge[:, None] * plane_val)[:, :, None] * row_val[:, None, :]).reshape(
            site_count, -1
        )
        block_sum = lax.dot_general(
            outer_prod, col_val, (((0,), (0,)), ((), ())), precision=three_pass
        )
        corner = (bucket * BZ, zero_index, zero_index)
        current = lax.dynamic_slice(grid_now, corner, window_shape)
        grid_now = lax.dynamic_update_slice(
            grid_now, current + block_sum.reshape(window_shape), corner
        )
        return (grid_now, (col_val, col_slope))

    charge_grid = jnp.zeros((CZ + 8, CY + 8, NX), jnp.float32)
    col_windows = []
    for bucket in range(n_buckets):
        charge_grid, window = spread_step(
            charge_grid, (bucket, site_charge[bucket], site_rel[bucket], site_base[bucket])
        )
        col_windows.append(window)
    rim_planes = jnp.concatenate([charge_grid[:4], charge_grid[CZ + 4 :]], axis=0)
    arrived = extended(rim_planes, (("slab", 0),), 4)
    inner_grid = charge_grid[4 : CZ + 4].at[:4].add(arrived[:4]).at[CZ - 4 :].add(arrived[12:])
    rim_rows = jnp.concatenate([inner_grid[:, :4], inner_grid[:, CY + 4 :]], axis=1)
    arrived = extended(rim_rows, (("pencil", 1),), 4)
    source_grid = (
        inner_grid[:, 4 : CY + 4].at[:, :4].add(arrived[:, :4]).at[:, CY - 4 :].add(arrived[:, 12:])
    )
    rows_wave = rows_all // n_slab
    column_part = -(-(-(-half_cols // n_pencil)) // 4) * 4
    wave_all = column_part * n_pencil
    x_ids = pencil_idx * column_part + jnp.arange(column_part, dtype=jnp.int32)
    forward_x, inverse_x = x_tables(NX, column_part, n_pencil)
    forward_y = block_table(rows_all, -1.0).reshape(2, n_slab, rows_wave, 2 * rows_all)
    forward_y = forward_y.transpose(1, 0, 2, 3).reshape(2 * rows_all, 2 * rows_all)
    forward_z = block_table(planes_all, -1.0).reshape(2 * planes_all, 2 * planes_all)
    inverse_z = block_table(planes_all, 1.0).reshape(2, n_slab, CZ, 2 * planes_all)
    inverse_z = inverse_z.transpose(1, 0, 2, 3).reshape(2 * planes_all, 2 * planes_all)
    rows_ext = CY + 8
    row_out = jnp.arange(n_pencil, dtype=jnp.int32)[:, None] * CY - 4
    row_out = jnp.mod(row_out + jnp.arange(rows_ext, dtype=jnp.int32)[None, :], rows_all)
    inverse_y = block_table(rows_all, 1.0, row_out.reshape(-1))
    inverse_y = inverse_y.reshape(2, n_pencil, rows_ext, 2 * rows_all).transpose(1, 0, 2, 3)
    inverse_y = inverse_y.reshape(n_pencil * 2 * rows_ext, 2 * rows_all)
    wave_x = lax.dot_general(
        forward_x, source_grid.reshape(CZ * CY, NX), (((1,), (1,)), ((), ())), precision=three_pass
    )
    wave_x = lax.all_to_all(
        wave_x.reshape(n_pencil, 2 * column_part, CZ * CY), "pencil", 0, 0, tiled=True
    )
    wave_x = wave_x.reshape(n_pencil, 2, column_part, CZ, CY).transpose(1, 0, 4, 3, 2)
    wave_y = jnp.dot(forward_y, wave_x.reshape(2 * rows_all, column_part * CZ), precision=three_pass)
    wave_y = lax.all_to_all(
        wave_y.reshape(n_slab, 2 * rows_wave, column_part * CZ), "slab", 0, 0, tiled=True
    )
    wave_y = wave_y.reshape(n_slab, 2, rows_wave, CZ, column_part).transpose(1, 0, 3, 2, 4)
    wave_z = jnp.dot(
        forward_z, wave_y.reshape(2 * planes_all, rows_wave * column_part), precision=three_pass
    ).reshape(2, planes_all, rows_wave, column_part)
    factor = influence(
        jnp.arange(planes_all, dtype=jnp.int32),
        planes_all,
        slab_idx * rows_wave + jnp.arange(rows_wave, dtype=jnp.int32),
        rows_all,
        x_ids,
        NX,
    )
    weighted = wave_z * factor[None]
    power = weighted[0] * wave_z[0] + weighted[1] * wave_z[1]
    x_weight = jnp.where((x_ids == 0) | (2 * x_ids == NX), 1.0, 2.0).astype(jnp.float32)
    x_weight = x_weight * (2 * x_ids <= NX).astype(jnp.float32)
    energy_terms = 0.5 * jnp.sum(power * x_weight)
    back_z = jnp.dot(
        inverse_z, weighted.reshape(2 * planes_all, rows_wave * column_part), precision=three_pass
    ).reshape(n_slab, 2 * CZ, rows_wave * column_part)
    carried = jnp.broadcast_to(energy_terms, (n_slab, 8, rows_wave * column_part))
    back_z = lax.all_to_all(
        jnp.concatenate([back_z, carried], axis=1), "slab", 0, 0, tiled=True
    )
    slab_energy = jnp.sum(back_z[:, 2 * CZ, 0])
    back_z = back_z[:, : 2 * CZ].reshape(n_slab, 2, CZ, rows_wave, column_part)
    back_z = back_z.transpose(1, 0, 3, 2, 4)
    back_y = jnp.dot(
        inverse_y, back_z.reshape(2 * rows_all, CZ * column_part), precision=three_pass
    ).reshape(n_pencil, 2 * rows_ext, CZ * column_part)
    carried = jnp.broadcast_to(slab_energy, (n_pencil, 8, CZ * column_part))
    back_y = lax.all_to_all(
        jnp.concatenate([back_y, carried], axis=1), "pencil", 0, 0, tiled=True
    )
    energy_sum = jnp.sum(back_y[:, 2 * rows_ext, 0])
    back_y = back_y[:, : 2 * rows_ext].reshape(n_pencil, 2, rows_ext, CZ, column_part)
    back_y = back_y.transpose(0, 1, 4, 3, 2)
    potential = lax.dot_general(
        back_y.reshape(2 * wave_all, CZ * rows_ext),
        inverse_x,
        (((0,), (0,)), ((), ())),
        precision=three_pass,
    ).reshape(CZ, rows_ext, NX)
    potential = extended(potential, (("slab", 0),), 4)

    flat_ids = jnp.arange((CY + 8) * (BZ + 8), dtype=jnp.int32)
    flat_row = (flat_ids % (CY + 8)).astype(jnp.float32)
    flat_plane = (flat_ids // (CY + 8)).astype(jnp.float32)

    def sample_step(inputs):
        bucket, rel_pos, base_pos, col_val, col_slope = inputs
        corner = (bucket * BZ, zero_index, zero_index)
        patch = lax.dynamic_slice(potential, corner, (BZ + 8, CY + 8, NX)).reshape(-1, NX)
        plane_first = (base_pos[0] - bucket * BZ + 1).astype(jnp.float32)
        row_first = (base_pos[1] + 1).astype(jnp.float32)
        plane_val, plane_slope = bspline(
            rel_pos[0][:, None] - (flat_plane[None, :] - plane_first[:, None]) + 6.0
        )
        row_val, row_slope = bspline(
            rel_pos[1][:, None] - (flat_row[None, :] - row_first[:, None]) + 6.0
        )
        fold_z = jnp.dot(plane_slope * row_val, patch, precision=three_pass)
        fold_y = jnp.dot(plane_val * row_slope, patch, precision=three_pass)
        fold_x = jnp.dot(plane_val * row_val, patch, precision=three_pass)
        grad_z = jnp.sum(fold_z * col_val, axis=1)
        grad_y = jnp.sum(fold_y * col_val, axis=1)
        grad_x = jnp.sum(fold_x * col_slope, axis=1)
        return jnp.stack([grad_z, grad_y, grad_x])

    slopes = jnp.stack(
        [
            sample_step((bucket, site_rel[bucket], site_base[bucket]) + col_windows[bucket])
            for bucket in range(n_buckets)
        ]
    )
    forces = -site_charge[:, None, :] * slopes
    site_forces = forces.reshape(n_buckets, 3, 2, capacity).transpose(2, 1, 0, 3).reshape(2, 3, -1)
    (descriptor_grad,) = pullback(-site_forces[1])
    total_slots = species.shape[0] * n_slab * n_pencil
    energy = energy_sum / float(total_slots)
    return (energy, site_forces, descriptor_grad)


def solution(mesh):
    in_specs = (
        P(("slab", "pencil"), None),
        P(("slab", "pencil")),
        P(("slab", "pencil")),
        P(None, ("slab", "pencil")),
        P(None, ("slab", "pencil")),
        P(),
        P(),
        P(),
        P(),
        P(),
        P(),
    )
    out_specs = (P(), P(None, None, ("slab", "pencil")), P(("slab", "pencil"), None))
    return jax.shard_map(body, mesh=mesh, in_specs=in_specs, out_specs=out_specs, check_vma=False)
```

```python
import math

import jax
import jax.numpy as jnp
from jax import lax
from jax.sharding import PartitionSpec as P

NX = 384
CZ = 16
CY = 48
BZ = 4


ion_table = (6.0, 1.0, 9.0, 7.0)
wannier_table = (-8.0, 0.0, -8.0, -8.0)
spline_coeffs = (1.0 / 120.0, 26.0 / 120.0, 66.0 / 120.0, 26.0 / 120.0, 1.0 / 120.0)
ewald_beta = 1.4
shift_scale = 0.9
three_pass = lax.Precision.HIGH


def extended(cells, sides, width):
    for axis, dim in sides:
        count = lax.axis_size(axis)
        head = lax.slice_in_dim(cells, 0, width, axis=dim)
        tail = lax.slice_in_dim(cells, cells.shape[dim] - width, cells.shape[dim], axis=dim)
        cells = jnp.concatenate(
            [
                lax.ppermute(tail, axis, [(i, (i + 1) % count) for i in range(count)]),
                cells,
                lax.ppermute(head, axis, [((i + 1) % count, i) for i in range(count)]),
            ],
            axis=dim,
        )
    return cells


def bspline(offset):
    folded = jnp.minimum(offset, 6.0 - offset)
    part_one = jnp.maximum(folded, 0.0)
    part_two = jnp.maximum(folded - 1.0, 0.0)
    part_three = jnp.maximum(folded - 2.0, 0.0)
    spline_val = (part_one**5 - 6.0 * part_two**5 + 15.0 * part_three**5) / 120.0
    spline_slope = (part_one**4 - 6.0 * part_two**4 + 15.0 * part_three**4) / 24.0
    return (spline_val, jnp.where(offset <= 3.0, spline_slope, -spline_slope))


def species_charge(species, charge_list):
    kind_ids = jnp.arange(len(charge_list), dtype=jnp.int32)
    levels = jnp.asarray(charge_list, jnp.float32)
    picked = jnp.where(species[None, :] == kind_ids[:, None], levels[:, None], 0.0)
    return jnp.sum(picked, axis=0)


def fitting(descriptors, weight_in, bias_in, weight_mid, bias_mid, weight_out, bias_out):
    hidden = jnp.tanh(
        jnp.dot(descriptors, weight_in, preferred_element_type=jnp.float32) + bias_in
    ).astype(jnp.bfloat16)
    for layer_idx in range(weight_mid.shape[0]):
        pre_act = (
            jnp.dot(hidden, weight_mid[layer_idx], preferred_element_type=jnp.float32)
            + bias_mid[layer_idx]
        )
        hidden = (hidden.astype(jnp.float32) + jnp.tanh(pre_act)).astype(jnp.bfloat16)
    output_raw = lax.dot_general(
        weight_out, hidden, (((1,), (1,)), ((), ())), preferred_element_type=jnp.float32
    )
    return shift_scale * jnp.tanh(output_raw + bias_out[:, None])


def axis_terms(index, length):
    signed = jnp.where(2 * index >= length, index - length, index).astype(jnp.float32) / length
    orders = jnp.arange(1, 6, dtype=jnp.int32)
    phases = (index[:, None] * orders[None, :] % length).astype(jnp.float32) * (
        2.0 * math.pi / length
    )
    coeffs = jnp.asarray(spline_coeffs, jnp.float32)
    real_sum = jnp.sum(coeffs[None, :] * jnp.cos(phases), axis=1)
    imag_sum = jnp.sum(coeffs[None, :] * jnp.sin(phases), axis=1)
    modulus = 1.0 / (real_sum * real_sum + imag_sum * imag_sum)
    damping = jnp.exp(-((math.pi / ewald_beta) ** 2) * signed * signed)
    return (signed * signed, damping * modulus)


def influence(z_index, z_len, y_index, y_len, x_index, x_len):
    z_sq, z_fac = axis_terms(z_index, z_len)
    y_sq, y_fac = axis_terms(y_index, y_len)
    x_sq, x_fac = axis_terms(x_index, x_len)
    squared = z_sq[:, None, None] + y_sq[None, :, None] + x_sq[None, None, :]
    safe_sq = jnp.where(squared > 0.0, squared, 1.0)
    volume = float(z_len * y_len * x_len)
    scaled = (
        z_fac[:, None, None]
        * y_fac[None, :, None]
        * x_fac[None, None, :]
        / (math.pi * volume * safe_sq)
    )
    return jnp.where(squared > 0.0, scaled, 0.0)


def block_table(length, sign, out_ids=None):
    index = jnp.arange(length, dtype=jnp.int32)
    out_ids = index if out_ids is None else out_ids
    angles = (out_ids[:, None] * index[None, :] % length).astype(jnp.float32) * (
        2.0 * math.pi / length
    )
    cosine = jnp.cos(angles)
    sine = jnp.sin(angles) * sign
    return jnp.stack([jnp.stack([cosine, -sine], axis=1), jnp.stack([sine, cosine], axis=1)])


def x_tables(length, part, count):
    positions = jnp.arange(length, dtype=jnp.int32)
    wave_ids = jnp.arange(part * count, dtype=jnp.int32)
    angles = (wave_ids[:, None] * positions[None, :] % length).astype(jnp.float32) * (
        2.0 * math.pi / length
    )
    kept_mask = (2 * wave_ids <= length).astype(jnp.float32)
    doubled = (
        jnp.where((wave_ids == 0) | (2 * wave_ids == length), 1.0, 2.0).astype(jnp.float32)
        * kept_mask
    )
    cosine = jnp.cos(angles).reshape(count, 1, part, length)
    sine = jnp.sin(angles).reshape(count, 1, part, length)
    kept = kept_mask.reshape(count, 1, part, 1)
    twice = doubled.reshape(count, 1, part, 1)
    forward = jnp.concatenate([cosine * kept, -sine * kept], axis=1)
    inverse = jnp.concatenate([cosine * twice, -sine * twice], axis=1)
    return (forward.reshape(-1, length), inverse.reshape(-1, length))


def dense_window(relative, start, length):
    cell_ids = jnp.arange(length, dtype=jnp.int32)
    distance = jnp.mod(cell_ids[None, :] - start[:, None], length).astype(jnp.float32)
    return bspline(relative[:, None] - distance + 6.0)


def body(
    descriptors,
    species,
    bucket_count,
    base_index,
    fraction,
    weight_in,
    bias_in,
    weight_mid,
    bias_mid,
    weight_out,
    bias_out,
):
    n_slab = lax.axis_size("slab")
    n_pencil = lax.axis_size("pencil")
    slab_idx = lax.axis_index("slab")
    pencil_idx = lax.axis_index("pencil")
    rows_all = CY * n_pencil
    planes_all = CZ * n_slab
    half_cols = NX // 2 + 1
    n_buckets = bucket_count.shape[0]
    capacity = species.shape[0] // n_buckets
    site_count = 2 * capacity
    slot_ids = jnp.arange(capacity, dtype=jnp.int32)
    in_use = (slot_ids[None, :] < bucket_count[:, None]).reshape(-1).astype(jnp.float32)
    charges = (
        jnp.stack([species_charge(species, ion_table), species_charge(species, wannier_table)])
        * in_use[None, :]
    )

    def network(features):
        return fitting(features, weight_in, bias_in, weight_mid, bias_mid, weight_out, bias_out)

    centroid_shift, pullback = jax.vjp(network, descriptors)
    relative = jnp.stack([fraction, fraction + centroid_shift])
    anchor = jnp.stack([slab_idx * CZ, pencil_idx * CY, jnp.zeros((), jnp.int32)])
    local_base = base_index - anchor[:, None]
    site_charge = (
        charges.reshape(2, n_buckets, capacity).transpose(1, 0, 2).reshape(n_buckets, site_count)
    )
    site_rel = (
        relative.reshape(2, 3, n_buckets, capacity)
        .transpose(2, 1, 0, 3)
        .reshape(n_buckets, 3, site_count)
    )
    site_base = jnp.broadcast_to(
        local_base.reshape(3, n_buckets, 1, capacity), (3, n_buckets, 2, capacity)
    )
    site_base = site_base.transpose(1, 0, 2, 3).reshape(n_buckets, 3, site_count)
    bucket_ids = jnp.arange(n_buckets, dtype=jnp.int32)
    window_shape = (BZ + 8, CY + 8, NX)
    zero_index = jnp.zeros((), jnp.int32)

    def spread_step(grid_now, inputs):
        bucket, charge, rel_pos, base_pos = inputs
        plane_val, plane_slope = dense_window(rel_pos[0], base_pos[0] - bucket * BZ + 1, BZ + 8)
        row_val, row_slope = dense_window(rel_pos[1], base_pos[1] + 1, CY + 8)
        col_val, col_slope = dense_window(rel_pos[2], base_pos[2] - 3, NX)
        outer_prod = ((charge[:, None] * plane_val)[:, :, None] * row_val[:, None, :]).reshape(
            site_count, -1
        )
        block_sum = lax.dot_general(
            outer_prod, col_val, (((0,), (0,)), ((), ())), precision=three_pass
        )
        corner = (bucket * BZ, zero_index, zero_index)
        current = lax.dynamic_slice(grid_now, corner, window_shape)
        grid_now = lax.dynamic_update_slice(
            grid_now, current + block_sum.reshape(window_shape), corner
        )
        return (grid_now, (col_val, col_slope))

    charge_grid = jnp.zeros((CZ + 8, CY + 8, NX), jnp.float32)
    col_windows = []
    for bucket in range(n_buckets):
        charge_grid, window = spread_step(
            charge_grid, (bucket, site_charge[bucket], site_rel[bucket], site_base[bucket])
        )
        col_windows.append(window)
    rim_planes = jnp.concatenate([charge_grid[:4], charge_grid[CZ + 4 :]], axis=0)
    arrived = extended(rim_planes, (("slab", 0),), 4)
    inner_grid = charge_grid[4 : CZ + 4].at[:4].add(arrived[:4]).at[CZ - 4 :].add(arrived[12:])
    rim_rows = jnp.concatenate([inner_grid[:, :4], inner_grid[:, CY + 4 :]], axis=1)
    arrived = extended(rim_rows, (("pencil", 1),), 4)
    source_grid = (
        inner_grid[:, 4 : CY + 4].at[:, :4].add(arrived[:, :4]).at[:, CY - 4 :].add(arrived[:, 12:])
    )
    rows_wave = rows_all // n_slab
    column_part = -(-(-(-half_cols // n_pencil)) // 4) * 4
    wave_all = column_part * n_pencil
    x_ids = pencil_idx * column_part + jnp.arange(column_part, dtype=jnp.int32)
    forward_x, inverse_x = x_tables(NX, column_part, n_pencil)
    forward_y = block_table(rows_all, -1.0).reshape(2, n_slab, rows_wave, 2 * rows_all)
    forward_y = forward_y.transpose(1, 0, 2, 3).reshape(2 * rows_all, 2 * rows_all)
    forward_z = block_table(planes_all, -1.0).reshape(2 * planes_all, 2 * planes_all)
    inverse_z = block_table(planes_all, 1.0).reshape(2, n_slab, CZ, 2 * planes_all)
    inverse_z = inverse_z.transpose(1, 0, 2, 3).reshape(2 * planes_all, 2 * planes_all)
    rows_ext = CY + 8
    row_out = jnp.arange(n_pencil, dtype=jnp.int32)[:, None] * CY - 4
    row_out = jnp.mod(row_out + jnp.arange(rows_ext, dtype=jnp.int32)[None, :], rows_all)
    inverse_y = block_table(rows_all, 1.0, row_out.reshape(-1))
    inverse_y = inverse_y.reshape(2, n_pencil, rows_ext, 2 * rows_all).transpose(1, 0, 2, 3)
    inverse_y = inverse_y.reshape(n_pencil * 2 * rows_ext, 2 * rows_all)
    wave_x = lax.dot_general(
        forward_x, source_grid.reshape(CZ * CY, NX), (((1,), (1,)), ((), ())), precision=three_pass
    )
    wave_x = lax.all_to_all(
        wave_x.reshape(n_pencil, 2 * column_part, CZ * CY), "pencil", 0, 0, tiled=True
    )
    wave_x = wave_x.reshape(n_pencil, 2, column_part, CZ, CY).transpose(1, 0, 4, 3, 2)
    wave_y = jnp.dot(forward_y, wave_x.reshape(2 * rows_all, column_part * CZ), precision=three_pass)
    wave_y = lax.all_to_all(
        wave_y.reshape(n_slab, 2 * rows_wave, column_part * CZ), "slab", 0, 0, tiled=True
    )
    wave_y = wave_y.reshape(n_slab, 2, rows_wave, CZ, column_part).transpose(1, 0, 3, 2, 4)
    wave_z = jnp.dot(
        forward_z, wave_y.reshape(2 * planes_all, rows_wave * column_part), precision=three_pass
    ).reshape(2, planes_all, rows_wave, column_part)
    factor = influence(
        jnp.arange(planes_all, dtype=jnp.int32),
        planes_all,
        slab_idx * rows_wave + jnp.arange(rows_wave, dtype=jnp.int32),
        rows_all,
        x_ids,
        NX,
    )
    weighted = wave_z * factor[None]
    power = weighted[0] * wave_z[0] + weighted[1] * wave_z[1]
    x_weight = jnp.where((x_ids == 0) | (2 * x_ids == NX), 1.0, 2.0).astype(jnp.float32)
    x_weight = x_weight * (2 * x_ids <= NX).astype(jnp.float32)
    energy_terms = 0.5 * jnp.sum(power * x_weight)
    back_z = jnp.dot(
        inverse_z, weighted.reshape(2 * planes_all, rows_wave * column_part), precision=three_pass
    ).reshape(n_slab, 2 * CZ, rows_wave * column_part)
    carried = jnp.broadcast_to(energy_terms, (n_slab, 8, rows_wave * column_part))
    back_z = lax.all_to_all(
        jnp.concatenate([back_z, carried], axis=1), "slab", 0, 0, tiled=True
    )
    slab_energy = jnp.sum(back_z[:, 2 * CZ, 0])
    back_z = back_z[:, : 2 * CZ].reshape(n_slab, 2, CZ, rows_wave, column_part)
    back_z = back_z.transpose(1, 0, 3, 2, 4)
    back_y = jnp.dot(
        inverse_y, back_z.reshape(2 * rows_all, CZ * column_part), precision=three_pass
    ).reshape(n_pencil, 2 * rows_ext, CZ * column_part)
    carried = jnp.broadcast_to(slab_energy, (n_pencil, 8, CZ * column_part))
    back_y = lax.all_to_all(
        jnp.concatenate([back_y, carried], axis=1), "pencil", 0, 0, tiled=True
    )
    energy_sum = jnp.sum(back_y[:, 2 * rows_ext, 0])
    back_y = back_y[:, : 2 * rows_ext].reshape(n_pencil, 2, rows_ext, CZ, column_part)
    back_y = back_y.transpose(0, 1, 4, 3, 2)
    potential = lax.dot_general(
        back_y.reshape(2 * wave_all, CZ * rows_ext),
        inverse_x,
        (((0,), (0,)), ((), ())),
        precision=three_pass,
    ).reshape(CZ, rows_ext, NX)
    potential = extended(potential, (("slab", 0),), 4)

    plane_cells = jnp.arange(BZ + 8, dtype=jnp.int32).astype(jnp.float32)
    row_cells = jnp.arange(CY + 8, dtype=jnp.int32).astype(jnp.float32)

    def sample_step(inputs):
        bucket, rel_pos, base_pos, col_val, col_slope = inputs
        corner = (bucket * BZ, zero_index, zero_index)
        patch = lax.dynamic_slice(potential, corner, (BZ + 8, CY + 8, NX)).reshape(-1, NX)
        plane_first = (base_pos[0] - bucket * BZ + 1).astype(jnp.float32)
        row_first = (base_pos[1] + 1).astype(jnp.float32)
        plane_val, plane_slope = bspline(
            rel_pos[0][:, None] - (plane_cells[None, :] - plane_first[:, None]) + 6.0
        )
        row_val, row_slope = bspline(
            rel_pos[1][:, None] - (row_cells[None, :] - row_first[:, None]) + 6.0
        )

        def outer(planes, rows):
            return (planes[:, :, None] * rows[:, None, :]).reshape(site_count, -1)

        weights = jnp.concatenate(
            [outer(plane_slope, row_val), outer(plane_val, row_slope), outer(plane_val, row_val)],
            axis=0,
        )
        folded = jnp.dot(weights, patch, precision=three_pass)
        grad_z = jnp.sum(folded[:site_count] * col_val, axis=1)
        grad_y = jnp.sum(folded[site_count : 2 * site_count] * col_val, axis=1)
        grad_x = jnp.sum(folded[2 * site_count :] * col_slope, axis=1)
        return jnp.stack([grad_z, grad_y, grad_x])

    slopes = jnp.stack(
        [
            sample_step((bucket, site_rel[bucket], site_base[bucket]) + col_windows[bucket])
            for bucket in range(n_buckets)
        ]
    )
    forces = -site_charge[:, None, :] * slopes
    site_forces = forces.reshape(n_buckets, 3, 2, capacity).transpose(2, 1, 0, 3).reshape(2, 3, -1)
    (descriptor_grad,) = pullback(-site_forces[1])
    total_slots = species.shape[0] * n_slab * n_pencil
    energy = energy_sum / float(total_slots)
    return (energy, site_forces, descriptor_grad)


def solution(mesh):
    in_specs = (
        P(("slab", "pencil"), None),
        P(("slab", "pencil")),
        P(("slab", "pencil")),
        P(None, ("slab", "pencil")),
        P(None, ("slab", "pencil")),
        P(),
        P(),
        P(),
        P(),
        P(),
        P(),
    )
    out_specs = (P(), P(None, None, ("slab", "pencil")), P(("slab", "pencil"), None))
    return jax.shard_map(body, mesh=mesh, in_specs=in_specs, out_specs=out_specs, check_vma=False)
```

```python
import math

import jax
import jax.numpy as jnp
from jax import lax
from jax.sharding import PartitionSpec as P

NX = 384
CZ = 16
CY = 48
BZ = 4


ion_table = (6.0, 1.0, 9.0, 7.0)
wannier_table = (-8.0, 0.0, -8.0, -8.0)
spline_coeffs = (1.0 / 120.0, 26.0 / 120.0, 66.0 / 120.0, 26.0 / 120.0, 1.0 / 120.0)
ewald_beta = 1.4
shift_scale = 0.9
three_pass = lax.Precision.HIGH


def extended(cells, sides, width):
    for axis, dim in sides:
        count = lax.axis_size(axis)
        head = lax.slice_in_dim(cells, 0, width, axis=dim)
        tail = lax.slice_in_dim(cells, cells.shape[dim] - width, cells.shape[dim], axis=dim)
        cells = jnp.concatenate(
            [
                lax.ppermute(tail, axis, [(i, (i + 1) % count) for i in range(count)]),
                cells,
                lax.ppermute(head, axis, [((i + 1) % count, i) for i in range(count)]),
            ],
            axis=dim,
        )
    return cells


def bspline(offset):
    folded = jnp.minimum(offset, 6.0 - offset)
    part_one = jnp.maximum(folded, 0.0)
    part_two = jnp.maximum(folded - 1.0, 0.0)
    part_three = jnp.maximum(folded - 2.0, 0.0)
    spline_val = (part_one**5 - 6.0 * part_two**5 + 15.0 * part_three**5) / 120.0
    spline_slope = (part_one**4 - 6.0 * part_two**4 + 15.0 * part_three**4) / 24.0
    return (spline_val, jnp.where(offset <= 3.0, spline_slope, -spline_slope))


def species_charge(species, charge_list):
    kind_ids = jnp.arange(len(charge_list), dtype=jnp.int32)
    levels = jnp.asarray(charge_list, jnp.float32)
    picked = jnp.where(species[None, :] == kind_ids[:, None], levels[:, None], 0.0)
    return jnp.sum(picked, axis=0)


def fitting(descriptors, weight_in, bias_in, weight_mid, bias_mid, weight_out, bias_out):
    hidden = jnp.tanh(
        jnp.dot(descriptors, weight_in, preferred_element_type=jnp.float32) + bias_in
    ).astype(jnp.bfloat16)
    for layer_idx in range(weight_mid.shape[0]):
        pre_act = (
            jnp.dot(hidden, weight_mid[layer_idx], preferred_element_type=jnp.float32)
            + bias_mid[layer_idx]
        )
        hidden = (hidden.astype(jnp.float32) + jnp.tanh(pre_act)).astype(jnp.bfloat16)
    output_raw = lax.dot_general(
        weight_out, hidden, (((1,), (1,)), ((), ())), preferred_element_type=jnp.float32
    )
    return shift_scale * jnp.tanh(output_raw + bias_out[:, None])


def axis_terms(index, length):
    signed = jnp.where(2 * index >= length, index - length, index).astype(jnp.float32) / length
    orders = jnp.arange(1, 6, dtype=jnp.int32)
    phases = (index[:, None] * orders[None, :] % length).astype(jnp.float32) * (
        2.0 * math.pi / length
    )
    coeffs = jnp.asarray(spline_coeffs, jnp.float32)
    real_sum = jnp.sum(coeffs[None, :] * jnp.cos(phases), axis=1)
    imag_sum = jnp.sum(coeffs[None, :] * jnp.sin(phases), axis=1)
    modulus = 1.0 / (real_sum * real_sum + imag_sum * imag_sum)
    damping = jnp.exp(-((math.pi / ewald_beta) ** 2) * signed * signed)
    return (signed * signed, damping * modulus)


def influence(z_index, z_len, y_index, y_len, x_index, x_len):
    z_sq, z_fac = axis_terms(z_index, z_len)
    y_sq, y_fac = axis_terms(y_index, y_len)
    x_sq, x_fac = axis_terms(x_index, x_len)
    squared = z_sq[:, None, None] + y_sq[None, :, None] + x_sq[None, None, :]
    safe_sq = jnp.where(squared > 0.0, squared, 1.0)
    volume = float(z_len * y_len * x_len)
    scaled = (
        z_fac[:, None, None]
        * y_fac[None, :, None]
        * x_fac[None, None, :]
        / (math.pi * volume * safe_sq)
    )
    return jnp.where(squared > 0.0, scaled, 0.0)


def block_table(length, sign, out_ids=None):
    index = jnp.arange(length, dtype=jnp.int32)
    out_ids = index if out_ids is None else out_ids
    angles = (out_ids[:, None] * index[None, :] % length).astype(jnp.float32) * (
        2.0 * math.pi / length
    )
    cosine = jnp.cos(angles)
    sine = jnp.sin(angles) * sign
    return jnp.stack([jnp.stack([cosine, -sine], axis=1), jnp.stack([sine, cosine], axis=1)])


def x_tables(length, part, count):
    positions = jnp.arange(length, dtype=jnp.int32)
    wave_ids = jnp.arange(part * count, dtype=jnp.int32)
    angles = (wave_ids[:, None] * positions[None, :] % length).astype(jnp.float32) * (
        2.0 * math.pi / length
    )
    kept_mask = (2 * wave_ids <= length).astype(jnp.float32)
    doubled = (
        jnp.where((wave_ids == 0) | (2 * wave_ids == length), 1.0, 2.0).astype(jnp.float32)
        * kept_mask
    )
    cosine = jnp.cos(angles).reshape(count, 1, part, length)
    sine = jnp.sin(angles).reshape(count, 1, part, length)
    kept = kept_mask.reshape(count, 1, part, 1)
    twice = doubled.reshape(count, 1, part, 1)
    forward = jnp.concatenate([cosine * kept, -sine * kept], axis=1)
    inverse = jnp.concatenate([cosine * twice, -sine * twice], axis=1)
    return (forward.reshape(-1, length), inverse.reshape(-1, length))


def dense_window(relative, start, length):
    cell_ids = jnp.arange(length, dtype=jnp.int32)
    distance = jnp.mod(cell_ids[None, :] - start[:, None], length).astype(jnp.float32)
    return bspline(relative[:, None] - distance + 6.0)


def body(
    descriptors,
    species,
    bucket_count,
    base_index,
    fraction,
    weight_in,
    bias_in,
    weight_mid,
    bias_mid,
    weight_out,
    bias_out,
):
    n_slab = lax.axis_size("slab")
    n_pencil = lax.axis_size("pencil")
    slab_idx = lax.axis_index("slab")
    pencil_idx = lax.axis_index("pencil")
    rows_all = CY * n_pencil
    planes_all = CZ * n_slab
    half_cols = NX // 2 + 1
    n_buckets = bucket_count.shape[0]
    capacity = species.shape[0] // n_buckets
    site_count = 2 * capacity
    slot_ids = jnp.arange(capacity, dtype=jnp.int32)
    in_use = (slot_ids[None, :] < bucket_count[:, None]).reshape(-1).astype(jnp.float32)
    charges = (
        jnp.stack([species_charge(species, ion_table), species_charge(species, wannier_table)])
        * in_use[None, :]
    )

    def network(features):
        return fitting(features, weight_in, bias_in, weight_mid, bias_mid, weight_out, bias_out)

    centroid_shift, pullback = jax.vjp(network, descriptors)
    relative = jnp.stack([fraction, fraction + centroid_shift])
    anchor = jnp.stack([slab_idx * CZ, pencil_idx * CY, jnp.zeros((), jnp.int32)])
    local_base = base_index - anchor[:, None]
    site_charge = (
        charges.reshape(2, n_buckets, capacity).transpose(1, 0, 2).reshape(n_buckets, site_count)
    )
    site_rel = (
        relative.reshape(2, 3, n_buckets, capacity)
        .transpose(2, 1, 0, 3)
        .reshape(n_buckets, 3, site_count)
    )
    site_base = jnp.broadcast_to(
        local_base.reshape(3, n_buckets, 1, capacity), (3, n_buckets, 2, capacity)
    )
    site_base = site_base.transpose(1, 0, 2, 3).reshape(n_buckets, 3, site_count)
    bucket_ids = jnp.arange(n_buckets, dtype=jnp.int32)
    window_shape = (BZ + 8, CY + 8, NX)
    zero_index = jnp.zeros((), jnp.int32)

    def spread_step(grid_now, inputs):
        bucket, charge, rel_pos, base_pos = inputs
        plane_val, plane_slope = dense_window(rel_pos[0], base_pos[0] - bucket * BZ + 1, BZ + 8)
        row_val, row_slope = dense_window(rel_pos[1], base_pos[1] + 1, CY + 8)
        col_val, col_slope = dense_window(rel_pos[2], base_pos[2] - 3, NX)
        outer_prod = ((charge[:, None] * plane_val)[:, :, None] * row_val[:, None, :]).reshape(
            site_count, -1
        )
        block_sum = lax.dot_general(
            outer_prod, col_val, (((0,), (0,)), ((), ())), precision=three_pass
        )
        corner = (bucket * BZ, zero_index, zero_index)
        current = lax.dynamic_slice(grid_now, corner, window_shape)
        grid_now = lax.dynamic_update_slice(
            grid_now, current + block_sum.reshape(window_shape), corner
        )
        return (grid_now, (col_val, col_slope))

    charge_grid = jnp.zeros((CZ + 8, CY + 8, NX), jnp.float32)
    col_windows = [None] * n_buckets
    edge_buckets = [b for b in range(n_buckets) if b * BZ < 4 or b * BZ + BZ + 8 > CZ + 4]
    inner_buckets = [b for b in range(n_buckets) if b not in edge_buckets]
    for bucket in edge_buckets:
        charge_grid, col_windows[bucket] = spread_step(
            charge_grid, (bucket, site_charge[bucket], site_rel[bucket], site_base[bucket])
        )
    rim_planes = jnp.concatenate([charge_grid[:4], charge_grid[CZ + 4 :]], axis=0)
    arrived = extended(rim_planes, (("slab", 0),), 4)
    for bucket in inner_buckets:
        charge_grid, col_windows[bucket] = spread_step(
            charge_grid, (bucket, site_charge[bucket], site_rel[bucket], site_base[bucket])
        )
    inner_grid = charge_grid[4 : CZ + 4].at[:4].add(arrived[:4]).at[CZ - 4 :].add(arrived[12:])
    rim_rows = jnp.concatenate([inner_grid[:, :4], inner_grid[:, CY + 4 :]], axis=1)
    arrived = extended(rim_rows, (("pencil", 1),), 4)
    source_grid = (
        inner_grid[:, 4 : CY + 4].at[:, :4].add(arrived[:, :4]).at[:, CY - 4 :].add(arrived[:, 12:])
    )
    rows_wave = rows_all // n_slab
    column_part = -(-(-(-half_cols // n_pencil)) // 4) * 4
    wave_all = column_part * n_pencil
    x_ids = pencil_idx * column_part + jnp.arange(column_part, dtype=jnp.int32)
    forward_x, inverse_x = x_tables(NX, column_part, n_pencil)
    forward_y = block_table(rows_all, -1.0).reshape(2, n_slab, rows_wave, 2 * rows_all)
    forward_y = forward_y.transpose(1, 0, 2, 3).reshape(2 * rows_all, 2 * rows_all)
    forward_z = block_table(planes_all, -1.0).reshape(2 * planes_all, 2 * planes_all)
    inverse_z = block_table(planes_all, 1.0).reshape(2, n_slab, CZ, 2 * planes_all)
    inverse_z = inverse_z.transpose(1, 0, 2, 3).reshape(2 * planes_all, 2 * planes_all)
    rows_ext = CY + 8
    row_out = jnp.arange(n_pencil, dtype=jnp.int32)[:, None] * CY - 4
    row_out = jnp.mod(row_out + jnp.arange(rows_ext, dtype=jnp.int32)[None, :], rows_all)
    inverse_y = block_table(rows_all, 1.0, row_out.reshape(-1))
    inverse_y = inverse_y.reshape(2, n_pencil, rows_ext, 2 * rows_all).transpose(1, 0, 2, 3)
    inverse_y = inverse_y.reshape(n_pencil * 2 * rows_ext, 2 * rows_all)
    wave_x = lax.dot_general(
        forward_x, source_grid.reshape(CZ * CY, NX), (((1,), (1,)), ((), ())), precision=three_pass
    )
    wave_x = lax.all_to_all(
        wave_x.reshape(n_pencil, 2 * column_part, CZ * CY), "pencil", 0, 0, tiled=True
    )
    wave_x = wave_x.reshape(n_pencil, 2, column_part, CZ, CY).transpose(1, 0, 4, 3, 2)
    wave_y = jnp.dot(forward_y, wave_x.reshape(2 * rows_all, column_part * CZ), precision=three_pass)
    wave_y = lax.all_to_all(
        wave_y.reshape(n_slab, 2 * rows_wave, column_part * CZ), "slab", 0, 0, tiled=True
    )
    wave_y = wave_y.reshape(n_slab, 2, rows_wave, CZ, column_part).transpose(1, 0, 3, 2, 4)
    wave_z = jnp.dot(
        forward_z, wave_y.reshape(2 * planes_all, rows_wave * column_part), precision=three_pass
    ).reshape(2, planes_all, rows_wave, column_part)
    factor = influence(
        jnp.arange(planes_all, dtype=jnp.int32),
        planes_all,
        slab_idx * rows_wave + jnp.arange(rows_wave, dtype=jnp.int32),
        rows_all,
        x_ids,
        NX,
    )
    weighted = wave_z * factor[None]
    power = weighted[0] * wave_z[0] + weighted[1] * wave_z[1]
    x_weight = jnp.where((x_ids == 0) | (2 * x_ids == NX), 1.0, 2.0).astype(jnp.float32)
    x_weight = x_weight * (2 * x_ids <= NX).astype(jnp.float32)
    energy_terms = 0.5 * jnp.sum(power * x_weight)
    back_z = jnp.dot(
        inverse_z, weighted.reshape(2 * planes_all, rows_wave * column_part), precision=three_pass
    ).reshape(n_slab, 2 * CZ, rows_wave * column_part)
    carried = jnp.broadcast_to(energy_terms, (n_slab, 8, rows_wave * column_part))
    back_z = lax.all_to_all(
        jnp.concatenate([back_z, carried], axis=1), "slab", 0, 0, tiled=True
    )
    slab_energy = jnp.sum(back_z[:, 2 * CZ, 0])
    back_z = back_z[:, : 2 * CZ].reshape(n_slab, 2, CZ, rows_wave, column_part)
    back_z = back_z.transpose(1, 0, 3, 2, 4)
    back_y = jnp.dot(
        inverse_y, back_z.reshape(2 * rows_all, CZ * column_part), precision=three_pass
    ).reshape(n_pencil, 2 * rows_ext, CZ * column_part)
    carried = jnp.broadcast_to(slab_energy, (n_pencil, 8, CZ * column_part))
    back_y = lax.all_to_all(
        jnp.concatenate([back_y, carried], axis=1), "pencil", 0, 0, tiled=True
    )
    energy_sum = jnp.sum(back_y[:, 2 * rows_ext, 0])
    back_y = back_y[:, : 2 * rows_ext].reshape(n_pencil, 2, rows_ext, CZ, column_part)
    back_y = back_y.transpose(0, 1, 4, 3, 2)
    potential = lax.dot_general(
        back_y.reshape(2 * wave_all, CZ * rows_ext),
        inverse_x,
        (((0,), (0,)), ((), ())),
        precision=three_pass,
    ).reshape(CZ, rows_ext, NX)
    potential = extended(potential, (("slab", 0),), 4)

    flat_ids = jnp.arange((CY + 8) * (BZ + 8), dtype=jnp.int32)
    flat_row = (flat_ids % (CY + 8)).astype(jnp.float32)
    flat_plane = (flat_ids // (CY + 8)).astype(jnp.float32)

    def sample_step(inputs):
        bucket, rel_pos, base_pos, col_val, col_slope = inputs
        corner = (bucket * BZ, zero_index, zero_index)
        patch = lax.dynamic_slice(potential, corner, (BZ + 8, CY + 8, NX)).reshape(-1, NX)
        plane_first = (base_pos[0] - bucket * BZ + 1).astype(jnp.float32)
        row_first = (base_pos[1] + 1).astype(jnp.float32)
        plane_val, plane_slope = bspline(
            rel_pos[0][:, None] - (flat_plane[None, :] - plane_first[:, None]) + 6.0
        )
        row_val, row_slope = bspline(
            rel_pos[1][:, None] - (flat_row[None, :] - row_first[:, None]) + 6.0
        )
        weights = jnp.concatenate(
            [plane_slope * row_val, plane_val * row_slope, plane_val * row_val], axis=0
        )
        folded = jnp.dot(weights, patch, precision=three_pass)
        grad_z = jnp.sum(folded[:site_count] * col_val, axis=1)
        grad_y = jnp.sum(folded[site_count : 2 * site_count] * col_val, axis=1)
        grad_x = jnp.sum(folded[2 * site_count :] * col_slope, axis=1)
        return jnp.stack([grad_z, grad_y, grad_x])

    slopes = jnp.stack(
        [
            sample_step((bucket, site_rel[bucket], site_base[bucket]) + col_windows[bucket])
            for bucket in range(n_buckets)
        ]
    )
    forces = -site_charge[:, None, :] * slopes
    site_forces = forces.reshape(n_buckets, 3, 2, capacity).transpose(2, 1, 0, 3).reshape(2, 3, -1)
    (descriptor_grad,) = pullback(-site_forces[1])
    total_slots = species.shape[0] * n_slab * n_pencil
    energy = energy_sum / float(total_slots)
    return (energy, site_forces, descriptor_grad)


def solution(mesh):
    in_specs = (
        P(("slab", "pencil"), None),
        P(("slab", "pencil")),
        P(("slab", "pencil")),
        P(None, ("slab", "pencil")),
        P(None, ("slab", "pencil")),
        P(),
        P(),
        P(),
        P(),
        P(),
        P(),
    )
    out_specs = (P(), P(None, None, ("slab", "pencil")), P(("slab", "pencil"), None))
    return jax.shard_map(body, mesh=mesh, in_specs=in_specs, out_specs=out_specs, check_vma=False)
```

```python
import math

import jax
import jax.numpy as jnp
from jax import lax
from jax.sharding import PartitionSpec as P

NX = 384
CZ = 16
CY = 48
BZ = 4


ion_table = (6.0, 1.0, 9.0, 7.0)
wannier_table = (-8.0, 0.0, -8.0, -8.0)
spline_coeffs = (1.0 / 120.0, 26.0 / 120.0, 66.0 / 120.0, 26.0 / 120.0, 1.0 / 120.0)
ewald_beta = 1.4
shift_scale = 0.9
three_pass = lax.Precision.HIGH


def extended(cells, sides, width):
    for axis, dim in sides:
        count = lax.axis_size(axis)
        head = lax.slice_in_dim(cells, 0, width, axis=dim)
        tail = lax.slice_in_dim(cells, cells.shape[dim] - width, cells.shape[dim], axis=dim)
        cells = jnp.concatenate(
            [
                lax.ppermute(tail, axis, [(i, (i + 1) % count) for i in range(count)]),
                cells,
                lax.ppermute(head, axis, [((i + 1) % count, i) for i in range(count)]),
            ],
            axis=dim,
        )
    return cells


def bspline(offset):
    folded = jnp.minimum(offset, 6.0 - offset)
    part_one = jnp.maximum(folded, 0.0)
    part_two = jnp.maximum(folded - 1.0, 0.0)
    part_three = jnp.maximum(folded - 2.0, 0.0)
    spline_val = (part_one**5 - 6.0 * part_two**5 + 15.0 * part_three**5) / 120.0
    spline_slope = (part_one**4 - 6.0 * part_two**4 + 15.0 * part_three**4) / 24.0
    return (spline_val, jnp.where(offset <= 3.0, spline_slope, -spline_slope))


def species_charge(species, charge_list):
    kind_ids = jnp.arange(len(charge_list), dtype=jnp.int32)
    levels = jnp.asarray(charge_list, jnp.float32)
    picked = jnp.where(species[None, :] == kind_ids[:, None], levels[:, None], 0.0)
    return jnp.sum(picked, axis=0)


def fitting(pre_input, weight_mid, bias_mid, weight_out, bias_out):
    hidden = jnp.tanh(pre_input).astype(jnp.bfloat16)
    for layer_idx in range(weight_mid.shape[0]):
        pre_act = (
            jnp.dot(hidden, weight_mid[layer_idx], preferred_element_type=jnp.float32)
            + bias_mid[layer_idx]
        )
        hidden = (hidden.astype(jnp.float32) + jnp.tanh(pre_act)).astype(jnp.bfloat16)
    output_raw = lax.dot_general(
        weight_out, hidden, (((1,), (1,)), ((), ())), preferred_element_type=jnp.float32
    )
    return shift_scale * jnp.tanh(output_raw + bias_out[:, None])


def axis_terms(index, length):
    signed = jnp.where(2 * index >= length, index - length, index).astype(jnp.float32) / length
    orders = jnp.arange(1, 6, dtype=jnp.int32)
    phases = (index[:, None] * orders[None, :] % length).astype(jnp.float32) * (
        2.0 * math.pi / length
    )
    coeffs = jnp.asarray(spline_coeffs, jnp.float32)
    real_sum = jnp.sum(coeffs[None, :] * jnp.cos(phases), axis=1)
    imag_sum = jnp.sum(coeffs[None, :] * jnp.sin(phases), axis=1)
    modulus = 1.0 / (real_sum * real_sum + imag_sum * imag_sum)
    damping = jnp.exp(-((math.pi / ewald_beta) ** 2) * signed * signed)
    return (signed * signed, damping * modulus)


def influence(z_index, z_len, y_index, y_len, x_index, x_len):
    z_sq, z_fac = axis_terms(z_index, z_len)
    y_sq, y_fac = axis_terms(y_index, y_len)
    x_sq, x_fac = axis_terms(x_index, x_len)
    squared = z_sq[:, None, None] + y_sq[None, :, None] + x_sq[None, None, :]
    safe_sq = jnp.where(squared > 0.0, squared, 1.0)
    volume = float(z_len * y_len * x_len)
    scaled = (
        z_fac[:, None, None]
        * y_fac[None, :, None]
        * x_fac[None, None, :]
        / (math.pi * volume * safe_sq)
    )
    return jnp.where(squared > 0.0, scaled, 0.0)


def block_table(length, sign, out_ids=None):
    index = jnp.arange(length, dtype=jnp.int32)
    out_ids = index if out_ids is None else out_ids
    angles = (out_ids[:, None] * index[None, :] % length).astype(jnp.float32) * (
        2.0 * math.pi / length
    )
    cosine = jnp.cos(angles)
    sine = jnp.sin(angles) * sign
    return jnp.stack([jnp.stack([cosine, -sine], axis=1), jnp.stack([sine, cosine], axis=1)])


def x_tables(length, part, count):
    positions = jnp.arange(length, dtype=jnp.int32)
    wave_ids = jnp.arange(part * count, dtype=jnp.int32)
    angles = (wave_ids[:, None] * positions[None, :] % length).astype(jnp.float32) * (
        2.0 * math.pi / length
    )
    kept_mask = (2 * wave_ids <= length).astype(jnp.float32)
    doubled = (
        jnp.where((wave_ids == 0) | (2 * wave_ids == length), 1.0, 2.0).astype(jnp.float32)
        * kept_mask
    )
    cosine = jnp.cos(angles).reshape(count, 1, part, length)
    sine = jnp.sin(angles).reshape(count, 1, part, length)
    kept = kept_mask.reshape(count, 1, part, 1)
    twice = doubled.reshape(count, 1, part, 1)
    forward = jnp.concatenate([cosine * kept, -sine * kept], axis=1)
    inverse = jnp.concatenate([cosine * twice, -sine * twice], axis=1)
    return (forward.reshape(-1, length), inverse.reshape(-1, length))


def dense_window(relative, start, length):
    cell_ids = jnp.arange(length, dtype=jnp.int32)
    distance = jnp.mod(cell_ids[None, :] - start[:, None], length).astype(jnp.float32)
    return bspline(relative[:, None] - distance + 6.0)


def body(
    descriptors,
    species,
    bucket_count,
    base_index,
    fraction,
    weight_in,
    bias_in,
    weight_mid,
    bias_mid,
    weight_out,
    bias_out,
):
    n_slab = lax.axis_size("slab")
    n_pencil = lax.axis_size("pencil")
    slab_idx = lax.axis_index("slab")
    pencil_idx = lax.axis_index("pencil")
    rows_all = CY * n_pencil
    planes_all = CZ * n_slab
    half_cols = NX // 2 + 1
    n_buckets = bucket_count.shape[0]
    capacity = species.shape[0] // n_buckets
    site_count = 2 * capacity
    slot_ids = jnp.arange(capacity, dtype=jnp.int32)
    in_use = (slot_ids[None, :] < bucket_count[:, None]).reshape(-1).astype(jnp.float32)
    charges = (
        jnp.stack([species_charge(species, ion_table), species_charge(species, wannier_table)])
        * in_use[None, :]
    )

    def network(pre_input):
        return fitting(pre_input, weight_mid, bias_mid, weight_out, bias_out)

    pre_input = jnp.dot(descriptors, weight_in, preferred_element_type=jnp.float32) + bias_in
    centroid_shift, pullback = jax.vjp(network, pre_input)
    relative = jnp.stack([fraction, fraction + centroid_shift])
    anchor = jnp.stack([slab_idx * CZ, pencil_idx * CY, jnp.zeros((), jnp.int32)])
    local_base = base_index - anchor[:, None]
    site_charge = (
        charges.reshape(2, n_buckets, capacity).transpose(1, 0, 2).reshape(n_buckets, site_count)
    )
    site_rel = (
        relative.reshape(2, 3, n_buckets, capacity)
        .transpose(2, 1, 0, 3)
        .reshape(n_buckets, 3, site_count)
    )
    site_base = jnp.broadcast_to(
        local_base.reshape(3, n_buckets, 1, capacity), (3, n_buckets, 2, capacity)
    )
    site_base = site_base.transpose(1, 0, 2, 3).reshape(n_buckets, 3, site_count)
    bucket_ids = jnp.arange(n_buckets, dtype=jnp.int32)
    window_shape = (BZ + 8, CY + 8, NX)
    zero_index = jnp.zeros((), jnp.int32)

    def spread_step(grid_now, inputs):
        bucket, charge, rel_pos, base_pos = inputs
        plane_val, plane_slope = dense_window(rel_pos[0], base_pos[0] - bucket * BZ + 1, BZ + 8)
        row_val, row_slope = dense_window(rel_pos[1], base_pos[1] + 1, CY + 8)
        col_val, col_slope = dense_window(rel_pos[2], base_pos[2] - 3, NX)
        outer_prod = ((charge[:, None] * plane_val)[:, :, None] * row_val[:, None, :]).reshape(
            site_count, -1
        )
        block_sum = lax.dot_general(
            outer_prod, col_val, (((0,), (0,)), ((), ())), precision=three_pass
        )
        corner = (bucket * BZ, zero_index, zero_index)
        current = lax.dynamic_slice(grid_now, corner, window_shape)
        grid_now = lax.dynamic_update_slice(
            grid_now, current + block_sum.reshape(window_shape), corner
        )
        return (grid_now, (col_val, col_slope))

    charge_grid = jnp.zeros((CZ + 8, CY + 8, NX), jnp.float32)
    col_windows = [None] * n_buckets
    edge_buckets = [b for b in range(n_buckets) if b * BZ < 4 or b * BZ + BZ + 8 > CZ + 4]
    inner_buckets = [b for b in range(n_buckets) if b not in edge_buckets]
    for bucket in edge_buckets:
        charge_grid, col_windows[bucket] = spread_step(
            charge_grid, (bucket, site_charge[bucket], site_rel[bucket], site_base[bucket])
        )
    rim_planes = jnp.concatenate([charge_grid[:4], charge_grid[CZ + 4 :]], axis=0)
    arrived = extended(rim_planes, (("slab", 0),), 4)
    for bucket in inner_buckets:
        charge_grid, col_windows[bucket] = spread_step(
            charge_grid, (bucket, site_charge[bucket], site_rel[bucket], site_base[bucket])
        )
    inner_grid = charge_grid[4 : CZ + 4].at[:4].add(arrived[:4]).at[CZ - 4 :].add(arrived[12:])
    rim_rows = jnp.concatenate([inner_grid[:, :4], inner_grid[:, CY + 4 :]], axis=1)
    arrived = extended(rim_rows, (("pencil", 1),), 4)
    source_grid = (
        inner_grid[:, 4 : CY + 4].at[:, :4].add(arrived[:, :4]).at[:, CY - 4 :].add(arrived[:, 12:])
    )
    rows_wave = rows_all // n_slab
    column_part = -(-(-(-half_cols // n_pencil)) // 4) * 4
    wave_all = column_part * n_pencil
    x_ids = pencil_idx * column_part + jnp.arange(column_part, dtype=jnp.int32)
    forward_x, inverse_x = x_tables(NX, column_part, n_pencil)
    forward_y = block_table(rows_all, -1.0).reshape(2, n_slab, rows_wave, 2 * rows_all)
    forward_y = forward_y.transpose(1, 0, 2, 3).reshape(2 * rows_all, 2 * rows_all)
    forward_z = block_table(planes_all, -1.0).reshape(2 * planes_all, 2 * planes_all)
    inverse_z = block_table(planes_all, 1.0).reshape(2, n_slab, CZ, 2 * planes_all)
    inverse_z = inverse_z.transpose(1, 0, 2, 3).reshape(2 * planes_all, 2 * planes_all)
    rows_ext = CY + 8
    row_out = jnp.arange(n_pencil, dtype=jnp.int32)[:, None] * CY - 4
    row_out = jnp.mod(row_out + jnp.arange(rows_ext, dtype=jnp.int32)[None, :], rows_all)
    inverse_y = block_table(rows_all, 1.0, row_out.reshape(-1))
    inverse_y = inverse_y.reshape(2, n_pencil, rows_ext, 2 * rows_all).transpose(1, 0, 2, 3)
    inverse_y = inverse_y.reshape(n_pencil * 2 * rows_ext, 2 * rows_all)
    wave_x = lax.dot_general(
        forward_x, source_grid.reshape(CZ * CY, NX), (((1,), (1,)), ((), ())), precision=three_pass
    )
    wave_x = lax.all_to_all(
        wave_x.reshape(n_pencil, 2 * column_part, CZ * CY), "pencil", 0, 0, tiled=True
    )
    wave_x = wave_x.reshape(n_pencil, 2, column_part, CZ, CY).transpose(1, 0, 4, 3, 2)
    wave_y = jnp.dot(forward_y, wave_x.reshape(2 * rows_all, column_part * CZ), precision=three_pass)
    wave_y = lax.all_to_all(
        wave_y.reshape(n_slab, 2 * rows_wave, column_part * CZ), "slab", 0, 0, tiled=True
    )
    wave_y = wave_y.reshape(n_slab, 2, rows_wave, CZ, column_part).transpose(1, 0, 3, 2, 4)
    wave_z = jnp.dot(
        forward_z, wave_y.reshape(2 * planes_all, rows_wave * column_part), precision=three_pass
    ).reshape(2, planes_all, rows_wave, column_part)
    factor = influence(
        jnp.arange(planes_all, dtype=jnp.int32),
        planes_all,
        slab_idx * rows_wave + jnp.arange(rows_wave, dtype=jnp.int32),
        rows_all,
        x_ids,
        NX,
    )
    weighted = wave_z * factor[None]
    power = weighted[0] * wave_z[0] + weighted[1] * wave_z[1]
    x_weight = jnp.where((x_ids == 0) | (2 * x_ids == NX), 1.0, 2.0).astype(jnp.float32)
    x_weight = x_weight * (2 * x_ids <= NX).astype(jnp.float32)
    energy_terms = 0.5 * jnp.sum(power * x_weight)
    back_z = jnp.dot(
        inverse_z, weighted.reshape(2 * planes_all, rows_wave * column_part), precision=three_pass
    ).reshape(n_slab, 2 * CZ, rows_wave * column_part)
    carried = jnp.broadcast_to(energy_terms, (n_slab, 8, rows_wave * column_part))
    back_z = lax.all_to_all(
        jnp.concatenate([back_z, carried], axis=1), "slab", 0, 0, tiled=True
    )
    slab_energy = jnp.sum(back_z[:, 2 * CZ, 0])
    back_z = back_z[:, : 2 * CZ].reshape(n_slab, 2, CZ, rows_wave, column_part)
    back_z = back_z.transpose(1, 0, 3, 2, 4)
    back_y = jnp.dot(
        inverse_y, back_z.reshape(2 * rows_all, CZ * column_part), precision=three_pass
    ).reshape(n_pencil, 2 * rows_ext, CZ * column_part)
    carried = jnp.broadcast_to(slab_energy, (n_pencil, 8, CZ * column_part))
    back_y = lax.all_to_all(
        jnp.concatenate([back_y, carried], axis=1), "pencil", 0, 0, tiled=True
    )
    energy_sum = jnp.sum(back_y[:, 2 * rows_ext, 0])
    back_y = back_y[:, : 2 * rows_ext].reshape(n_pencil, 2, rows_ext, CZ, column_part)
    back_y = back_y.transpose(0, 1, 4, 3, 2)
    potential = lax.dot_general(
        back_y.reshape(2 * wave_all, CZ * rows_ext),
        inverse_x,
        (((0,), (0,)), ((), ())),
        precision=three_pass,
    ).reshape(CZ, rows_ext, NX)
    potential = extended(potential, (("slab", 0),), 4)

    flat_ids = jnp.arange((CY + 8) * (BZ + 8), dtype=jnp.int32)
    flat_row = (flat_ids % (CY + 8)).astype(jnp.float32)
    flat_plane = (flat_ids // (CY + 8)).astype(jnp.float32)

    def sample_step(inputs):
        bucket, rel_pos, base_pos, col_val, col_slope = inputs
        corner = (bucket * BZ, zero_index, zero_index)
        patch = lax.dynamic_slice(potential, corner, (BZ + 8, CY + 8, NX)).reshape(-1, NX)
        plane_first = (base_pos[0] - bucket * BZ + 1).astype(jnp.float32)
        row_first = (base_pos[1] + 1).astype(jnp.float32)
        plane_val, plane_slope = bspline(
            rel_pos[0][:, None] - (flat_plane[None, :] - plane_first[:, None]) + 6.0
        )
        row_val, row_slope = bspline(
            rel_pos[1][:, None] - (flat_row[None, :] - row_first[:, None]) + 6.0
        )
        weights = jnp.concatenate(
            [plane_slope * row_val, plane_val * row_slope, plane_val * row_val], axis=0
        )
        folded = jnp.dot(weights, patch, precision=three_pass)
        grad_z = jnp.sum(folded[:site_count] * col_val, axis=1)
        grad_y = jnp.sum(folded[site_count : 2 * site_count] * col_val, axis=1)
        grad_x = jnp.sum(folded[2 * site_count :] * col_slope, axis=1)
        return jnp.stack([grad_z, grad_y, grad_x])

    slopes = jnp.stack(
        [
            sample_step((bucket, site_rel[bucket], site_base[bucket]) + col_windows[bucket])
            for bucket in range(n_buckets)
        ]
    )
    forces = -site_charge[:, None, :] * slopes
    site_forces = forces.reshape(n_buckets, 3, 2, capacity).transpose(2, 1, 0, 3).reshape(2, 3, -1)
    (input_grad,) = pullback(-site_forces[1])
    descriptor_grad = lax.dot_general(
        input_grad.astype(jnp.bfloat16),
        weight_in,
        (((1,), (1,)), ((), ())),
        preferred_element_type=jnp.float32,
    ).astype(jnp.bfloat16)
    total_slots = species.shape[0] * n_slab * n_pencil
    energy = energy_sum / float(total_slots)
    return (energy, site_forces, descriptor_grad)


def solution(mesh):
    in_specs = (
        P(("slab", "pencil"), None),
        P(("slab", "pencil")),
        P(("slab", "pencil")),
        P(None, ("slab", "pencil")),
        P(None, ("slab", "pencil")),
        P(),
        P(),
        P(),
        P(),
        P(),
        P(),
    )
    out_specs = (P(), P(None, None, ("slab", "pencil")), P(("slab", "pencil"), None))
    return jax.shard_map(body, mesh=mesh, in_specs=in_specs, out_specs=out_specs, check_vma=False)
```
